32 devices in a mesh: event: 4 (over y, x), region: 8 (over z, core).
Axes of the slice: x: 2, y: 2, z: 4, core: 2. Of those that a mesh axis runs over, the one named last changes fastest.
Arguments:
- queries_in: bfloat16 [4096, 512], P('event'), parts along dimension 0, may hold values from -144 to 144
- hits_in: bfloat16 [32768, 512], P(('event', 'region')), parts along dimension 0, may hold values from -6 to 6
- w_query: bfloat16 [512, 512], replicated, may hold values from -0.25 to 0.25
- w_key: bfloat16 [512, 512], replicated, may hold values from -0.25 to 0.25
- w_value: bfloat16 [512, 512], replicated, may hold values from -0.25 to 0.25
- w_out: bfloat16 [512, 512], replicated, may hold values from -0.25 to 0.25
- mask_list: int32 [32, 16], P('event'), parts along dimension 0, may hold values from 0 to 63, all different within a row
- grad_out: bfloat16 [4096, 512], P('event'), parts along dimension 0, may hold values from -6 to 6
Outputs:
- layer_out: bfloat16 [4096, 512], P('event'), parts along dimension 0
- grad_queries: bfloat16 [4096, 512], P('event'), parts along dimension 0
- grad_hits: bfloat16 [32768, 512], P(('event', 'region')), parts along dimension 0
- grad_wq: float32 [2048, 512], P('event'), parts along dimension 0
- grad_wk: float32 [2048, 512], P('event'), parts along dimension 0
- grad_wv: float32 [2048, 512], P('event'), parts along dimension 0
- grad_wo: float32 [2048, 512], P('event'), parts along dimension 0
The draws below stay inside these ranges and needn't reach their ends.
There are 4 independent parts, one for each index of `event`. The reference program is written for one: setup_inputs(seed, part) draws one part's arguments, and reference() takes and returns one part's arrays. A program takes and returns all parts, laid end to end along the dimension named above; an argument that names none is the same for every part. Nothing has to cross between parts.
Inputs may be any that keep to these rules, and one draw needn't show every extreme that they name: `mask_list`: each row names 16 different hit blocks, and every hit block is named by some row.
All inputs are finite; a program needn't handle non-finite values.
Results may differ from the reference program's by a relative error of at most 0.04.
The reference program's roundings to bfloat16 on the way (of `attended`, `grad_att`, `grad_vals`, `grad_scores`, `grad_keys` and `grad_q`) count: a program that leaves them out, or rounds other values in their place, can miss the bound.
Values may be sent and summed in bfloat16 or wider, within the bound.
No kernel may reach another device: no remote copies, remote signals or barrier semaphores. Data moves between devices by JAX's collectives and lax.ppermute only.
A program may use at most 192 MiB of HBM per device.

```python
import math
import jax
import jax.numpy as jnp
from jax import lax

D = 512
HEADS = 8
BLOCK = 128
QUERIES = 1024
HIT_DEV = 1024
HITS = 8192
HBLK_DEV = 8
NBLOCKS = 64
QBLOCKS = 8
LIST = 16
N_REGION = 8


def draw_queries_in(key, part):
    base = jnp.clip(jax.random.normal(key, (QUERIES, D), jnp.float32), -6.0, 6.0)
    return base.astype(jnp.bfloat16)


def levels(own_key, dims, cuts, low, largest):
    factor_of, own = 1.0, jax.random.fold_in(own_key, 6)
    for dim, blocks in cuts:
        heights = jnp.exp(jax.random.uniform(jax.random.fold_in(own, dim), (blocks,), jnp.float32, low / len(cuts), largest / len(cuts)))
        factor_of = factor_of * jnp.repeat(heights, dims[dim] // blocks).reshape([-1 if axis == dim else 1 for axis in range(len(dims))])
    return factor_of


def different_ones(own_key, rows, count, top, lift):
    ranking = jax.random.permutation(jax.random.fold_in(own_key, 1), count)
    boost = ranking
    for power in range(3):
        boost = boost * boost // count
    boost = boost * lift // count
    lots = jax.random.randint(jax.random.fold_in(own_key, 2), (rows, count), 0, 4096) + boost
    fixed_rows = jax.random.permutation(jax.random.fold_in(own_key, 3), rows)[jnp.arange(count) % rows]
    lots = jnp.where(jnp.arange(rows)[:, None] == fixed_rows[None, :], 1 << 14, lots)
    merit = lots * count + jnp.arange(count)
    return lax.top_k(merit.astype(jnp.int32), top)[1].astype(jnp.int32)


def gaussian(own_key, shape, deviation, reach, pieces=(), held_as=jnp.bfloat16):
    loudness = levels(own_key, shape, pieces, -0.22, 0.18) if pieces else 1.0
    values = jax.random.normal(own_key, shape, jnp.float32) * deviation * loudness
    return jnp.minimum(jnp.maximum(values, -reach), reach).astype(held_as)


def setup_inputs(seed: int = 0, part: int = 0) -> dict:
    key_of = jax.random.split(jax.random.key(seed), 9)
    part_splits = jax.random.split(jax.random.fold_in(key_of[8], part), 9)
    return {
        "queries_in": draw_queries_in(jax.random.fold_in(jax.random.fold_in(key_of[8], part), 71), part),
        "hits_in": gaussian(part_splits[1], (HITS, D), 1.0, 6.0, ((0, 8),)),
        "w_query": gaussian(key_of[2], (D, D), D ** -0.5, 0.25),
        "w_key": gaussian(key_of[3], (D, D), D ** -0.5, 0.25),
        "w_value": gaussian(key_of[4], (D, D), D ** -0.5, 0.25),
        "w_out": gaussian(key_of[5], (D, D), D ** -0.5, 0.25),
        "mask_list": different_ones(part_splits[6], QBLOCKS, NBLOCKS, LIST, 4096),
        "grad_out": gaussian(part_splits[7], (QUERIES, D), 1.0, 6.0),
    }


def split_heads(array):
    return array.reshape(array.shape[:-1] + (HEADS, array.shape[-1] // HEADS))

def combine_stack(numerators, maxima, totals):
    peak = lax.optimization_barrier(jnp.max(maxima, axis=0))
    weights = jnp.exp(maxima - peak[None])
    total = lax.optimization_barrier(jnp.sum(totals * weights, axis=0))
    head_dim = numerators.shape[-1] // maxima.shape[-1]
    numer = lax.optimization_barrier(jnp.sum(numerators * jnp.repeat(weights, head_dim, axis=-1), axis=0))
    return (numer, peak, total)

def reference(queries_in, hits_in, w_query, w_key, w_value, w_out, mask_list, grad_out):
    f32 = jnp.float32
    bf16 = jnp.bfloat16
    score_scale = 1.0 / math.sqrt(D // HEADS)
    blockmask = jnp.any(mask_list[:, :, None] == jnp.arange(NBLOCKS, dtype=jnp.int32)[None, None, :], axis=1)
    query = jnp.dot(queries_in, w_query, preferred_element_type=f32).astype(bf16)
    query_heads = split_heads(query).astype(f32)
    hits_split = hits_in.reshape(N_REGION, HIT_DEV, D)
    region_cols = jnp.transpose(blockmask.reshape(QBLOCKS, N_REGION, HBLK_DEV), (1, 0, 2))

    def project(hits_part):
        keys = jnp.dot(hits_part, w_key, preferred_element_type=f32).astype(bf16)
        vals = jnp.dot(hits_part, w_value, preferred_element_type=f32).astype(bf16)
        return (keys, vals)

    def full_mask(columns):
        return jnp.repeat(jnp.repeat(columns, BLOCK, axis=0), BLOCK, axis=1)[:, None, :]

    def region_scores(keys, allowed):
        return jnp.einsum('qhd,khd->qhk', query_heads, split_heads(keys).astype(f32)) * score_scale

    def forward_region(inputs):
        hits_part, columns = inputs
        keys, vals = project(hits_part)
        allowed = full_mask(columns)
        scores = region_scores(keys, allowed)
        masked = jnp.where(allowed, scores, -1e+30)
        maxima = lax.optimization_barrier(jnp.max(masked, axis=2))
        exponents = jnp.where(allowed, jnp.exp(masked - maxima[..., None]), 0.0)
        totals = lax.optimization_barrier(jnp.sum(exponents, axis=2))
        numer = jnp.einsum('qhk,khd->qhd', exponents.astype(bf16).astype(f32), split_heads(vals).astype(f32))
        return (numer.reshape(QUERIES, D), maxima, totals)
    numer_all, maxima_all, totals_all = lax.map(forward_region, (hits_split, region_cols))
    numer, peak, total = combine_stack(numer_all, maxima_all, totals_all)
    head_dim = D // HEADS
    attended = (numer / jnp.repeat(total, head_dim, axis=-1)).astype(bf16)
    log_total = peak + jnp.log(total)
    layer_out = (queries_in.astype(f32) + jnp.dot(attended, w_out, preferred_element_type=f32)).astype(bf16)
    grad_att = jnp.dot(grad_out, w_out.T, preferred_element_type=f32).astype(bf16)
    grad_wo = jnp.dot(attended.T, grad_out, preferred_element_type=f32)
    grad_heads = split_heads(grad_att).astype(f32)
    deltas = lax.optimization_barrier(jnp.sum(grad_heads * split_heads(attended).astype(f32), axis=2))

    def backward_region(running, inputs):
        hits_part, columns = inputs
        keys, vals = project(hits_part)
        allowed = full_mask(columns)
        scores = region_scores(keys, allowed)
        probs = jnp.where(allowed, jnp.exp(scores - log_total[..., None]), 0.0)
        grad_vals = jnp.einsum('qhk,qhd->khd', probs.astype(bf16).astype(f32), grad_heads)
        grad_probs = jnp.einsum('qhd,khd->qhk', grad_heads, split_heads(vals).astype(f32))
        grad_scores = (probs * (grad_probs - deltas[..., None]) * score_scale).astype(bf16).astype(f32)
        grad_q = jnp.einsum('qhk,khd->qhd', grad_scores, split_heads(keys).astype(f32)).reshape(QUERIES, D)
        grad_keys = jnp.einsum('qhk,qhd->khd', grad_scores, query_heads)
        return (running + grad_q, (grad_keys.reshape(HIT_DEV, D).astype(bf16), grad_vals.reshape(HIT_DEV, D).astype(bf16)))
    grad_q_sum, (keys_grad, vals_grad) = lax.scan(backward_region, jnp.zeros((QUERIES, D), f32), (hits_split, region_cols))
    grad_q = grad_q_sum.astype(bf16)
    keys_grad = keys_grad.reshape(HITS, D)
    vals_grad = vals_grad.reshape(HITS, D)
    grad_wq = jnp.dot(queries_in.T, grad_q, preferred_element_type=f32)
    grad_wk = jnp.dot(hits_in.T, keys_grad, preferred_element_type=f32)
    grad_wv = jnp.dot(hits_in.T, vals_grad, preferred_element_type=f32)
    grad_queries = (grad_out.astype(f32) + jnp.dot(grad_q, w_query.T, preferred_element_type=f32)).astype(bf16)
    grad_hits = (jnp.dot(keys_grad, w_key.T, preferred_element_type=f32) + jnp.dot(vals_grad, w_value.T, preferred_element_type=f32)).astype(bf16)
    return (layer_out, grad_queries, grad_hits, grad_wq, grad_wk, grad_wv, grad_wo)
```

```python
import functools
import math

import jax
import jax.numpy as jnp
from jax import lax
from jax.experimental import pallas as pl
from jax.experimental.pallas import tpu as pltpu
from jax.sharding import PartitionSpec as P

HEADS = 8
BLOCK = 128
TQ = 256


def _fwd_kernel(q_ref, k_ref, v_ref, cm_ref, numer_ref, m_ref, l_ref, *, scale):
    q = q_ref[0]
    k = k_ref[0]
    v = v_ref[0]
    s = lax.dot_general(q, k, (((1,), (1,)), ((), ())), preferred_element_type=jnp.float32) * scale
    tq, nk = s.shape
    nb = tq // BLOCK
    s3 = s.reshape(nb, BLOCK, nk)
    allowed = cm_ref[...] > 0.5
    masked = jnp.where(allowed, s3, -1e30)
    mx = jnp.max(masked, axis=2, keepdims=True)
    e = jnp.where(allowed, jnp.exp(masked - mx), 0.0)
    tot = jnp.sum(e, axis=2, keepdims=True)
    numer = jnp.dot(
        e.reshape(tq, nk).astype(jnp.bfloat16), v, preferred_element_type=jnp.float32
    )
    numer_ref[0] = numer
    m_ref[0] = mx.reshape(tq, 1)
    l_ref[0] = tot.reshape(tq, 1)


def _bwd_kernel(q_ref, k_ref, v_ref, ga_ref, lt_ref, dl_ref, cm_ref, dq_ref, dk_ref, dv_ref, *, scale):
    i = pl.program_id(1)

    @pl.when(i == 0)
    def _():
        dk_ref[...] = jnp.zeros_like(dk_ref)
        dv_ref[...] = jnp.zeros_like(dv_ref)

    q = q_ref[0]
    k = k_ref[0]
    v = v_ref[0]
    ga = ga_ref[0]
    s = lax.dot_general(q, k, (((1,), (1,)), ((), ())), preferred_element_type=jnp.float32) * scale
    tq, nk = s.shape
    nb = tq // BLOCK
    s3 = s.reshape(nb, BLOCK, nk)
    allowed = cm_ref[...] > 0.5
    lt = lt_ref[0].reshape(nb, BLOCK, 1)
    p = jnp.where(allowed, jnp.exp(s3 - lt), 0.0).reshape(tq, nk)
    dv_ref[0] += lax.dot_general(
        p.astype(jnp.bfloat16), ga, (((0,), (0,)), ((), ())), preferred_element_type=jnp.float32
    )
    dp = lax.dot_general(ga, v, (((1,), (1,)), ((), ())), preferred_element_type=jnp.float32)
    ds = (p * (dp - dl_ref[0]) * scale).astype(jnp.bfloat16)
    dq_ref[0] = jnp.dot(ds, k, preferred_element_type=jnp.float32)
    dk_ref[0] += lax.dot_general(
        ds, q, (((0,), (0,)), ((), ())), preferred_element_type=jnp.float32
    )


def _forward(qT, kT, vT, cm, scale):
    heads, nq, hd = qT.shape
    nk = kT.shape[1]
    nb = TQ // BLOCK
    f32 = jnp.float32
    return pl.pallas_call(
        functools.partial(_fwd_kernel, scale=scale),
        grid=(heads, nq // TQ),
        in_specs=[
            pl.BlockSpec((1, TQ, hd), lambda h, i: (h, i, 0)),
            pl.BlockSpec((1, nk, hd), lambda h, i: (h, 0, 0)),
            pl.BlockSpec((1, nk, hd), lambda h, i: (h, 0, 0)),
            pl.BlockSpec((nb, 1, nk), lambda h, i: (i, 0, 0)),
        ],
        out_specs=[
            pl.BlockSpec((1, TQ, hd), lambda h, i: (h, i, 0)),
            pl.BlockSpec((1, TQ, 1), lambda h, i: (h, i, 0)),
            pl.BlockSpec((1, TQ, 1), lambda h, i: (h, i, 0)),
        ],
        out_shape=[
            jax.ShapeDtypeStruct((heads, nq, hd), f32),
            jax.ShapeDtypeStruct((heads, nq, 1), f32),
            jax.ShapeDtypeStruct((heads, nq, 1), f32),
        ],
    )(qT, kT, vT, cm)


def _backward(qT, kT, vT, gaT, lt, dl, cm, scale):
    heads, nq, hd = qT.shape
    nk = kT.shape[1]
    nb = TQ // BLOCK
    f32 = jnp.float32
    return pl.pallas_call(
        functools.partial(_bwd_kernel, scale=scale),
        grid=(heads, nq // TQ),
        in_specs=[
            pl.BlockSpec((1, TQ, hd), lambda h, i: (h, i, 0)),
            pl.BlockSpec((1, nk, hd), lambda h, i: (h, 0, 0)),
            pl.BlockSpec((1, nk, hd), lambda h, i: (h, 0, 0)),
            pl.BlockSpec((1, TQ, hd), lambda h, i: (h, i, 0)),
            pl.BlockSpec((1, TQ, 1), lambda h, i: (h, i, 0)),
            pl.BlockSpec((1, TQ, 1), lambda h, i: (h, i, 0)),
            pl.BlockSpec((nb, 1, nk), lambda h, i: (i, 0, 0)),
        ],
        out_specs=[
            pl.BlockSpec((1, TQ, hd), lambda h, i: (h, i, 0)),
            pl.BlockSpec((1, nk, hd), lambda h, i: (h, 0, 0)),
            pl.BlockSpec((1, nk, hd), lambda h, i: (h, 0, 0)),
        ],
        out_shape=[
            jax.ShapeDtypeStruct((heads, nq, hd), f32),
            jax.ShapeDtypeStruct((heads, nk, hd), f32),
            jax.ShapeDtypeStruct((heads, nk, hd), f32),
        ],
        compiler_params=pltpu.CompilerParams(dimension_semantics=("parallel", "arbitrary")),
    )(qT, kT, vT, gaT, lt, dl, cm)


def on_device(queries_in, hits_in, w_query, w_key, w_value, w_out, mask_list, grad_out):
    f32 = jnp.float32
    bf16 = jnp.bfloat16
    region_index = lax.axis_index("region")
    n_queries, width = queries_in.shape
    n_hits = hits_in.shape[0]
    head_dim = width // HEADS
    scale = 1.0 / math.sqrt(head_dim)
    hit_blocks = n_hits // BLOCK
    q_blocks = n_queries // BLOCK
    local_ids = region_index * hit_blocks + jnp.arange(hit_blocks, dtype=jnp.int32)
    blockmask = jnp.any(mask_list[:, :, None] == local_ids[None, None, :], axis=1)
    cm = jnp.repeat(blockmask.astype(f32), BLOCK, axis=1).reshape(q_blocks, 1, n_hits)

    def heads(x):
        return x.reshape(x.shape[0], HEADS, head_dim).transpose(1, 0, 2)

    def joined(x):
        return x.transpose(1, 0, 2).reshape(x.shape[1], width)

    query = jnp.dot(queries_in, w_query, preferred_element_type=f32).astype(bf16)
    keys = jnp.dot(hits_in, w_key, preferred_element_type=f32).astype(bf16)
    vals = jnp.dot(hits_in, w_value, preferred_element_type=f32).astype(bf16)
    qT, kT, vT = heads(query), heads(keys), heads(vals)

    numer_r, max_r, total_r = _forward(qT, kT, vT, cm, scale)
    peak = lax.pmax(max_r, "region")
    weight = jnp.exp(max_r - peak)
    numer, total = lax.psum((numer_r * weight, total_r * weight), "region")
    attended_h = (numer / total).astype(bf16)
    log_total = peak + jnp.log(total)
    attended = joined(attended_h)
    layer_out = (
        queries_in.astype(f32) + jnp.dot(attended, w_out, preferred_element_type=f32)
    ).astype(bf16)
    grad_att = lax.dot_general(
        grad_out, w_out, (((1,), (1,)), ((), ())), preferred_element_type=f32
    ).astype(bf16)
    grad_wo = jnp.einsum("qa,qb->ab", attended, grad_out, preferred_element_type=f32)
    gaT = heads(grad_att)
    deltas = jnp.sum(gaT.astype(f32) * attended_h.astype(f32), axis=2, keepdims=True)

    dq_r, dk, dv = _backward(qT, kT, vT, gaT, log_total, deltas, cm, scale)
    keys_grad = joined(dk).astype(bf16)
    vals_grad = joined(dv).astype(bf16)
    query_grad_local = joined(dq_r)
    wk_part = jnp.einsum("ka,kb->ab", hits_in, keys_grad, preferred_element_type=f32)
    wv_part = jnp.einsum("ka,kb->ab", hits_in, vals_grad, preferred_element_type=f32)
    query_grad_sum, grad_wk, grad_wv = lax.psum(
        (query_grad_local.astype(bf16), wk_part.astype(bf16), wv_part.astype(bf16)), "region"
    )
    grad_wk = grad_wk.astype(f32)
    grad_wv = grad_wv.astype(f32)
    grad_q = query_grad_sum
    grad_wq = jnp.einsum("qa,qb->ab", queries_in, grad_q, preferred_element_type=f32)
    grad_queries = (
        grad_out.astype(f32)
        + lax.dot_general(grad_q, w_query, (((1,), (1,)), ((), ())), preferred_element_type=f32)
    ).astype(bf16)
    grad_hits = (
        lax.dot_general(keys_grad, w_key, (((1,), (1,)), ((), ())), preferred_element_type=f32)
        + lax.dot_general(vals_grad, w_value, (((1,), (1,)), ((), ())), preferred_element_type=f32)
    ).astype(bf16)
    return (layer_out, grad_queries, grad_hits, grad_wq, grad_wk, grad_wv, grad_wo)


def solution(mesh):
    in_specs = (
        P("event", None),
        P(("event", "region"), None),
        P(),
        P(),
        P(),
        P(),
        P("event", None),
        P("event", None),
    )
    out_specs = (
        P("event", None),
        P("event", None),
        P(("event", "region"), None),
        P("event", None),
        P("event", None),
        P("event", None),
        P("event", None),
    )
    return jax.shard_map(
        on_device, mesh=mesh, in_specs=in_specs, out_specs=out_specs, check_vma=False
    )
```

```python
import functools
import math

import jax
import jax.numpy as jnp
from jax import lax
from jax.experimental import pallas as pl
from jax.experimental.pallas import tpu as pltpu
from jax.sharding import PartitionSpec as P

HEADS = 8
BLOCK = 128
TQ = 256


def _fwd_kernel(q_ref, k_ref, v_ref, cm_ref, numer_ref, m_ref, l_ref, *, scale):
    q = q_ref[0]
    k = k_ref[0]
    v = v_ref[0]
    s = lax.dot_general(q, k, (((1,), (1,)), ((), ())), preferred_element_type=jnp.float32) * scale
    tq, nk = s.shape
    nb = tq // BLOCK
    s3 = s.reshape(nb, BLOCK, nk)
    allowed = cm_ref[...] > 0.5
    masked = jnp.where(allowed, s3, -1e30)
    mx = jnp.max(masked, axis=2, keepdims=True)
    e = jnp.where(allowed, jnp.exp(masked - mx), 0.0)
    tot = jnp.sum(e, axis=2, keepdims=True)
    numer = jnp.dot(
        e.reshape(tq, nk).astype(jnp.bfloat16), v, preferred_element_type=jnp.float32
    )
    numer_ref[0] = numer
    m_ref[0] = mx.reshape(tq, 1)
    l_ref[0] = tot.reshape(tq, 1)


def _bwd_kernel(q_ref, k_ref, v_ref, ga_ref, lt_ref, dl_ref, cm_ref, dq_ref, dk_ref, dv_ref, *, scale):
    i = pl.program_id(1)

    @pl.when(i == 0)
    def _():
        dk_ref[...] = jnp.zeros_like(dk_ref)
        dv_ref[...] = jnp.zeros_like(dv_ref)

    q = q_ref[0]
    k = k_ref[0]
    v = v_ref[0]
    ga = ga_ref[0]
    s = lax.dot_general(q, k, (((1,), (1,)), ((), ())), preferred_element_type=jnp.float32) * scale
    tq, nk = s.shape
    nb = tq // BLOCK
    s3 = s.reshape(nb, BLOCK, nk)
    allowed = cm_ref[...] > 0.5
    lt = lt_ref[0].reshape(nb, BLOCK, 1)
    p = jnp.where(allowed, jnp.exp(s3 - lt), 0.0).reshape(tq, nk)
    dv_ref[0] += lax.dot_general(
        p.astype(jnp.bfloat16), ga, (((0,), (0,)), ((), ())), preferred_element_type=jnp.float32
    )
    dp = lax.dot_general(ga, v, (((1,), (1,)), ((), ())), preferred_element_type=jnp.float32)
    ds = (p * (dp - dl_ref[0]) * scale).astype(jnp.bfloat16)
    dq_ref[0] = jnp.dot(ds, k, preferred_element_type=jnp.float32)
    dk_ref[0] += lax.dot_general(
        ds, q, (((0,), (0,)), ((), ())), preferred_element_type=jnp.float32
    )


def _forward(qT, kT, vT, cm, scale):
    heads, nq, hd = qT.shape
    nk = kT.shape[1]
    nb = TQ // BLOCK
    f32 = jnp.float32
    return pl.pallas_call(
        functools.partial(_fwd_kernel, scale=scale),
        grid=(heads, nq // TQ),
        in_specs=[
            pl.BlockSpec((1, TQ, hd), lambda h, i: (h, i, 0)),
            pl.BlockSpec((1, nk, hd), lambda h, i: (h, 0, 0)),
            pl.BlockSpec((1, nk, hd), lambda h, i: (h, 0, 0)),
            pl.BlockSpec((nb, 1, nk), lambda h, i: (i, 0, 0)),
        ],
        out_specs=[
            pl.BlockSpec((1, TQ, hd), lambda h, i: (h, i, 0)),
            pl.BlockSpec((1, TQ, 1), lambda h, i: (h, i, 0)),
            pl.BlockSpec((1, TQ, 1), lambda h, i: (h, i, 0)),
        ],
        out_shape=[
            jax.ShapeDtypeStruct((heads, nq, hd), f32),
            jax.ShapeDtypeStruct((heads, nq, 1), f32),
            jax.ShapeDtypeStruct((heads, nq, 1), f32),
        ],
    )(qT, kT, vT, cm)


def _backward(qT, kT, vT, gaT, lt, dl, cm, scale):
    heads, nq, hd = qT.shape
    nk = kT.shape[1]
    nb = TQ // BLOCK
    f32 = jnp.float32
    return pl.pallas_call(
        functools.partial(_bwd_kernel, scale=scale),
        grid=(heads, nq // TQ),
        in_specs=[
            pl.BlockSpec((1, TQ, hd), lambda h, i: (h, i, 0)),
            pl.BlockSpec((1, nk, hd), lambda h, i: (h, 0, 0)),
            pl.BlockSpec((1, nk, hd), lambda h, i: (h, 0, 0)),
            pl.BlockSpec((1, TQ, hd), lambda h, i: (h, i, 0)),
            pl.BlockSpec((1, TQ, 1), lambda h, i: (h, i, 0)),
            pl.BlockSpec((1, TQ, 1), lambda h, i: (h, i, 0)),
            pl.BlockSpec((nb, 1, nk), lambda h, i: (i, 0, 0)),
        ],
        out_specs=[
            pl.BlockSpec((1, TQ, hd), lambda h, i: (h, i, 0)),
            pl.BlockSpec((1, nk, hd), lambda h, i: (h, 0, 0)),
            pl.BlockSpec((1, nk, hd), lambda h, i: (h, 0, 0)),
        ],
        out_shape=[
            jax.ShapeDtypeStruct((heads, nq, hd), f32),
            jax.ShapeDtypeStruct((heads, nk, hd), f32),
            jax.ShapeDtypeStruct((heads, nk, hd), f32),
        ],
        compiler_params=pltpu.CompilerParams(dimension_semantics=("parallel", "arbitrary")),
    )(qT, kT, vT, gaT, lt, dl, cm)


def on_device(queries_in, hits_in, w_query, w_key, w_value, w_out, mask_list, grad_out):
    f32 = jnp.float32
    bf16 = jnp.bfloat16
    region_index = lax.axis_index("region")
    n_queries, width = queries_in.shape
    n_hits = hits_in.shape[0]
    head_dim = width // HEADS
    scale = 1.0 / math.sqrt(head_dim)
    hit_blocks = n_hits // BLOCK
    q_blocks = n_queries // BLOCK
    local_ids = region_index * hit_blocks + jnp.arange(hit_blocks, dtype=jnp.int32)
    blockmask = jnp.any(mask_list[:, :, None] == local_ids[None, None, :], axis=1)
    cm = jnp.repeat(blockmask.astype(f32), BLOCK, axis=1).reshape(q_blocks, 1, n_hits)

    def heads(x):
        return x.reshape(x.shape[0], HEADS, head_dim).transpose(1, 0, 2)

    def joined(x):
        return x.transpose(1, 0, 2).reshape(x.shape[1], width)

    query = jnp.dot(queries_in, w_query, preferred_element_type=f32).astype(bf16)
    keys = jnp.dot(hits_in, w_key, preferred_element_type=f32).astype(bf16)
    vals = jnp.dot(hits_in, w_value, preferred_element_type=f32).astype(bf16)
    qT, kT, vT = heads(query), heads(keys), heads(vals)

    numer_r, max_r, total_r = _forward(qT, kT, vT, cm, scale)
    max_r = max_r.reshape(HEADS, n_queries)
    total_r = total_r.reshape(HEADS, n_queries)
    peak = lax.pmax(max_r, "region")
    weight = jnp.exp(max_r - peak)
    spread = jnp.repeat(weight.T, head_dim, axis=1)
    numer, total = lax.psum((joined(numer_r) * spread, total_r * weight), "region")
    attended = (numer / jnp.repeat(total.T, head_dim, axis=1)).astype(bf16)
    log_total = (peak + jnp.log(total)).reshape(HEADS, n_queries, 1)
    attended_h = heads(attended)
    layer_out = (
        queries_in.astype(f32) + jnp.dot(attended, w_out, preferred_element_type=f32)
    ).astype(bf16)
    grad_att = lax.dot_general(
        grad_out, w_out, (((1,), (1,)), ((), ())), preferred_element_type=f32
    ).astype(bf16)
    grad_wo = jnp.einsum("qa,qb->ab", attended, grad_out, preferred_element_type=f32)
    gaT = heads(grad_att)
    deltas = jnp.sum(gaT.astype(f32) * attended_h.astype(f32), axis=2, keepdims=True)

    dq_r, dk, dv = _backward(qT, kT, vT, gaT, log_total, deltas, cm, scale)
    keys_grad = joined(dk).astype(bf16)
    vals_grad = joined(dv).astype(bf16)
    query_grad_local = joined(dq_r)
    wk_part = jnp.einsum("ka,kb->ab", hits_in, keys_grad, preferred_element_type=f32)
    wv_part = jnp.einsum("ka,kb->ab", hits_in, vals_grad, preferred_element_type=f32)
    query_grad_sum, grad_wk, grad_wv = lax.psum(
        (query_grad_local.astype(bf16), wk_part.astype(bf16), wv_part.astype(bf16)), "region"
    )
    grad_wk = grad_wk.astype(f32)
    grad_wv = grad_wv.astype(f32)
    grad_q = query_grad_sum
    grad_wq = jnp.einsum("qa,qb->ab", queries_in, grad_q, preferred_element_type=f32)
    grad_queries = (
        grad_out.astype(f32)
        + lax.dot_general(grad_q, w_query, (((1,), (1,)), ((), ())), preferred_element_type=f32)
    ).astype(bf16)
    grad_hits = (
        lax.dot_general(keys_grad, w_key, (((1,), (1,)), ((), ())), preferred_element_type=f32)
        + lax.dot_general(vals_grad, w_value, (((1,), (1,)), ((), ())), preferred_element_type=f32)
    ).astype(bf16)
    return (layer_out, grad_queries, grad_hits, grad_wq, grad_wk, grad_wv, grad_wo)


def solution(mesh):
    in_specs = (
        P("event", None),
        P(("event", "region"), None),
        P(),
        P(),
        P(),
        P(),
        P("event", None),
        P("event", None),
    )
    out_specs = (
        P("event", None),
        P("event", None),
        P(("event", "region"), None),
        P("event", None),
        P("event", None),
        P("event", None),
        P("event", None),
    )
    return jax.shard_map(
        on_device, mesh=mesh, in_specs=in_specs, out_specs=out_specs, check_vma=False
    )
```

```python
import functools
import math

import jax
import jax.numpy as jnp
from jax import lax
from jax.experimental import pallas as pl
from jax.experimental.pallas import tpu as pltpu
from jax.sharding import PartitionSpec as P

HEADS = 8
BLOCK = 128
TQ = 256


def _fwd_kernel(q_ref, k_ref, v_ref, cm_ref, numer_ref, m_ref, l_ref, *, scale):
    q = q_ref[0]
    k = k_ref[0]
    v = v_ref[0]
    s = lax.dot_general(q, k, (((1,), (1,)), ((), ())), preferred_element_type=jnp.float32) * scale
    tq, nk = s.shape
    nb = tq // BLOCK
    s3 = s.reshape(nb, BLOCK, nk)
    allowed = cm_ref[...] > 0.5
    masked = jnp.where(allowed, s3, -1e30)
    mx = jnp.max(masked, axis=2, keepdims=True)
    e = jnp.where(allowed, jnp.exp(masked - mx), 0.0)
    tot = jnp.sum(e, axis=2, keepdims=True)
    numer = jnp.dot(
        e.reshape(tq, nk).astype(jnp.bfloat16), v, preferred_element_type=jnp.float32
    )
    numer_ref[0] = numer
    m_ref[0] = mx.reshape(tq, 1)
    l_ref[0] = tot.reshape(tq, 1)


def _bwd_kernel(q_ref, k_ref, v_ref, ga_ref, lt_ref, dl_ref, cm_ref, dq_ref, dk_ref, dv_ref, *, scale):
    i = pl.program_id(1)

    @pl.when(i == 0)
    def _():
        dk_ref[...] = jnp.zeros_like(dk_ref)
        dv_ref[...] = jnp.zeros_like(dv_ref)

    q = q_ref[0]
    k = k_ref[0]
    v = v_ref[0]
    ga = ga_ref[0]
    s = lax.dot_general(q, k, (((1,), (1,)), ((), ())), preferred_element_type=jnp.float32) * scale
    tq, nk = s.shape
    nb = tq // BLOCK
    s3 = s.reshape(nb, BLOCK, nk)
    allowed = cm_ref[...] > 0.5
    lt = lt_ref[0].reshape(nb, BLOCK, 1)
    p = jnp.where(allowed, jnp.exp(s3 - lt), 0.0).reshape(tq, nk)
    dv_ref[0] += lax.dot_general(
        p.astype(jnp.bfloat16), ga, (((0,), (0,)), ((), ())), preferred_element_type=jnp.float32
    )
    dp = lax.dot_general(ga, v, (((1,), (1,)), ((), ())), preferred_element_type=jnp.float32)
    ds = (p * (dp - dl_ref[0]) * scale).astype(jnp.bfloat16)
    dq_ref[0] = jnp.dot(ds, k, preferred_element_type=jnp.float32)
    dk_ref[0] += lax.dot_general(
        ds, q, (((0,), (0,)), ((), ())), preferred_element_type=jnp.float32
    )


def _forward(qT, kT, vT, cm, scale):
    heads, nq, hd = qT.shape
    nk = kT.shape[1]
    nb = TQ // BLOCK
    f32 = jnp.float32
    return pl.pallas_call(
        functools.partial(_fwd_kernel, scale=scale),
        grid=(heads, nq // TQ),
        in_specs=[
            pl.BlockSpec((1, TQ, hd), lambda h, i: (h, i, 0)),
            pl.BlockSpec((1, nk, hd), lambda h, i: (h, 0, 0)),
            pl.BlockSpec((1, nk, hd), lambda h, i: (h, 0, 0)),
            pl.BlockSpec((nb, 1, nk), lambda h, i: (i, 0, 0)),
        ],
        out_specs=[
            pl.BlockSpec((1, TQ, hd), lambda h, i: (h, i, 0)),
            pl.BlockSpec((1, TQ, 1), lambda h, i: (h, i, 0)),
            pl.BlockSpec((1, TQ, 1), lambda h, i: (h, i, 0)),
        ],
        out_shape=[
            jax.ShapeDtypeStruct((heads, nq, hd), f32),
            jax.ShapeDtypeStruct((heads, nq, 1), f32),
            jax.ShapeDtypeStruct((heads, nq, 1), f32),
        ],
    )(qT, kT, vT, cm)


def _backward(qT, kT, vT, gaT, lt, dl, cm, scale):
    heads, nq, hd = qT.shape
    nk = kT.shape[1]
    nb = TQ // BLOCK
    f32 = jnp.float32
    return pl.pallas_call(
        functools.partial(_bwd_kernel, scale=scale),
        grid=(heads, nq // TQ),
        in_specs=[
            pl.BlockSpec((1, TQ, hd), lambda h, i: (h, i, 0)),
            pl.BlockSpec((1, nk, hd), lambda h, i: (h, 0, 0)),
            pl.BlockSpec((1, nk, hd), lambda h, i: (h, 0, 0)),
            pl.BlockSpec((1, TQ, hd), lambda h, i: (h, i, 0)),
            pl.BlockSpec((1, TQ, 1), lambda h, i: (h, i, 0)),
            pl.BlockSpec((1, TQ, 1), lambda h, i: (h, i, 0)),
            pl.BlockSpec((nb, 1, nk), lambda h, i: (i, 0, 0)),
        ],
        out_specs=[
            pl.BlockSpec((1, TQ, hd), lambda h, i: (h, i, 0)),
            pl.BlockSpec((1, nk, hd), lambda h, i: (h, 0, 0)),
            pl.BlockSpec((1, nk, hd), lambda h, i: (h, 0, 0)),
        ],
        out_shape=[
            jax.ShapeDtypeStruct((heads, nq, hd), f32),
            jax.ShapeDtypeStruct((heads, nk, hd), f32),
            jax.ShapeDtypeStruct((heads, nk, hd), f32),
        ],
        compiler_params=pltpu.CompilerParams(dimension_semantics=("parallel", "arbitrary")),
    )(qT, kT, vT, gaT, lt, dl, cm)


def on_device(queries_in, hits_in, w_query, w_key, w_value, w_out, mask_list, grad_out):
    f32 = jnp.float32
    bf16 = jnp.bfloat16
    region_index = lax.axis_index("region")
    n_queries, width = queries_in.shape
    n_hits = hits_in.shape[0]
    head_dim = width // HEADS
    scale = 1.0 / math.sqrt(head_dim)
    hit_blocks = n_hits // BLOCK
    q_blocks = n_queries // BLOCK
    local_ids = region_index * hit_blocks + jnp.arange(hit_blocks, dtype=jnp.int32)
    blockmask = jnp.any(mask_list[:, :, None] == local_ids[None, None, :], axis=1)
    cm = jnp.repeat(blockmask.astype(f32), BLOCK, axis=1).reshape(q_blocks, 1, n_hits)

    def heads(x):
        return x.reshape(x.shape[0], HEADS, head_dim).transpose(1, 0, 2)

    def joined(x):
        return x.transpose(1, 0, 2).reshape(x.shape[1], width)

    query = jnp.dot(queries_in, w_query, preferred_element_type=f32).astype(bf16)
    keys = jnp.dot(hits_in, w_key, preferred_element_type=f32).astype(bf16)
    vals = jnp.dot(hits_in, w_value, preferred_element_type=f32).astype(bf16)
    qT, kT, vT = heads(query), heads(keys), heads(vals)

    numer_r, max_r, total_r = _forward(qT, kT, vT, cm, scale)
    max_r = max_r.reshape(HEADS, n_queries)
    total_r = total_r.reshape(HEADS, n_queries)
    stats = lax.all_gather(jnp.concatenate([max_r, total_r], axis=0), "region")
    peak = jnp.max(stats[:, :HEADS], axis=0)
    total = jnp.sum(stats[:, HEADS:] * jnp.exp(stats[:, :HEADS] - peak[None]), axis=0)
    weight = jnp.exp(max_r - peak)
    spread = jnp.repeat(weight.T, head_dim, axis=1)
    numer = lax.psum((joined(numer_r) * spread).astype(bf16), "region").astype(f32)
    attended = (numer / jnp.repeat(total.T, head_dim, axis=1)).astype(bf16)
    log_total = (peak + jnp.log(total)).reshape(HEADS, n_queries, 1)
    attended_h = heads(attended)
    layer_out = (
        queries_in.astype(f32) + jnp.dot(attended, w_out, preferred_element_type=f32)
    ).astype(bf16)
    grad_att = lax.dot_general(
        grad_out, w_out, (((1,), (1,)), ((), ())), preferred_element_type=f32
    ).astype(bf16)
    grad_wo = jnp.einsum("qa,qb->ab", attended, grad_out, preferred_element_type=f32)
    gaT = heads(grad_att)
    deltas = jnp.sum(gaT.astype(f32) * attended_h.astype(f32), axis=2, keepdims=True)

    dq_r, dk, dv = _backward(qT, kT, vT, gaT, log_total, deltas, cm, scale)
    keys_grad = joined(dk).astype(bf16)
    vals_grad = joined(dv).astype(bf16)
    query_grad_local = joined(dq_r)
    wk_part = jnp.einsum("ka,kb->ab", hits_in, keys_grad, preferred_element_type=f32)
    wv_part = jnp.einsum("ka,kb->ab", hits_in, vals_grad, preferred_element_type=f32)
    query_grad_sum, grad_wk, grad_wv = lax.psum(
        (query_grad_local.astype(bf16), wk_part.astype(bf16), wv_part.astype(bf16)), "region"
    )
    grad_wk = grad_wk.astype(f32)
    grad_wv = grad_wv.astype(f32)
    grad_q = query_grad_sum
    grad_wq = jnp.einsum("qa,qb->ab", queries_in, grad_q, preferred_element_type=f32)
    grad_queries = (
        grad_out.astype(f32)
        + lax.dot_general(grad_q, w_query, (((1,), (1,)), ((), ())), preferred_element_type=f32)
    ).astype(bf16)
    grad_hits = (
        lax.dot_general(keys_grad, w_key, (((1,), (1,)), ((), ())), preferred_element_type=f32)
        + lax.dot_general(vals_grad, w_value, (((1,), (1,)), ((), ())), preferred_element_type=f32)
    ).astype(bf16)
    return (layer_out, grad_queries, grad_hits, grad_wq, grad_wk, grad_wv, grad_wo)


def solution(mesh):
    in_specs = (
        P("event", None),
        P(("event", "region"), None),
        P(),
        P(),
        P(),
        P(),
        P("event", None),
        P("event", None),
    )
    out_specs = (
        P("event", None),
        P("event", None),
        P(("event", "region"), None),
        P("event", None),
        P("event", None),
        P("event", None),
        P("event", None),
    )
    return jax.shard_map(
        on_device, mesh=mesh, in_specs=in_specs, out_specs=out_specs, check_vma=False
    )
```

```python
import functools
import math

import jax
import jax.numpy as jnp
from jax import lax
from jax.experimental import pallas as pl
from jax.experimental.pallas import tpu as pltpu
from jax.sharding import PartitionSpec as P

HEADS = 8
BLOCK = 128
TQ = 256


def _fwd_kernel(q_ref, k_ref, v_ref, cm_ref, numer_ref, m_ref, l_ref, *, scale):
    q = q_ref[0]
    k = k_ref[0]
    v = v_ref[0]
    s = lax.dot_general(q, k, (((1,), (1,)), ((), ())), preferred_element_type=jnp.float32) * scale
    tq, nk = s.shape
    nb = tq // BLOCK
    s3 = s.reshape(nb, BLOCK, nk)
    allowed = cm_ref[...] > 0.5
    masked = jnp.where(allowed, s3, -1e30)
    mx = jnp.max(masked, axis=2, keepdims=True)
    e = jnp.where(allowed, jnp.exp(masked - mx), 0.0)
    tot = jnp.sum(e, axis=2, keepdims=True)
    numer = jnp.dot(
        e.reshape(tq, nk).astype(jnp.bfloat16), v, preferred_element_type=jnp.float32
    )
    numer_ref[0] = numer
    m_ref[0] = mx.reshape(tq, 1)
    l_ref[0] = tot.reshape(tq, 1)


def _bwd_kernel(q_ref, k_ref, v_ref, ga_ref, lt_ref, dl_ref, cm_ref, dq_ref, dk_ref, dv_ref, *, scale):
    i = pl.program_id(1)

    @pl.when(i == 0)
    def _():
        dk_ref[...] = jnp.zeros_like(dk_ref)
        dv_ref[...] = jnp.zeros_like(dv_ref)

    q = q_ref[0]
    k = k_ref[0]
    v = v_ref[0]
    ga = ga_ref[0]
    s = lax.dot_general(q, k, (((1,), (1,)), ((), ())), preferred_element_type=jnp.float32) * scale
    tq, nk = s.shape
    nb = tq // BLOCK
    s3 = s.reshape(nb, BLOCK, nk)
    allowed = cm_ref[...] > 0.5
    lt = lt_ref[0].reshape(nb, BLOCK, 1)
    p = jnp.where(allowed, jnp.exp(s3 - lt), 0.0).reshape(tq, nk)
    dv_ref[0] += lax.dot_general(
        p.astype(jnp.bfloat16), ga, (((0,), (0,)), ((), ())), preferred_element_type=jnp.float32
    )
    dp = lax.dot_general(ga, v, (((1,), (1,)), ((), ())), preferred_element_type=jnp.float32)
    ds = (p * (dp - dl_ref[0]) * scale).astype(jnp.bfloat16)
    dq_ref[0] = jnp.dot(ds, k, preferred_element_type=jnp.float32)
    dk_ref[0] += lax.dot_general(
        ds, q, (((0,), (0,)), ((), ())), preferred_element_type=jnp.float32
    )


def _forward(qT, kT, vT, cm, scale):
    heads, nq, hd = qT.shape
    nk = kT.shape[1]
    nb = TQ // BLOCK
    f32 = jnp.float32
    return pl.pallas_call(
        functools.partial(_fwd_kernel, scale=scale),
        grid=(heads, nq // TQ),
        in_specs=[
            pl.BlockSpec((1, TQ, hd), lambda h, i: (h, i, 0)),
            pl.BlockSpec((1, nk, hd), lambda h, i: (h, 0, 0)),
            pl.BlockSpec((1, nk, hd), lambda h, i: (h, 0, 0)),
            pl.BlockSpec((nb, 1, nk), lambda h, i: (i, 0, 0)),
        ],
        out_specs=[
            pl.BlockSpec((1, TQ, hd), lambda h, i: (h, i, 0)),
            pl.BlockSpec((1, TQ, 1), lambda h, i: (h, i, 0)),
            pl.BlockSpec((1, TQ, 1), lambda h, i: (h, i, 0)),
        ],
        out_shape=[
            jax.ShapeDtypeStruct((heads, nq, hd), f32),
            jax.ShapeDtypeStruct((heads, nq, 1), f32),
            jax.ShapeDtypeStruct((heads, nq, 1), f32),
        ],
    )(qT, kT, vT, cm)


def _backward(qT, kT, vT, gaT, lt, dl, cm, scale):
    heads, nq, hd = qT.shape
    nk = kT.shape[1]
    nb = TQ // BLOCK
    f32 = jnp.float32
    return pl.pallas_call(
        functools.partial(_bwd_kernel, scale=scale),
        grid=(heads, nq // TQ),
        in_specs=[
            pl.BlockSpec((1, TQ, hd), lambda h, i: (h, i, 0)),
            pl.BlockSpec((1, nk, hd), lambda h, i: (h, 0, 0)),
            pl.BlockSpec((1, nk, hd), lambda h, i: (h, 0, 0)),
            pl.BlockSpec((1, TQ, hd), lambda h, i: (h, i, 0)),
            pl.BlockSpec((1, TQ, 1), lambda h, i: (h, i, 0)),
            pl.BlockSpec((1, TQ, 1), lambda h, i: (h, i, 0)),
            pl.BlockSpec((nb, 1, nk), lambda h, i: (i, 0, 0)),
        ],
        out_specs=[
            pl.BlockSpec((1, TQ, hd), lambda h, i: (h, i, 0)),
            pl.BlockSpec((1, nk, hd), lambda h, i: (h, 0, 0)),
            pl.BlockSpec((1, nk, hd), lambda h, i: (h, 0, 0)),
        ],
        out_shape=[
            jax.ShapeDtypeStruct((heads, nq, hd), f32),
            jax.ShapeDtypeStruct((heads, nk, hd), f32),
            jax.ShapeDtypeStruct((heads, nk, hd), f32),
        ],
        compiler_params=pltpu.CompilerParams(dimension_semantics=("parallel", "arbitrary")),
    )(qT, kT, vT, gaT, lt, dl, cm)


def on_device(queries_in, hits_in, w_query, w_key, w_value, w_out, mask_list, grad_out):
    f32 = jnp.float32
    bf16 = jnp.bfloat16
    region_index = lax.axis_index("region")
    n_queries, width = queries_in.shape
    n_hits = hits_in.shape[0]
    head_dim = width // HEADS
    scale = 1.0 / math.sqrt(head_dim)
    hit_blocks = n_hits // BLOCK
    q_blocks = n_queries // BLOCK
    local_ids = region_index * hit_blocks + jnp.arange(hit_blocks, dtype=jnp.int32)
    blockmask = jnp.any(mask_list[:, :, None] == local_ids[None, None, :], axis=1)
    cm = jnp.repeat(blockmask.astype(f32), BLOCK, axis=1).reshape(q_blocks, 1, n_hits)

    def heads(x):
        return x.reshape(x.shape[0], HEADS, head_dim).transpose(1, 0, 2)

    def joined(x):
        return x.transpose(1, 0, 2).reshape(x.shape[1], width)

    query = jnp.dot(queries_in, w_query, preferred_element_type=f32).astype(bf16)
    keys = jnp.dot(hits_in, w_key, preferred_element_type=f32).astype(bf16)
    vals = jnp.dot(hits_in, w_value, preferred_element_type=f32).astype(bf16)
    qT, kT, vT = heads(query), heads(keys), heads(vals)

    regions = lax.axis_size("region")
    numer_r, max_r, total_r = _forward(qT, kT, vT, cm, scale)
    numer = joined(numer_r)
    peak = max_r.reshape(HEADS, n_queries)
    total = total_r.reshape(HEADS, n_queries)
    rows = n_queries
    base = 0
    steps = []
    k = 0
    while (1 << k) < regions:
        bit = (region_index >> k) & 1
        half = rows // 2
        pairs = [(i, i ^ (1 << k)) for i in range(regions)]
        mine = (
            lax.dynamic_slice_in_dim(numer, bit * half, half, 0),
            lax.dynamic_slice_in_dim(peak, bit * half, half, 1),
            lax.dynamic_slice_in_dim(total, bit * half, half, 1),
        )
        theirs = lax.ppermute(
            (
                lax.dynamic_slice_in_dim(numer, (1 - bit) * half, half, 0),
                lax.dynamic_slice_in_dim(peak, (1 - bit) * half, half, 1),
                lax.dynamic_slice_in_dim(total, (1 - bit) * half, half, 1),
            ),
            "region",
            pairs,
        )
        top = jnp.maximum(mine[1], theirs[1])
        scale_a = jnp.exp(mine[1] - top)
        scale_b = jnp.exp(theirs[1] - top)
        numer = mine[0] * jnp.repeat(scale_a.T, head_dim, axis=1) + theirs[0] * jnp.repeat(
            scale_b.T, head_dim, axis=1
        )
        total = mine[2] * scale_a + theirs[2] * scale_b
        peak = top
        base = base + bit * half
        steps.append((k, bit, half))
        rows = half
        k += 1
    attended_part = (numer / jnp.repeat(total.T, head_dim, axis=1)).astype(bf16)
    log_part = peak + jnp.log(total)
    grad_att = lax.dot_general(
        grad_out, w_out, (((1,), (1,)), ((), ())), preferred_element_type=f32
    ).astype(bf16)
    grad_att_part = lax.dynamic_slice_in_dim(grad_att, base, rows, 0)
    delta_part = jnp.sum(
        (grad_att_part.astype(f32) * attended_part.astype(f32)).reshape(rows, HEADS, head_dim),
        axis=2,
    ).T
    gathered = (attended_part, jnp.concatenate([log_part, delta_part], axis=0))
    for k, bit, half in reversed(steps):
        pairs = [(i, i ^ (1 << k)) for i in range(regions)]
        other = lax.ppermute(gathered, "region", pairs)
        lo = jax.tree.map(lambda a, b: jnp.where(bit == 0, a, b), gathered, other)
        hi = jax.tree.map(lambda a, b: jnp.where(bit == 0, b, a), gathered, other)
        gathered = (
            jnp.concatenate([lo[0], hi[0]], axis=0),
            jnp.concatenate([lo[1], hi[1]], axis=1),
        )
    attended = gathered[0]
    log_total = gathered[1][:HEADS].reshape(HEADS, n_queries, 1)
    deltas = gathered[1][HEADS:].reshape(HEADS, n_queries, 1)
    layer_out = (
        queries_in.astype(f32) + jnp.dot(attended, w_out, preferred_element_type=f32)
    ).astype(bf16)
    grad_wo = jnp.einsum("qa,qb->ab", attended, grad_out, preferred_element_type=f32)
    gaT = heads(grad_att)

    dq_r, dk, dv = _backward(qT, kT, vT, gaT, log_total, deltas, cm, scale)
    keys_grad = joined(dk).astype(bf16)
    vals_grad = joined(dv).astype(bf16)
    wk_part = jnp.einsum("ka,kb->ab", hits_in, keys_grad, preferred_element_type=f32)
    wv_part = jnp.einsum("ka,kb->ab", hits_in, vals_grad, preferred_element_type=f32)
    summed = jnp.concatenate([joined(dq_r), wk_part, wv_part], axis=0)
    for k, bit, half in steps:
        half = summed.shape[0] // 2
        pairs = [(i, i ^ (1 << k)) for i in range(regions)]
        other = lax.ppermute(lax.dynamic_slice_in_dim(summed, (1 - bit) * half, half, 0), "region", pairs)
        summed = lax.dynamic_slice_in_dim(summed, bit * half, half, 0) + other
    for k, bit, half in reversed(steps):
        pairs = [(i, i ^ (1 << k)) for i in range(regions)]
        other = lax.ppermute(summed, "region", pairs)
        summed = jnp.concatenate(
            [jnp.where(bit == 0, summed, other), jnp.where(bit == 0, other, summed)], axis=0
        )
    query_grad_sum = summed[:n_queries].astype(bf16)
    grad_wk = summed[n_queries : n_queries + width]
    grad_wv = summed[n_queries + width :]
    grad_q = query_grad_sum
    grad_wq = jnp.einsum("qa,qb->ab", queries_in, grad_q, preferred_element_type=f32)
    grad_queries = (
        grad_out.astype(f32)
        + lax.dot_general(grad_q, w_query, (((1,), (1,)), ((), ())), preferred_element_type=f32)
    ).astype(bf16)
    grad_hits = (
        lax.dot_general(keys_grad, w_key, (((1,), (1,)), ((), ())), preferred_element_type=f32)
        + lax.dot_general(vals_grad, w_value, (((1,), (1,)), ((), ())), preferred_element_type=f32)
    ).astype(bf16)
    return (layer_out, grad_queries, grad_hits, grad_wq, grad_wk, grad_wv, grad_wo)


def solution(mesh):
    in_specs = (
        P("event", None),
        P(("event", "region"), None),
        P(),
        P(),
        P(),
        P(),
        P("event", None),
        P("event", None),
    )
    out_specs = (
        P("event", None),
        P("event", None),
        P(("event", "region"), None),
        P("event", None),
        P("event", None),
        P("event", None),
        P("event", None),
    )
    return jax.shard_map(
        on_device, mesh=mesh, in_specs=in_specs, out_specs=out_specs, check_vma=False
    )
```

```python
import functools
import math

import jax
import jax.numpy as jnp
from jax import lax
from jax.experimental import pallas as pl
from jax.experimental.pallas import tpu as pltpu
from jax.sharding import PartitionSpec as P

HEADS = 8
BLOCK = 128
TQ = 256


def _fwd_kernel(q_ref, k_ref, v_ref, cm_ref, numer_ref, m_ref, l_ref, *, scale):
    q = q_ref[0]
    k = k_ref[0]
    v = v_ref[0]
    s = lax.dot_general(q, k, (((1,), (1,)), ((), ())), preferred_element_type=jnp.float32) * scale
    tq, nk = s.shape
    nb = tq // BLOCK
    s3 = s.reshape(nb, BLOCK, nk)
    allowed = cm_ref[...] > 0.5
    masked = jnp.where(allowed, s3, -1e30)
    mx = jnp.max(masked, axis=2, keepdims=True)
    e = jnp.where(allowed, jnp.exp(masked - mx), 0.0)
    tot = jnp.sum(e, axis=2, keepdims=True)
    numer = jnp.dot(
        e.reshape(tq, nk).astype(jnp.bfloat16), v, preferred_element_type=jnp.float32
    )
    numer_ref[0] = numer
    m_ref[0] = mx.reshape(tq, 1)
    l_ref[0] = tot.reshape(tq, 1)


def _bwd_kernel(q_ref, k_ref, v_ref, ga_ref, lt_ref, dl_ref, cm_ref, dq_ref, dk_ref, dv_ref, *, scale):
    i = pl.program_id(1)

    @pl.when(i == 0)
    def _():
        dk_ref[...] = jnp.zeros_like(dk_ref)
        dv_ref[...] = jnp.zeros_like(dv_ref)

    q = q_ref[0]
    k = k_ref[0]
    v = v_ref[0]
    ga = ga_ref[0]
    s = lax.dot_general(q, k, (((1,), (1,)), ((), ())), preferred_element_type=jnp.float32) * scale
    tq, nk = s.shape
    nb = tq // BLOCK
    s3 = s.reshape(nb, BLOCK, nk)
    allowed = cm_ref[...] > 0.5
    lt = lt_ref[0].reshape(nb, BLOCK, 1)
    p = jnp.where(allowed, jnp.exp(s3 - lt), 0.0).reshape(tq, nk)
    dv_ref[0] += lax.dot_general(
        p.astype(jnp.bfloat16), ga, (((0,), (0,)), ((), ())), preferred_element_type=jnp.float32
    )
    dp = lax.dot_general(ga, v, (((1,), (1,)), ((), ())), preferred_element_type=jnp.float32)
    ds = (p * (dp - dl_ref[0]) * scale).astype(jnp.bfloat16)
    dq_ref[0] = jnp.dot(ds, k, preferred_element_type=jnp.float32)
    dk_ref[0] += lax.dot_general(
        ds, q, (((0,), (0,)), ((), ())), preferred_element_type=jnp.float32
    )


def _forward(qT, kT, vT, cm, scale):
    heads, nq, hd = qT.shape
    nk = kT.shape[1]
    nb = TQ // BLOCK
    f32 = jnp.float32
    return pl.pallas_call(
        functools.partial(_fwd_kernel, scale=scale),
        grid=(heads, nq // TQ),
        in_specs=[
            pl.BlockSpec((1, TQ, hd), lambda h, i: (h, i, 0)),
            pl.BlockSpec((1, nk, hd), lambda h, i: (h, 0, 0)),
            pl.BlockSpec((1, nk, hd), lambda h, i: (h, 0, 0)),
            pl.BlockSpec((nb, 1, nk), lambda h, i: (i, 0, 0)),
        ],
        out_specs=[
            pl.BlockSpec((1, TQ, hd), lambda h, i: (h, i, 0)),
            pl.BlockSpec((1, TQ, 1), lambda h, i: (h, i, 0)),
            pl.BlockSpec((1, TQ, 1), lambda h, i: (h, i, 0)),
        ],
        out_shape=[
            jax.ShapeDtypeStruct((heads, nq, hd), f32),
            jax.ShapeDtypeStruct((heads, nq, 1), f32),
            jax.ShapeDtypeStruct((heads, nq, 1), f32),
        ],
    )(qT, kT, vT, cm)


def _backward(qT, kT, vT, gaT, lt, dl, cm, scale):
    heads, nq, hd = qT.shape
    nk = kT.shape[1]
    nb = TQ // BLOCK
    f32 = jnp.float32
    return pl.pallas_call(
        functools.partial(_bwd_kernel, scale=scale),
        grid=(heads, nq // TQ),
        in_specs=[
            pl.BlockSpec((1, TQ, hd), lambda h, i: (h, i, 0)),
            pl.BlockSpec((1, nk, hd), lambda h, i: (h, 0, 0)),
            pl.BlockSpec((1, nk, hd), lambda h, i: (h, 0, 0)),
            pl.BlockSpec((1, TQ, hd), lambda h, i: (h, i, 0)),
            pl.BlockSpec((1, TQ, 1), lambda h, i: (h, i, 0)),
            pl.BlockSpec((1, TQ, 1), lambda h, i: (h, i, 0)),
            pl.BlockSpec((nb, 1, nk), lambda h, i: (i, 0, 0)),
        ],
        out_specs=[
            pl.BlockSpec((1, TQ, hd), lambda h, i: (h, i, 0)),
            pl.BlockSpec((1, nk, hd), lambda h, i: (h, 0, 0)),
            pl.BlockSpec((1, nk, hd), lambda h, i: (h, 0, 0)),
        ],
        out_shape=[
            jax.ShapeDtypeStruct((heads, nq, hd), f32),
            jax.ShapeDtypeStruct((heads, nk, hd), f32),
            jax.ShapeDtypeStruct((heads, nk, hd), f32),
        ],
        compiler_params=pltpu.CompilerParams(dimension_semantics=("parallel", "arbitrary")),
    )(qT, kT, vT, gaT, lt, dl, cm)


def on_device(queries_in, hits_in, w_query, w_key, w_value, w_out, mask_list, grad_out):
    f32 = jnp.float32
    bf16 = jnp.bfloat16
    region_index = lax.axis_index("region")
    n_queries, width = queries_in.shape
    n_hits = hits_in.shape[0]
    head_dim = width // HEADS
    scale = 1.0 / math.sqrt(head_dim)
    hit_blocks = n_hits // BLOCK
    q_blocks = n_queries // BLOCK
    local_ids = region_index * hit_blocks + jnp.arange(hit_blocks, dtype=jnp.int32)
    blockmask = jnp.any(mask_list[:, :, None] == local_ids[None, None, :], axis=1)
    cm = jnp.repeat(blockmask.astype(f32), BLOCK, axis=1).reshape(q_blocks, 1, n_hits)

    def heads(x):
        return x.reshape(x.shape[0], HEADS, head_dim).transpose(1, 0, 2)

    def joined(x):
        return x.transpose(1, 0, 2).reshape(x.shape[1], width)

    query = jnp.dot(queries_in, w_query, preferred_element_type=f32).astype(bf16)
    keys = jnp.dot(hits_in, w_key, preferred_element_type=f32).astype(bf16)
    vals = jnp.dot(hits_in, w_value, preferred_element_type=f32).astype(bf16)
    qT, kT, vT = heads(query), heads(keys), heads(vals)

    regions = lax.axis_size("region")
    numer_r, max_r, total_r = _forward(qT, kT, vT, cm, scale)
    numer = joined(numer_r)
    peak = max_r.reshape(HEADS, n_queries)
    total = total_r.reshape(HEADS, n_queries)
    rows = n_queries
    base = 0
    steps = []
    k = 0
    while (1 << k) < regions:
        bit = (region_index >> k) & 1
        half = rows // 2
        pairs = [(i, i ^ (1 << k)) for i in range(regions)]
        mine = (
            lax.dynamic_slice_in_dim(numer, bit * half, half, 0),
            lax.dynamic_slice_in_dim(peak, bit * half, half, 1),
            lax.dynamic_slice_in_dim(total, bit * half, half, 1),
        )
        theirs = lax.ppermute(
            (
                lax.dynamic_slice_in_dim(numer, (1 - bit) * half, half, 0),
                lax.dynamic_slice_in_dim(peak, (1 - bit) * half, half, 1),
                lax.dynamic_slice_in_dim(total, (1 - bit) * half, half, 1),
            ),
            "region",
            pairs,
        )
        top = jnp.maximum(mine[1], theirs[1])
        scale_a = jnp.exp(mine[1] - top)
        scale_b = jnp.exp(theirs[1] - top)
        numer = mine[0] * jnp.repeat(scale_a.T, head_dim, axis=1) + theirs[0] * jnp.repeat(
            scale_b.T, head_dim, axis=1
        )
        total = mine[2] * scale_a + theirs[2] * scale_b
        peak = top
        base = base + bit * half
        steps.append((k, bit, half))
        rows = half
        k += 1
    attended_part = (numer / jnp.repeat(total.T, head_dim, axis=1)).astype(bf16)
    log_part = peak + jnp.log(total)
    grad_att = lax.dot_general(
        grad_out, w_out, (((1,), (1,)), ((), ())), preferred_element_type=f32
    ).astype(bf16)
    grad_att_part = lax.dynamic_slice_in_dim(grad_att, base, rows, 0)
    delta_part = jnp.sum(
        (grad_att_part.astype(f32) * attended_part.astype(f32)).reshape(rows, HEADS, head_dim),
        axis=2,
    ).T
    gathered = (attended_part, jnp.concatenate([log_part, delta_part], axis=0))
    for k, bit, half in reversed(steps):
        pairs = [(i, i ^ (1 << k)) for i in range(regions)]
        other = lax.ppermute(gathered, "region", pairs)
        lo = jax.tree.map(lambda a, b: jnp.where(bit == 0, a, b), gathered, other)
        hi = jax.tree.map(lambda a, b: jnp.where(bit == 0, b, a), gathered, other)
        gathered = (
            jnp.concatenate([lo[0], hi[0]], axis=0),
            jnp.concatenate([lo[1], hi[1]], axis=1),
        )
    attended = gathered[0]
    log_total = gathered[1][:HEADS].reshape(HEADS, n_queries, 1)
    deltas = gathered[1][HEADS:].reshape(HEADS, n_queries, 1)
    layer_out = (
        queries_in.astype(f32) + jnp.dot(attended, w_out, preferred_element_type=f32)
    ).astype(bf16)
    grad_wo = jnp.einsum("qa,qb->ab", attended, grad_out, preferred_element_type=f32)
    gaT = heads(grad_att)

    dq_r, dk, dv = _backward(qT, kT, vT, gaT, log_total, deltas, cm, scale)
    keys_grad = joined(dk).astype(bf16)
    vals_grad = joined(dv).astype(bf16)
    wk_part = jnp.einsum("ka,kb->ab", hits_in, keys_grad, preferred_element_type=f32)
    wv_part = jnp.einsum("ka,kb->ab", hits_in, vals_grad, preferred_element_type=f32)
    query_grad_sum, grad_wk, grad_wv = lax.psum(
        (joined(dq_r).astype(bf16), wk_part.astype(bf16), wv_part.astype(bf16)), "region"
    )
    grad_wk = grad_wk.astype(f32)
    grad_wv = grad_wv.astype(f32)
    grad_q = query_grad_sum
    grad_wq = jnp.einsum("qa,qb->ab", queries_in, grad_q, preferred_element_type=f32)
    grad_queries = (
        grad_out.astype(f32)
        + lax.dot_general(grad_q, w_query, (((1,), (1,)), ((), ())), preferred_element_type=f32)
    ).astype(bf16)
    grad_hits = (
        lax.dot_general(keys_grad, w_key, (((1,), (1,)), ((), ())), preferred_element_type=f32)
        + lax.dot_general(vals_grad, w_value, (((1,), (1,)), ((), ())), preferred_element_type=f32)
    ).astype(bf16)
    return (layer_out, grad_queries, grad_hits, grad_wq, grad_wk, grad_wv, grad_wo)


def solution(mesh):
    in_specs = (
        P("event", None),
        P(("event", "region"), None),
        P(),
        P(),
        P(),
        P(),
        P("event", None),
        P("event", None),
    )
    out_specs = (
        P("event", None),
        P("event", None),
        P(("event", "region"), None),
        P("event", None),
        P("event", None),
        P("event", None),
        P("event", None),
    )
    return jax.shard_map(
        on_device, mesh=mesh, in_specs=in_specs, out_specs=out_specs, check_vma=False
    )
```

```python
import functools
import math

import jax
import jax.numpy as jnp
from jax import lax
from jax.experimental import pallas as pl
from jax.experimental.pallas import tpu as pltpu
from jax.sharding import PartitionSpec as P

HEADS = 8
BLOCK = 128
TQ = 256


def _fwd_kernel(need_ref, q_ref, k_ref, v_ref, cm_ref, numer_ref, m_ref, l_ref, s_scr, m_scr, l_scr, acc_scr, *, scale):
    i = pl.program_id(1)
    n_tiles = pl.num_programs(1)
    q = q_ref[0]
    tq = q.shape[0]
    nk = k_ref.shape[1]
    nb = tq // BLOCK
    chunks = nk // BLOCK
    m_scr[...] = jnp.full(m_scr.shape, -1e30, jnp.float32)
    l_scr[...] = jnp.zeros(l_scr.shape, jnp.float32)
    acc_scr[...] = jnp.zeros(acc_scr.shape, jnp.float32)
    for c in range(chunks):
        @pl.when(need_ref[i * chunks + c] != 0)
        def _():
            k = k_ref[0, c * BLOCK : (c + 1) * BLOCK, :]
            s = lax.dot_general(q, k, (((1,), (1,)), ((), ())), preferred_element_type=jnp.float32) * scale
            allowed = cm_ref[:, :, c * BLOCK : (c + 1) * BLOCK] > 0.5
            masked = jnp.where(allowed, s.reshape(nb, BLOCK, BLOCK), -1e30)
            s_scr[c] = masked.reshape(tq, BLOCK)
            m_scr[...] = jnp.maximum(m_scr[...], jnp.max(masked, axis=2, keepdims=True).reshape(tq, 1))

    for c in range(chunks):
        @pl.when(need_ref[i * chunks + c] != 0)
        def _():
            allowed = cm_ref[:, :, c * BLOCK : (c + 1) * BLOCK] > 0.5
            mx = m_scr[...].reshape(nb, BLOCK, 1)
            e = jnp.where(allowed, jnp.exp(s_scr[c].reshape(nb, BLOCK, BLOCK) - mx), 0.0).reshape(tq, BLOCK)
            l_scr[...] += jnp.sum(e, axis=1, keepdims=True)
            v = v_ref[0, c * BLOCK : (c + 1) * BLOCK, :]
            acc_scr[...] += jnp.dot(e.astype(jnp.bfloat16), v, preferred_element_type=jnp.float32)

    numer_ref[0] = acc_scr[...]
    m_ref[0] = m_scr[...]
    l_ref[0] = l_scr[...]


def _bwd_kernel(need_ref, q_ref, k_ref, v_ref, ga_ref, lt_ref, dl_ref, cm_ref, dq_ref, dk_ref, dv_ref, dq_scr, *, scale):
    i = pl.program_id(1)

    @pl.when(i == 0)
    def _():
        dk_ref[...] = jnp.zeros_like(dk_ref)
        dv_ref[...] = jnp.zeros_like(dv_ref)

    q = q_ref[0]
    ga = ga_ref[0]
    tq = q.shape[0]
    nk = k_ref.shape[1]
    nb = tq // BLOCK
    chunks = nk // BLOCK
    dq_scr[...] = jnp.zeros(dq_scr.shape, jnp.float32)
    for c in range(chunks):
        @pl.when(need_ref[i * chunks + c] != 0)
        def _():
            k = k_ref[0, c * BLOCK : (c + 1) * BLOCK, :]
            v = v_ref[0, c * BLOCK : (c + 1) * BLOCK, :]
            s = lax.dot_general(q, k, (((1,), (1,)), ((), ())), preferred_element_type=jnp.float32) * scale
            allowed = cm_ref[:, :, c * BLOCK : (c + 1) * BLOCK] > 0.5
            lt = lt_ref[0].reshape(nb, BLOCK, 1)
            p = jnp.where(allowed, jnp.exp(s.reshape(nb, BLOCK, BLOCK) - lt), 0.0).reshape(tq, BLOCK)
            dv_ref[0, c * BLOCK : (c + 1) * BLOCK, :] += lax.dot_general(
                p.astype(jnp.bfloat16), ga, (((0,), (0,)), ((), ())), preferred_element_type=jnp.float32
            )
            dp = lax.dot_general(ga, v, (((1,), (1,)), ((), ())), preferred_element_type=jnp.float32)
            ds = (p * (dp - dl_ref[0]) * scale).astype(jnp.bfloat16)
            dq_scr[...] += jnp.dot(ds, k, preferred_element_type=jnp.float32)
            dk_ref[0, c * BLOCK : (c + 1) * BLOCK, :] += lax.dot_general(
                ds, q, (((0,), (0,)), ((), ())), preferred_element_type=jnp.float32
            )

    dq_ref[0] = dq_scr[...]


def _forward(need, qT, kT, vT, cm, scale):
    heads, nq, hd = qT.shape
    nk = kT.shape[1]
    nb = TQ // BLOCK
    f32 = jnp.float32
    grid_spec = pltpu.PrefetchScalarGridSpec(
        num_scalar_prefetch=1,
        grid=(heads, nq // TQ),
        in_specs=[
            pl.BlockSpec((1, TQ, hd), lambda h, i, n: (h, i, 0)),
            pl.BlockSpec((1, nk, hd), lambda h, i, n: (h, 0, 0)),
            pl.BlockSpec((1, nk, hd), lambda h, i, n: (h, 0, 0)),
            pl.BlockSpec((nb, 1, nk), lambda h, i, n: (i, 0, 0)),
        ],
        out_specs=[
            pl.BlockSpec((1, TQ, hd), lambda h, i, n: (h, i, 0)),
            pl.BlockSpec((1, TQ, 1), lambda h, i, n: (h, i, 0)),
            pl.BlockSpec((1, TQ, 1), lambda h, i, n: (h, i, 0)),
        ],
        scratch_shapes=[
            pltpu.VMEM((nk // BLOCK, TQ, BLOCK), f32),
            pltpu.VMEM((TQ, 1), f32),
            pltpu.VMEM((TQ, 1), f32),
            pltpu.VMEM((TQ, hd), f32),
        ],
    )
    return pl.pallas_call(
        functools.partial(_fwd_kernel, scale=scale),
        grid_spec=grid_spec,
        out_shape=[
            jax.ShapeDtypeStruct((heads, nq, hd), f32),
            jax.ShapeDtypeStruct((heads, nq, 1), f32),
            jax.ShapeDtypeStruct((heads, nq, 1), f32),
        ],
    )(need, qT, kT, vT, cm)


def _backward(need, qT, kT, vT, gaT, lt, dl, cm, scale):
    heads, nq, hd = qT.shape
    nk = kT.shape[1]
    nb = TQ // BLOCK
    f32 = jnp.float32
    grid_spec = pltpu.PrefetchScalarGridSpec(
        num_scalar_prefetch=1,
        grid=(heads, nq // TQ),
        in_specs=[
            pl.BlockSpec((1, TQ, hd), lambda h, i, n: (h, i, 0)),
            pl.BlockSpec((1, nk, hd), lambda h, i, n: (h, 0, 0)),
            pl.BlockSpec((1, nk, hd), lambda h, i, n: (h, 0, 0)),
            pl.BlockSpec((1, TQ, hd), lambda h, i, n: (h, i, 0)),
            pl.BlockSpec((1, TQ, 1), lambda h, i, n: (h, i, 0)),
            pl.BlockSpec((1, TQ, 1), lambda h, i, n: (h, i, 0)),
            pl.BlockSpec((nb, 1, nk), lambda h, i, n: (i, 0, 0)),
        ],
        out_specs=[
            pl.BlockSpec((1, TQ, hd), lambda h, i, n: (h, i, 0)),
            pl.BlockSpec((1, nk, hd), lambda h, i, n: (h, 0, 0)),
            pl.BlockSpec((1, nk, hd), lambda h, i, n: (h, 0, 0)),
        ],
        scratch_shapes=[pltpu.VMEM((TQ, hd), f32)],
    )
    return pl.pallas_call(
        functools.partial(_bwd_kernel, scale=scale),
        grid_spec=grid_spec,
        out_shape=[
            jax.ShapeDtypeStruct((heads, nq, hd), f32),
            jax.ShapeDtypeStruct((heads, nk, hd), f32),
            jax.ShapeDtypeStruct((heads, nk, hd), f32),
        ],
        compiler_params=pltpu.CompilerParams(dimension_semantics=("parallel", "arbitrary")),
    )(need, qT, kT, vT, gaT, lt, dl, cm)


def on_device(queries_in, hits_in, w_query, w_key, w_value, w_out, mask_list, grad_out):
    f32 = jnp.float32
    bf16 = jnp.bfloat16
    region_index = lax.axis_index("region")
    n_queries, width = queries_in.shape
    n_hits = hits_in.shape[0]
    head_dim = width // HEADS
    scale = 1.0 / math.sqrt(head_dim)
    hit_blocks = n_hits // BLOCK
    q_blocks = n_queries // BLOCK
    local_ids = region_index * hit_blocks + jnp.arange(hit_blocks, dtype=jnp.int32)
    blockmask = jnp.any(mask_list[:, :, None] == local_ids[None, None, :], axis=1)
    cm = jnp.repeat(blockmask.astype(f32), BLOCK, axis=1).reshape(q_blocks, 1, n_hits)
    need = jnp.any(blockmask.reshape(n_queries // TQ, TQ // BLOCK, hit_blocks), axis=1).astype(jnp.int32).reshape(-1)

    def heads(x):
        return x.reshape(x.shape[0], HEADS, head_dim).transpose(1, 0, 2)

    def joined(x):
        return x.transpose(1, 0, 2).reshape(x.shape[1], width)

    query = jnp.dot(queries_in, w_query, preferred_element_type=f32).astype(bf16)
    keys = jnp.dot(hits_in, w_key, preferred_element_type=f32).astype(bf16)
    vals = jnp.dot(hits_in, w_value, preferred_element_type=f32).astype(bf16)
    qT, kT, vT = heads(query), heads(keys), heads(vals)

    regions = lax.axis_size("region")
    numer_r, max_r, total_r = _forward(need, qT, kT, vT, cm, scale)
    numer = joined(numer_r)
    peak = max_r.reshape(HEADS, n_queries)
    total = total_r.reshape(HEADS, n_queries)
    rows = n_queries
    base = 0
    steps = []
    k = 0
    while (1 << k) < regions:
        bit = (region_index >> k) & 1
        half = rows // 2
        pairs = [(i, i ^ (1 << k)) for i in range(regions)]
        mine = (
            lax.dynamic_slice_in_dim(numer, bit * half, half, 0),
            lax.dynamic_slice_in_dim(peak, bit * half, half, 1),
            lax.dynamic_slice_in_dim(total, bit * half, half, 1),
        )
        theirs = lax.ppermute(
            (
                lax.dynamic_slice_in_dim(numer, (1 - bit) * half, half, 0),
                lax.dynamic_slice_in_dim(peak, (1 - bit) * half, half, 1),
                lax.dynamic_slice_in_dim(total, (1 - bit) * half, half, 1),
            ),
            "region",
            pairs,
        )
        top = jnp.maximum(mine[1], theirs[1])
        scale_a = jnp.exp(mine[1] - top)
        scale_b = jnp.exp(theirs[1] - top)
        numer = mine[0] * jnp.repeat(scale_a.T, head_dim, axis=1) + theirs[0] * jnp.repeat(
            scale_b.T, head_dim, axis=1
        )
        total = mine[2] * scale_a + theirs[2] * scale_b
        peak = top
        base = base + bit * half
        steps.append((k, bit, half))
        rows = half
        k += 1
    attended_part = (numer / jnp.repeat(total.T, head_dim, axis=1)).astype(bf16)
    log_part = peak + jnp.log(total)
    grad_att = lax.dot_general(
        grad_out, w_out, (((1,), (1,)), ((), ())), preferred_element_type=f32
    ).astype(bf16)
    grad_att_part = lax.dynamic_slice_in_dim(grad_att, base, rows, 0)
    delta_part = jnp.sum(
        (grad_att_part.astype(f32) * attended_part.astype(f32)).reshape(rows, HEADS, head_dim),
        axis=2,
    ).T
    gathered = (attended_part, jnp.concatenate([log_part, delta_part], axis=0))
    for k, bit, half in reversed(steps):
        pairs = [(i, i ^ (1 << k)) for i in range(regions)]
        other = lax.ppermute(gathered, "region", pairs)
        lo = jax.tree.map(lambda a, b: jnp.where(bit == 0, a, b), gathered, other)
        hi = jax.tree.map(lambda a, b: jnp.where(bit == 0, b, a), gathered, other)
        gathered = (
            jnp.concatenate([lo[0], hi[0]], axis=0),
            jnp.concatenate([lo[1], hi[1]], axis=1),
        )
    attended = gathered[0]
    log_total = gathered[1][:HEADS].reshape(HEADS, n_queries, 1)
    deltas = gathered[1][HEADS:].reshape(HEADS, n_queries, 1)
    layer_out = (
        queries_in.astype(f32) + jnp.dot(attended, w_out, preferred_element_type=f32)
    ).astype(bf16)
    grad_wo = jnp.einsum("qa,qb->ab", attended, grad_out, preferred_element_type=f32)
    gaT = heads(grad_att)

    dq_r, dk, dv = _backward(need, qT, kT, vT, gaT, log_total, deltas, cm, scale)
    keys_grad = joined(dk).astype(bf16)
    vals_grad = joined(dv).astype(bf16)
    wk_part = jnp.einsum("ka,kb->ab", hits_in, keys_grad, preferred_element_type=f32)
    wv_part = jnp.einsum("ka,kb->ab", hits_in, vals_grad, preferred_element_type=f32)
    query_grad_sum, grad_wk, grad_wv = lax.psum(
        (joined(dq_r).astype(bf16), wk_part.astype(bf16), wv_part.astype(bf16)), "region"
    )
    grad_wk = grad_wk.astype(f32)
    grad_wv = grad_wv.astype(f32)
    grad_q = query_grad_sum
    grad_wq = jnp.einsum("qa,qb->ab", queries_in, grad_q, preferred_element_type=f32)
    grad_queries = (
        grad_out.astype(f32)
        + lax.dot_general(grad_q, w_query, (((1,), (1,)), ((), ())), preferred_element_type=f32)
    ).astype(bf16)
    grad_hits = (
        lax.dot_general(keys_grad, w_key, (((1,), (1,)), ((), ())), preferred_element_type=f32)
        + lax.dot_general(vals_grad, w_value, (((1,), (1,)), ((), ())), preferred_element_type=f32)
    ).astype(bf16)
    return (layer_out, grad_queries, grad_hits, grad_wq, grad_wk, grad_wv, grad_wo)


def solution(mesh):
    in_specs = (
        P("event", None),
        P(("event", "region"), None),
        P(),
        P(),
        P(),
        P(),
        P("event", None),
        P("event", None),
    )
    out_specs = (
        P("event", None),
        P("event", None),
        P(("event", "region"), None),
        P("event", None),
        P("event", None),
        P("event", None),
        P("event", None),
    )
    return jax.shard_map(
        on_device, mesh=mesh, in_specs=in_specs, out_specs=out_specs, check_vma=False
    )
```

```python
import functools
import math

import jax
import jax.numpy as jnp
from jax import lax
from jax.experimental import pallas as pl
from jax.experimental.pallas import tpu as pltpu
from jax.sharding import PartitionSpec as P

HEADS = 8
BLOCK = 128
TQ = 512


def _fwd_kernel(q_ref, k_ref, v_ref, cm_ref, numer_ref, m_ref, l_ref, *, scale):
    q = q_ref[0]
    k = k_ref[0]
    v = v_ref[0]
    s = lax.dot_general(q, k, (((1,), (1,)), ((), ())), preferred_element_type=jnp.float32) * scale
    tq, nk = s.shape
    nb = tq // BLOCK
    s3 = s.reshape(nb, BLOCK, nk)
    allowed = cm_ref[...] > 0.5
    masked = jnp.where(allowed, s3, -1e30)
    mx = jnp.max(masked, axis=2, keepdims=True)
    e = jnp.where(allowed, jnp.exp(masked - mx), 0.0)
    tot = jnp.sum(e, axis=2, keepdims=True)
    numer = jnp.dot(
        e.reshape(tq, nk).astype(jnp.bfloat16), v, preferred_element_type=jnp.float32
    )
    numer_ref[0] = numer
    m_ref[0] = mx.reshape(tq, 1)
    l_ref[0] = tot.reshape(tq, 1)


def _bwd_kernel(q_ref, k_ref, v_ref, ga_ref, lt_ref, dl_ref, cm_ref, dq_ref, dk_ref, dv_ref, *, scale):
    i = pl.program_id(1)

    @pl.when(i == 0)
    def _():
        dk_ref[...] = jnp.zeros_like(dk_ref)
        dv_ref[...] = jnp.zeros_like(dv_ref)

    q = q_ref[0]
    k = k_ref[0]
    v = v_ref[0]
    ga = ga_ref[0]
    s = lax.dot_general(q, k, (((1,), (1,)), ((), ())), preferred_element_type=jnp.float32) * scale
    tq, nk = s.shape
    nb = tq // BLOCK
    s3 = s.reshape(nb, BLOCK, nk)
    allowed = cm_ref[...] > 0.5
    lt = lt_ref[0].reshape(nb, BLOCK, 1)
    p = jnp.where(allowed, jnp.exp(s3 - lt), 0.0).reshape(tq, nk)
    dv_ref[0] += lax.dot_general(
        p.astype(jnp.bfloat16), ga, (((0,), (0,)), ((), ())), preferred_element_type=jnp.float32
    )
    dp = lax.dot_general(ga, v, (((1,), (1,)), ((), ())), preferred_element_type=jnp.float32)
    ds = (p * (dp - dl_ref[0]) * scale).astype(jnp.bfloat16)
    dq_ref[0] = jnp.dot(ds, k, preferred_element_type=jnp.float32)
    dk_ref[0] += lax.dot_general(
        ds, q, (((0,), (0,)), ((), ())), preferred_element_type=jnp.float32
    )


def _forward(qT, kT, vT, cm, scale):
    heads, nq, hd = qT.shape
    nk = kT.shape[1]
    nb = TQ // BLOCK
    f32 = jnp.float32
    return pl.pallas_call(
        functools.partial(_fwd_kernel, scale=scale),
        grid=(heads, nq // TQ),
        in_specs=[
            pl.BlockSpec((1, TQ, hd), lambda h, i: (h, i, 0)),
            pl.BlockSpec((1, nk, hd), lambda h, i: (h, 0, 0)),
            pl.BlockSpec((1, nk, hd), lambda h, i: (h, 0, 0)),
            pl.BlockSpec((nb, 1, nk), lambda h, i: (i, 0, 0)),
        ],
        out_specs=[
            pl.BlockSpec((1, TQ, hd), lambda h, i: (h, i, 0)),
            pl.BlockSpec((1, TQ, 1), lambda h, i: (h, i, 0)),
            pl.BlockSpec((1, TQ, 1), lambda h, i: (h, i, 0)),
        ],
        out_shape=[
            jax.ShapeDtypeStruct((heads, nq, hd), f32),
            jax.ShapeDtypeStruct((heads, nq, 1), f32),
            jax.ShapeDtypeStruct((heads, nq, 1), f32),
        ],
    )(qT, kT, vT, cm)


def _backward(qT, kT, vT, gaT, lt, dl, cm, scale):
    heads, nq, hd = qT.shape
    nk = kT.shape[1]
    nb = TQ // BLOCK
    f32 = jnp.float32
    return pl.pallas_call(
        functools.partial(_bwd_kernel, scale=scale),
        grid=(heads, nq // TQ),
        in_specs=[
            pl.BlockSpec((1, TQ, hd), lambda h, i: (h, i, 0)),
            pl.BlockSpec((1, nk, hd), lambda h, i: (h, 0, 0)),
            pl.BlockSpec((1, nk, hd), lambda h, i: (h, 0, 0)),
            pl.BlockSpec((1, TQ, hd), lambda h, i: (h, i, 0)),
            pl.BlockSpec((1, TQ, 1), lambda h, i: (h, i, 0)),
            pl.BlockSpec((1, TQ, 1), lambda h, i: (h, i, 0)),
            pl.BlockSpec((nb, 1, nk), lambda h, i: (i, 0, 0)),
        ],
        out_specs=[
            pl.BlockSpec((1, TQ, hd), lambda h, i: (h, i, 0)),
            pl.BlockSpec((1, nk, hd), lambda h, i: (h, 0, 0)),
            pl.BlockSpec((1, nk, hd), lambda h, i: (h, 0, 0)),
        ],
        out_shape=[
            jax.ShapeDtypeStruct((heads, nq, hd), f32),
            jax.ShapeDtypeStruct((heads, nk, hd), f32),
            jax.ShapeDtypeStruct((heads, nk, hd), f32),
        ],
        compiler_params=pltpu.CompilerParams(dimension_semantics=("parallel", "arbitrary")),
    )(qT, kT, vT, gaT, lt, dl, cm)


def on_device(queries_in, hits_in, w_query, w_key, w_value, w_out, mask_list, grad_out):
    f32 = jnp.float32
    bf16 = jnp.bfloat16
    region_index = lax.axis_index("region")
    n_queries, width = queries_in.shape
    n_hits = hits_in.shape[0]
    head_dim = width // HEADS
    scale = 1.0 / math.sqrt(head_dim)
    hit_blocks = n_hits // BLOCK
    q_blocks = n_queries // BLOCK
    local_ids = region_index * hit_blocks + jnp.arange(hit_blocks, dtype=jnp.int32)
    blockmask = jnp.any(mask_list[:, :, None] == local_ids[None, None, :], axis=1)
    cm = jnp.repeat(blockmask.astype(f32), BLOCK, axis=1).reshape(q_blocks, 1, n_hits)

    def heads(x):
        return x.reshape(x.shape[0], HEADS, head_dim).transpose(1, 0, 2)

    def joined(x):
        return x.transpose(1, 0, 2).reshape(x.shape[1], width)

    query = jnp.dot(queries_in, w_query, preferred_element_type=f32).astype(bf16)
    keys = jnp.dot(hits_in, w_key, preferred_element_type=f32).astype(bf16)
    vals = jnp.dot(hits_in, w_value, preferred_element_type=f32).astype(bf16)
    qT, kT, vT = heads(query), heads(keys), heads(vals)

    regions = lax.axis_size("region")
    numer_r, max_r, total_r = _forward(qT, kT, vT, cm, scale)
    numer = joined(numer_r)
    peak = max_r.reshape(HEADS, n_queries)
    total = total_r.reshape(HEADS, n_queries)
    rows = n_queries
    base = 0
    steps = []
    k = 0
    while (1 << k) < regions:
        bit = (region_index >> k) & 1
        half = rows // 2
        pairs = [(i, i ^ (1 << k)) for i in range(regions)]
        mine = (
            lax.dynamic_slice_in_dim(numer, bit * half, half, 0),
            lax.dynamic_slice_in_dim(peak, bit * half, half, 1),
            lax.dynamic_slice_in_dim(total, bit * half, half, 1),
        )
        theirs = lax.ppermute(
            (
                lax.dynamic_slice_in_dim(numer, (1 - bit) * half, half, 0),
                lax.dynamic_slice_in_dim(peak, (1 - bit) * half, half, 1),
                lax.dynamic_slice_in_dim(total, (1 - bit) * half, half, 1),
            ),
            "region",
            pairs,
        )
        top = jnp.maximum(mine[1], theirs[1])
        scale_a = jnp.exp(mine[1] - top)
        scale_b = jnp.exp(theirs[1] - top)
        numer = mine[0] * jnp.repeat(scale_a.T, head_dim, axis=1) + theirs[0] * jnp.repeat(
            scale_b.T, head_dim, axis=1
        )
        total = mine[2] * scale_a + theirs[2] * scale_b
        peak = top
        base = base + bit * half
        steps.append((k, bit, half))
        rows = half
        k += 1
    attended_part = (numer / jnp.repeat(total.T, head_dim, axis=1)).astype(bf16)
    log_part = peak + jnp.log(total)
    grad_att = lax.dot_general(
        grad_out, w_out, (((1,), (1,)), ((), ())), preferred_element_type=f32
    ).astype(bf16)
    grad_att_part = lax.dynamic_slice_in_dim(grad_att, base, rows, 0)
    delta_part = jnp.sum(
        (grad_att_part.astype(f32) * attended_part.astype(f32)).reshape(rows, HEADS, head_dim),
        axis=2,
    ).T
    gathered = (attended_part, jnp.concatenate([log_part, delta_part], axis=0))
    for k, bit, half in reversed(steps):
        pairs = [(i, i ^ (1 << k)) for i in range(regions)]
        other = lax.ppermute(gathered, "region", pairs)
        lo = jax.tree.map(lambda a, b: jnp.where(bit == 0, a, b), gathered, other)
        hi = jax.tree.map(lambda a, b: jnp.where(bit == 0, b, a), gathered, other)
        gathered = (
            jnp.concatenate([lo[0], hi[0]], axis=0),
            jnp.concatenate([lo[1], hi[1]], axis=1),
        )
    attended = gathered[0]
    log_total = gathered[1][:HEADS].reshape(HEADS, n_queries, 1)
    deltas = gathered[1][HEADS:].reshape(HEADS, n_queries, 1)
    layer_out = (
        queries_in.astype(f32) + jnp.dot(attended, w_out, preferred_element_type=f32)
    ).astype(bf16)
    grad_wo = jnp.einsum("qa,qb->ab", attended, grad_out, preferred_element_type=f32)
    gaT = heads(grad_att)

    dq_r, dk, dv = _backward(qT, kT, vT, gaT, log_total, deltas, cm, scale)
    keys_grad = joined(dk).astype(bf16)
    vals_grad = joined(dv).astype(bf16)
    wk_part = jnp.einsum("ka,kb->ab", hits_in, keys_grad, preferred_element_type=f32)
    wv_part = jnp.einsum("ka,kb->ab", hits_in, vals_grad, preferred_element_type=f32)
    query_grad_sum, grad_wk, grad_wv = lax.psum(
        (joined(dq_r).astype(bf16), wk_part.astype(bf16), wv_part.astype(bf16)), "region"
    )
    grad_wk = grad_wk.astype(f32)
    grad_wv = grad_wv.astype(f32)
    grad_q = query_grad_sum
    grad_wq = jnp.einsum("qa,qb->ab", queries_in, grad_q, preferred_element_type=f32)
    grad_queries = (
        grad_out.astype(f32)
        + lax.dot_general(grad_q, w_query, (((1,), (1,)), ((), ())), preferred_element_type=f32)
    ).astype(bf16)
    grad_hits = (
        lax.dot_general(keys_grad, w_key, (((1,), (1,)), ((), ())), preferred_element_type=f32)
        + lax.dot_general(vals_grad, w_value, (((1,), (1,)), ((), ())), preferred_element_type=f32)
    ).astype(bf16)
    return (layer_out, grad_queries, grad_hits, grad_wq, grad_wk, grad_wv, grad_wo)


def solution(mesh):
    in_specs = (
        P("event", None),
        P(("event", "region"), None),
        P(),
        P(),
        P(),
        P(),
        P("event", None),
        P("event", None),
    )
    out_specs = (
        P("event", None),
        P("event", None),
        P(("event", "region"), None),
        P("event", None),
        P("event", None),
        P("event", None),
        P("event", None),
    )
    return jax.shard_map(
        on_device, mesh=mesh, in_specs=in_specs, out_specs=out_specs, check_vma=False
    )
```

```python
import functools
import math

import jax
import jax.numpy as jnp
from jax import lax
from jax.experimental import pallas as pl
from jax.experimental.pallas import tpu as pltpu
from jax.sharding import PartitionSpec as P

HEADS = 8
BLOCK = 128
TQ = 512


def _fwd_kernel(q_ref, k_ref, v_ref, cm_ref, numer_ref, m_ref, l_ref, *, scale):
    q = q_ref[0]
    k = k_ref[0]
    v = v_ref[0]
    s = lax.dot_general(q, k, (((1,), (1,)), ((), ())), preferred_element_type=jnp.float32) * scale
    tq, nk = s.shape
    nb = tq // BLOCK
    s3 = s.reshape(nb, BLOCK, nk)
    allowed = cm_ref[...] > 0.5
    masked = jnp.where(allowed, s3, -1e30)
    mx = jnp.max(masked, axis=2, keepdims=True)
    e = jnp.where(allowed, jnp.exp(masked - mx), 0.0)
    tot = jnp.sum(e, axis=2, keepdims=True)
    numer = jnp.dot(
        e.reshape(tq, nk).astype(jnp.bfloat16), v, preferred_element_type=jnp.float32
    )
    numer_ref[0] = numer
    m_ref[0] = mx.reshape(tq, 1)
    l_ref[0] = tot.reshape(tq, 1)


def _bwd_kernel(q_ref, k_ref, v_ref, ga_ref, lt_ref, dl_ref, cm_ref, dq_ref, dk_ref, dv_ref, *, scale):
    i = pl.program_id(1)

    @pl.when(i == 0)
    def _():
        dk_ref[...] = jnp.zeros_like(dk_ref)
        dv_ref[...] = jnp.zeros_like(dv_ref)

    q = q_ref[0]
    k = k_ref[0]
    v = v_ref[0]
    ga = ga_ref[0]
    s = lax.dot_general(q, k, (((1,), (1,)), ((), ())), preferred_element_type=jnp.float32) * scale
    tq, nk = s.shape
    nb = tq // BLOCK
    s3 = s.reshape(nb, BLOCK, nk)
    allowed = cm_ref[...] > 0.5
    lt = lt_ref[0].reshape(nb, BLOCK, 1)
    p = jnp.where(allowed, jnp.exp(s3 - lt), 0.0).reshape(tq, nk)
    dv_ref[0] += lax.dot_general(
        p.astype(jnp.bfloat16), ga, (((0,), (0,)), ((), ())), preferred_element_type=jnp.float32
    )
    dp = lax.dot_general(ga, v, (((1,), (1,)), ((), ())), preferred_element_type=jnp.float32)
    ds = (p * (dp - dl_ref[0]) * scale).astype(jnp.bfloat16)
    dq_ref[0] = jnp.dot(ds, k, preferred_element_type=jnp.float32)
    dk_ref[0] += lax.dot_general(
        ds, q, (((0,), (0,)), ((), ())), preferred_element_type=jnp.float32
    )


def _forward(qT, kT, vT, cm, scale):
    heads, nq, hd = qT.shape
    nk = kT.shape[1]
    nb = TQ // BLOCK
    f32 = jnp.float32
    return pl.pallas_call(
        functools.partial(_fwd_kernel, scale=scale),
        grid=(heads, nq // TQ),
        in_specs=[
            pl.BlockSpec((1, TQ, hd), lambda h, i: (h, i, 0)),
            pl.BlockSpec((1, nk, hd), lambda h, i: (h, 0, 0)),
            pl.BlockSpec((1, nk, hd), lambda h, i: (h, 0, 0)),
            pl.BlockSpec((nb, 1, nk), lambda h, i: (i, 0, 0)),
        ],
        out_specs=[
            pl.BlockSpec((1, TQ, hd), lambda h, i: (h, i, 0)),
            pl.BlockSpec((1, TQ, 1), lambda h, i: (h, i, 0)),
            pl.BlockSpec((1, TQ, 1), lambda h, i: (h, i, 0)),
        ],
        out_shape=[
            jax.ShapeDtypeStruct((heads, nq, hd), f32),
            jax.ShapeDtypeStruct((heads, nq, 1), f32),
            jax.ShapeDtypeStruct((heads, nq, 1), f32),
        ],
    )(qT, kT, vT, cm)


def _backward(qT, kT, vT, gaT, lt, dl, cm, scale):
    heads, nq, hd = qT.shape
    nk = kT.shape[1]
    nb = TQ // BLOCK
    f32 = jnp.float32
    return pl.pallas_call(
        functools.partial(_bwd_kernel, scale=scale),
        grid=(heads, nq // TQ),
        in_specs=[
            pl.BlockSpec((1, TQ, hd), lambda h, i: (h, i, 0)),
            pl.BlockSpec((1, nk, hd), lambda h, i: (h, 0, 0)),
            pl.BlockSpec((1, nk, hd), lambda h, i: (h, 0, 0)),
            pl.BlockSpec((1, TQ, hd), lambda h, i: (h, i, 0)),
            pl.BlockSpec((1, TQ, 1), lambda h, i: (h, i, 0)),
            pl.BlockSpec((1, TQ, 1), lambda h, i: (h, i, 0)),
            pl.BlockSpec((nb, 1, nk), lambda h, i: (i, 0, 0)),
        ],
        out_specs=[
            pl.BlockSpec((1, TQ, hd), lambda h, i: (h, i, 0)),
            pl.BlockSpec((1, nk, hd), lambda h, i: (h, 0, 0)),
            pl.BlockSpec((1, nk, hd), lambda h, i: (h, 0, 0)),
        ],
        out_shape=[
            jax.ShapeDtypeStruct((heads, nq, hd), f32),
            jax.ShapeDtypeStruct((heads, nk, hd), f32),
            jax.ShapeDtypeStruct((heads, nk, hd), f32),
        ],
        compiler_params=pltpu.CompilerParams(dimension_semantics=("parallel", "arbitrary")),
    )(qT, kT, vT, gaT, lt, dl, cm)


def on_device(queries_in, hits_in, w_query, w_key, w_value, w_out, mask_list, grad_out):
    f32 = jnp.float32
    bf16 = jnp.bfloat16
    region_index = lax.axis_index("region")
    n_queries, width = queries_in.shape
    n_hits = hits_in.shape[0]
    head_dim = width // HEADS
    scale = 1.0 / math.sqrt(head_dim)
    hit_blocks = n_hits // BLOCK
    q_blocks = n_queries // BLOCK
    local_ids = region_index * hit_blocks + jnp.arange(hit_blocks, dtype=jnp.int32)
    blockmask = jnp.any(mask_list[:, :, None] == local_ids[None, None, :], axis=1)
    cm = jnp.repeat(blockmask.astype(f32), BLOCK, axis=1).reshape(q_blocks, 1, n_hits)

    def heads(x):
        return x.reshape(x.shape[0], HEADS, head_dim).transpose(1, 0, 2)

    def joined(x):
        return x.transpose(1, 0, 2).reshape(x.shape[1], width)

    def project(x, w):
        return jnp.einsum(
            "nd,dhe->hne", x, w.reshape(width, HEADS, head_dim), preferred_element_type=f32
        ).astype(bf16)

    qT, kT, vT = project(queries_in, w_query), project(hits_in, w_key), project(hits_in, w_value)

    regions = lax.axis_size("region")
    numer_r, max_r, total_r = _forward(qT, kT, vT, cm, scale)
    numer = joined(numer_r)
    peak = max_r.reshape(HEADS, n_queries)
    total = total_r.reshape(HEADS, n_queries)
    rows = n_queries
    base = 0
    steps = []
    k = 0
    while (1 << k) < regions:
        bit = (region_index >> k) & 1
        half = rows // 2
        pairs = [(i, i ^ (1 << k)) for i in range(regions)]
        mine = (
            lax.dynamic_slice_in_dim(numer, bit * half, half, 0),
            lax.dynamic_slice_in_dim(peak, bit * half, half, 1),
            lax.dynamic_slice_in_dim(total, bit * half, half, 1),
        )
        theirs = lax.ppermute(
            (
                lax.dynamic_slice_in_dim(numer, (1 - bit) * half, half, 0),
                lax.dynamic_slice_in_dim(peak, (1 - bit) * half, half, 1),
                lax.dynamic_slice_in_dim(total, (1 - bit) * half, half, 1),
            ),
            "region",
            pairs,
        )
        top = jnp.maximum(mine[1], theirs[1])
        scale_a = jnp.exp(mine[1] - top)
        scale_b = jnp.exp(theirs[1] - top)
        numer = mine[0] * jnp.repeat(scale_a.T, head_dim, axis=1) + theirs[0] * jnp.repeat(
            scale_b.T, head_dim, axis=1
        )
        total = mine[2] * scale_a + theirs[2] * scale_b
        peak = top
        base = base + bit * half
        steps.append((k, bit, half))
        rows = half
        k += 1
    attended_part = (numer / jnp.repeat(total.T, head_dim, axis=1)).astype(bf16)
    log_part = peak + jnp.log(total)
    grad_att = lax.dot_general(
        grad_out, w_out, (((1,), (1,)), ((), ())), preferred_element_type=f32
    ).astype(bf16)
    grad_att_part = lax.dynamic_slice_in_dim(grad_att, base, rows, 0)
    delta_part = jnp.sum(
        (grad_att_part.astype(f32) * attended_part.astype(f32)).reshape(rows, HEADS, head_dim),
        axis=2,
    ).T
    gathered = (attended_part, jnp.concatenate([log_part, delta_part], axis=0))
    for k, bit, half in reversed(steps):
        pairs = [(i, i ^ (1 << k)) for i in range(regions)]
        other = lax.ppermute(gathered, "region", pairs)
        lo = jax.tree.map(lambda a, b: jnp.where(bit == 0, a, b), gathered, other)
        hi = jax.tree.map(lambda a, b: jnp.where(bit == 0, b, a), gathered, other)
        gathered = (
            jnp.concatenate([lo[0], hi[0]], axis=0),
            jnp.concatenate([lo[1], hi[1]], axis=1),
        )
    attended = gathered[0]
    log_total = gathered[1][:HEADS].reshape(HEADS, n_queries, 1)
    deltas = gathered[1][HEADS:].reshape(HEADS, n_queries, 1)
    layer_out = (
        queries_in.astype(f32) + jnp.dot(attended, w_out, preferred_element_type=f32)
    ).astype(bf16)
    grad_wo = jnp.einsum("qa,qb->ab", attended, grad_out, preferred_element_type=f32)
    gaT = jnp.einsum(
        "nd,hed->hne", grad_out, w_out.reshape(HEADS, head_dim, width), preferred_element_type=f32
    ).astype(bf16)

    dq_r, dk, dv = _backward(qT, kT, vT, gaT, log_total, deltas, cm, scale)
    keys_grad = dk.astype(bf16)
    vals_grad = dv.astype(bf16)
    wk_part = jnp.einsum("nd,hne->dhe", hits_in, keys_grad, preferred_element_type=f32).reshape(width, width)
    wv_part = jnp.einsum("nd,hne->dhe", hits_in, vals_grad, preferred_element_type=f32).reshape(width, width)
    query_grad_sum, grad_wk, grad_wv = lax.psum(
        (joined(dq_r).astype(bf16), wk_part.astype(bf16), wv_part.astype(bf16)), "region"
    )
    grad_wk = grad_wk.astype(f32)
    grad_wv = grad_wv.astype(f32)
    grad_q = query_grad_sum
    grad_wq = jnp.einsum("qa,qb->ab", queries_in, grad_q, preferred_element_type=f32)
    grad_queries = (
        grad_out.astype(f32)
        + lax.dot_general(grad_q, w_query, (((1,), (1,)), ((), ())), preferred_element_type=f32)
    ).astype(bf16)
    grad_hits = (
        jnp.einsum("hne,dhe->nd", keys_grad, w_key.reshape(width, HEADS, head_dim), preferred_element_type=f32)
        + jnp.einsum("hne,dhe->nd", vals_grad, w_value.reshape(width, HEADS, head_dim), preferred_element_type=f32)
    ).astype(bf16)
    return (layer_out, grad_queries, grad_hits, grad_wq, grad_wk, grad_wv, grad_wo)


def solution(mesh):
    in_specs = (
        P("event", None),
        P(("event", "region"), None),
        P(),
        P(),
        P(),
        P(),
        P("event", None),
        P("event", None),
    )
    out_specs = (
        P("event", None),
        P("event", None),
        P(("event", "region"), None),
        P("event", None),
        P("event", None),
        P("event", None),
        P("event", None),
    )
    return jax.shard_map(
        on_device, mesh=mesh, in_specs=in_specs, out_specs=out_specs, check_vma=False
    )
```

```python
import functools
import math

import jax
import jax.numpy as jnp
from jax import lax
from jax.experimental import pallas as pl
from jax.experimental.pallas import tpu as pltpu
from jax.sharding import PartitionSpec as P

HEADS = 8
BLOCK = 128
TQ = 512


def _fwd_kernel(q_ref, k_ref, v_ref, cm_ref, numer_ref, m_ref, l_ref, *, scale):
    q = q_ref[0]
    k = k_ref[0]
    v = v_ref[0]
    s = lax.dot_general(q, k, (((1,), (1,)), ((), ())), preferred_element_type=jnp.float32) * scale
    tq, nk = s.shape
    nb = tq // BLOCK
    s3 = s.reshape(nb, BLOCK, nk)
    allowed = cm_ref[...] > 0.5
    masked = jnp.where(allowed, s3, -1e30)
    mx = jnp.max(masked, axis=2, keepdims=True)
    e = jnp.where(allowed, jnp.exp(masked - mx), 0.0)
    tot = jnp.sum(e, axis=2, keepdims=True)
    numer = jnp.dot(
        e.reshape(tq, nk).astype(jnp.bfloat16), v, preferred_element_type=jnp.float32
    )
    numer_ref[0] = numer
    m_ref[0] = mx.reshape(tq, 1)
    l_ref[0] = tot.reshape(tq, 1)


def _bwd_kernel(q_ref, k_ref, v_ref, ga_ref, lt_ref, dl_ref, cm_ref, dq_ref, dk_ref, dv_ref, *, scale):
    i = pl.program_id(1)

    @pl.when(i == 0)
    def _():
        dk_ref[...] = jnp.zeros_like(dk_ref)
        dv_ref[...] = jnp.zeros_like(dv_ref)

    q = q_ref[0]
    k = k_ref[0]
    v = v_ref[0]
    ga = ga_ref[0]
    s = lax.dot_general(q, k, (((1,), (1,)), ((), ())), preferred_element_type=jnp.float32) * scale
    tq, nk = s.shape
    nb = tq // BLOCK
    s3 = s.reshape(nb, BLOCK, nk)
    allowed = cm_ref[...] > 0.5
    lt = lt_ref[0].reshape(nb, BLOCK, 1)
    p = jnp.where(allowed, jnp.exp(s3 - lt), 0.0).reshape(tq, nk)
    dv_ref[0] += lax.dot_general(
        p.astype(jnp.bfloat16), ga, (((0,), (0,)), ((), ())), preferred_element_type=jnp.float32
    )
    dp = lax.dot_general(ga, v, (((1,), (1,)), ((), ())), preferred_element_type=jnp.float32)
    ds = (p * (dp - dl_ref[0]) * scale).astype(jnp.bfloat16)
    dq_ref[0] = jnp.dot(ds, k, preferred_element_type=jnp.float32)
    dk_ref[0] += lax.dot_general(
        ds, q, (((0,), (0,)), ((), ())), preferred_element_type=jnp.float32
    )


def _forward(qT, kT, vT, cm, scale):
    heads, nq, hd = qT.shape
    nk = kT.shape[1]
    nb = TQ // BLOCK
    f32 = jnp.float32
    return pl.pallas_call(
        functools.partial(_fwd_kernel, scale=scale),
        grid=(heads, nq // TQ),
        in_specs=[
            pl.BlockSpec((1, TQ, hd), lambda h, i: (h, i, 0)),
            pl.BlockSpec((1, nk, hd), lambda h, i: (h, 0, 0)),
            pl.BlockSpec((1, nk, hd), lambda h, i: (h, 0, 0)),
            pl.BlockSpec((nb, 1, nk), lambda h, i: (i, 0, 0)),
        ],
        out_specs=[
            pl.BlockSpec((1, TQ, hd), lambda h, i: (h, i, 0)),
            pl.BlockSpec((1, TQ, 1), lambda h, i: (h, i, 0)),
            pl.BlockSpec((1, TQ, 1), lambda h, i: (h, i, 0)),
        ],
        out_shape=[
            jax.ShapeDtypeStruct((heads, nq, hd), f32),
            jax.ShapeDtypeStruct((heads, nq, 1), f32),
            jax.ShapeDtypeStruct((heads, nq, 1), f32),
        ],
    )(qT, kT, vT, cm)


def _backward(qT, kT, vT, gaT, lt, dl, cm, scale):
    heads, nq, hd = qT.shape
    nk = kT.shape[1]
    tile = min(nq, 2 * TQ)
    nb = tile // BLOCK
    f32 = jnp.float32
    return pl.pallas_call(
        functools.partial(_bwd_kernel, scale=scale),
        grid=(heads, nq // tile),
        in_specs=[
            pl.BlockSpec((1, tile, hd), lambda h, i: (h, i, 0)),
            pl.BlockSpec((1, nk, hd), lambda h, i: (h, 0, 0)),
            pl.BlockSpec((1, nk, hd), lambda h, i: (h, 0, 0)),
            pl.BlockSpec((1, tile, hd), lambda h, i: (h, i, 0)),
            pl.BlockSpec((1, tile, 1), lambda h, i: (h, i, 0)),
            pl.BlockSpec((1, tile, 1), lambda h, i: (h, i, 0)),
            pl.BlockSpec((nb, 1, nk), lambda h, i: (i, 0, 0)),
        ],
        out_specs=[
            pl.BlockSpec((1, tile, hd), lambda h, i: (h, i, 0)),
            pl.BlockSpec((1, nk, hd), lambda h, i: (h, 0, 0)),
            pl.BlockSpec((1, nk, hd), lambda h, i: (h, 0, 0)),
        ],
        out_shape=[
            jax.ShapeDtypeStruct((heads, nq, hd), f32),
            jax.ShapeDtypeStruct((heads, nk, hd), f32),
            jax.ShapeDtypeStruct((heads, nk, hd), f32),
        ],
        compiler_params=pltpu.CompilerParams(
            dimension_semantics=("parallel", "arbitrary"), vmem_limit_bytes=48 * 1024 * 1024
        ),
    )(qT, kT, vT, gaT, lt, dl, cm)


def on_device(queries_in, hits_in, w_query, w_key, w_value, w_out, mask_list, grad_out):
    f32 = jnp.float32
    bf16 = jnp.bfloat16
    region_index = lax.axis_index("region")
    n_queries, width = queries_in.shape
    n_hits = hits_in.shape[0]
    head_dim = width // HEADS
    scale = 1.0 / math.sqrt(head_dim)
    hit_blocks = n_hits // BLOCK
    q_blocks = n_queries // BLOCK
    local_ids = region_index * hit_blocks + jnp.arange(hit_blocks, dtype=jnp.int32)
    blockmask = jnp.any(mask_list[:, :, None] == local_ids[None, None, :], axis=1)
    cm = jnp.repeat(blockmask.astype(f32), BLOCK, axis=1).reshape(q_blocks, 1, n_hits)

    def heads(x):
        return x.reshape(x.shape[0], HEADS, head_dim).transpose(1, 0, 2)

    def joined(x):
        return x.transpose(1, 0, 2).reshape(x.shape[1], width)

    query = jnp.dot(queries_in, w_query, preferred_element_type=f32).astype(bf16)
    keys = jnp.dot(hits_in, w_key, preferred_element_type=f32).astype(bf16)
    vals = jnp.dot(hits_in, w_value, preferred_element_type=f32).astype(bf16)
    qT, kT, vT = heads(query), heads(keys), heads(vals)

    regions = lax.axis_size("region")
    numer_r, max_r, total_r = _forward(qT, kT, vT, cm, scale)
    numer = joined(numer_r)
    peak = max_r.reshape(HEADS, n_queries)
    total = total_r.reshape(HEADS, n_queries)
    rows = n_queries
    base = 0
    steps = []
    k = 0
    while (1 << k) < regions:
        bit = (region_index >> k) & 1
        half = rows // 2
        pairs = [(i, i ^ (1 << k)) for i in range(regions)]
        mine = (
            lax.dynamic_slice_in_dim(numer, bit * half, half, 0),
            lax.dynamic_slice_in_dim(peak, bit * half, half, 1),
            lax.dynamic_slice_in_dim(total, bit * half, half, 1),
        )
        theirs = lax.ppermute(
            (
                lax.dynamic_slice_in_dim(numer, (1 - bit) * half, half, 0).astype(bf16),
                lax.dynamic_slice_in_dim(peak, (1 - bit) * half, half, 1),
                lax.dynamic_slice_in_dim(total, (1 - bit) * half, half, 1),
            ),
            "region",
            pairs,
        )
        top = jnp.maximum(mine[1], theirs[1])
        scale_a = jnp.exp(mine[1] - top)
        scale_b = jnp.exp(theirs[1] - top)
        numer = mine[0] * jnp.repeat(scale_a.T, head_dim, axis=1) + theirs[0].astype(f32) * jnp.repeat(
            scale_b.T, head_dim, axis=1
        )
        total = mine[2] * scale_a + theirs[2] * scale_b
        peak = top
        base = base + bit * half
        steps.append((k, bit, half))
        rows = half
        k += 1
    attended_part = (numer / jnp.repeat(total.T, head_dim, axis=1)).astype(bf16)
    log_part = peak + jnp.log(total)
    grad_att = lax.dot_general(
        grad_out, w_out, (((1,), (1,)), ((), ())), preferred_element_type=f32
    ).astype(bf16)
    grad_att_part = lax.dynamic_slice_in_dim(grad_att, base, rows, 0)
    delta_part = jnp.sum(
        (grad_att_part.astype(f32) * attended_part.astype(f32)).reshape(rows, HEADS, head_dim),
        axis=2,
    ).T
    gathered = (attended_part, jnp.concatenate([log_part, delta_part], axis=0))
    for k, bit, half in reversed(steps):
        pairs = [(i, i ^ (1 << k)) for i in range(regions)]
        other = lax.ppermute(gathered, "region", pairs)
        lo = jax.tree.map(lambda a, b: jnp.where(bit == 0, a, b), gathered, other)
        hi = jax.tree.map(lambda a, b: jnp.where(bit == 0, b, a), gathered, other)
        gathered = (
            jnp.concatenate([lo[0], hi[0]], axis=0),
            jnp.concatenate([lo[1], hi[1]], axis=1),
        )
    attended = gathered[0]
    log_total = gathered[1][:HEADS].reshape(HEADS, n_queries, 1)
    deltas = gathered[1][HEADS:].reshape(HEADS, n_queries, 1)
    layer_out = (
        queries_in.astype(f32) + jnp.dot(attended, w_out, preferred_element_type=f32)
    ).astype(bf16)
    grad_wo = jnp.einsum("qa,qb->ab", attended, grad_out, preferred_element_type=f32)
    gaT = heads(grad_att)

    dq_r, dk, dv = _backward(qT, kT, vT, gaT, log_total, deltas, cm, scale)
    keys_grad = joined(dk).astype(bf16)
    vals_grad = joined(dv).astype(bf16)
    wk_part = jnp.einsum("ka,kb->ab", hits_in, keys_grad, preferred_element_type=f32)
    wv_part = jnp.einsum("ka,kb->ab", hits_in, vals_grad, preferred_element_type=f32)
    query_grad_sum, grad_wk, grad_wv = lax.psum(
        (joined(dq_r).astype(bf16), wk_part.astype(bf16), wv_part.astype(bf16)), "region"
    )
    grad_wk = grad_wk.astype(f32)
    grad_wv = grad_wv.astype(f32)
    grad_q = query_grad_sum
    grad_wq = jnp.einsum("qa,qb->ab", queries_in, grad_q, preferred_element_type=f32)
    grad_queries = (
        grad_out.astype(f32)
        + lax.dot_general(grad_q, w_query, (((1,), (1,)), ((), ())), preferred_element_type=f32)
    ).astype(bf16)
    grad_hits = (
        lax.dot_general(keys_grad, w_key, (((1,), (1,)), ((), ())), preferred_element_type=f32)
        + lax.dot_general(vals_grad, w_value, (((1,), (1,)), ((), ())), preferred_element_type=f32)
    ).astype(bf16)
    return (layer_out, grad_queries, grad_hits, grad_wq, grad_wk, grad_wv, grad_wo)


def solution(mesh):
    in_specs = (
        P("event", None),
        P(("event", "region"), None),
        P(),
        P(),
        P(),
        P(),
        P("event", None),
        P("event", None),
    )
    out_specs = (
        P("event", None),
        P("event", None),
        P(("event", "region"), None),
        P("event", None),
        P("event", None),
        P("event", None),
        P("event", None),
    )
    return jax.shard_map(
        on_device, mesh=mesh, in_specs=in_specs, out_specs=out_specs, check_vma=False
    )
```

```python
import functools
import math

import jax
import jax.numpy as jnp
from jax import lax
from jax.experimental import pallas as pl
from jax.experimental.pallas import tpu as pltpu
from jax.sharding import PartitionSpec as P

HEADS = 8
BLOCK = 128
TQ = 512


def _fwd_kernel(q_ref, k_ref, vt_ref, cm_ref, numer_ref, m_ref, l_ref, *, scale):
    q = q_ref[0]
    k = k_ref[0]
    vt = vt_ref[0]
    s = lax.dot_general(k, q, (((1,), (1,)), ((), ())), preferred_element_type=jnp.float32) * scale
    nk, tq = s.shape
    hb = nk // BLOCK
    s3 = s.reshape(hb, BLOCK, tq)
    allowed = cm_ref[...] > 0.5
    masked = jnp.where(allowed, s3, -1e30)
    mx = jnp.max(jnp.max(masked, axis=0), axis=0, keepdims=True)
    e = jnp.where(allowed, jnp.exp(masked - mx[None]), 0.0)
    tot = jnp.sum(jnp.sum(e, axis=0), axis=0, keepdims=True)
    numer_ref[0] = jnp.dot(
        vt, e.reshape(nk, tq).astype(jnp.bfloat16), preferred_element_type=jnp.float32
    )
    m_ref[0] = mx
    l_ref[0] = tot


def _bwd_kernel(q_ref, k_ref, v_ref, kt_ref, ga_ref, lt_ref, dl_ref, cm_ref, dq_ref, dk_ref, dv_ref, *, scale):
    i = pl.program_id(1)

    @pl.when(i == 0)
    def _():
        dk_ref[...] = jnp.zeros_like(dk_ref)
        dv_ref[...] = jnp.zeros_like(dv_ref)

    q = q_ref[0]
    k = k_ref[0]
    v = v_ref[0]
    ga = ga_ref[0]
    s = lax.dot_general(k, q, (((1,), (1,)), ((), ())), preferred_element_type=jnp.float32) * scale
    nk, tq = s.shape
    hb = nk // BLOCK
    s3 = s.reshape(hb, BLOCK, tq)
    allowed = cm_ref[...] > 0.5
    p = jnp.where(allowed, jnp.exp(s3 - lt_ref[...]), 0.0).reshape(nk, tq)
    dv_ref[0] += jnp.dot(p.astype(jnp.bfloat16), ga, preferred_element_type=jnp.float32)
    dp = lax.dot_general(v, ga, (((1,), (1,)), ((), ())), preferred_element_type=jnp.float32)
    ds = (p * (dp - dl_ref[0]) * scale).astype(jnp.bfloat16)
    dk_ref[0] += jnp.dot(ds, q, preferred_element_type=jnp.float32)
    dq_ref[0] = jnp.dot(kt_ref[0], ds, preferred_element_type=jnp.float32)


def _forward(qT, kT, vTT, cm, scale):
    heads, nq, hd = qT.shape
    nk = kT.shape[1]
    hb = nk // BLOCK
    f32 = jnp.float32
    return pl.pallas_call(
        functools.partial(_fwd_kernel, scale=scale),
        grid=(heads, nq // TQ),
        in_specs=[
            pl.BlockSpec((1, TQ, hd), lambda h, i: (h, i, 0)),
            pl.BlockSpec((1, nk, hd), lambda h, i: (h, 0, 0)),
            pl.BlockSpec((1, hd, nk), lambda h, i: (h, 0, 0)),
            pl.BlockSpec((hb, 1, TQ), lambda h, i: (0, 0, i)),
        ],
        out_specs=[
            pl.BlockSpec((1, hd, TQ), lambda h, i: (h, 0, i)),
            pl.BlockSpec((1, 1, TQ), lambda h, i: (h, 0, i)),
            pl.BlockSpec((1, 1, TQ), lambda h, i: (h, 0, i)),
        ],
        out_shape=[
            jax.ShapeDtypeStruct((heads, hd, nq), f32),
            jax.ShapeDtypeStruct((heads, 1, nq), f32),
            jax.ShapeDtypeStruct((heads, 1, nq), f32),
        ],
        compiler_params=pltpu.CompilerParams(vmem_limit_bytes=48 * 1024 * 1024),
    )(qT, kT, vTT, cm)


def _backward(qT, kT, vT, kTT, gaT, lt, dl, cm, scale):
    heads, nq, hd = qT.shape
    nk = kT.shape[1]
    hb = nk // BLOCK
    tile = min(nq, 2 * TQ)
    f32 = jnp.float32
    return pl.pallas_call(
        functools.partial(_bwd_kernel, scale=scale),
        grid=(heads, nq // tile),
        in_specs=[
            pl.BlockSpec((1, tile, hd), lambda h, i: (h, i, 0)),
            pl.BlockSpec((1, nk, hd), lambda h, i: (h, 0, 0)),
            pl.BlockSpec((1, nk, hd), lambda h, i: (h, 0, 0)),
            pl.BlockSpec((1, hd, nk), lambda h, i: (h, 0, 0)),
            pl.BlockSpec((1, tile, hd), lambda h, i: (h, i, 0)),
            pl.BlockSpec((1, 1, tile), lambda h, i: (h, 0, i)),
            pl.BlockSpec((1, 1, tile), lambda h, i: (h, 0, i)),
            pl.BlockSpec((hb, 1, tile), lambda h, i: (0, 0, i)),
        ],
        out_specs=[
            pl.BlockSpec((1, hd, tile), lambda h, i: (h, 0, i)),
            pl.BlockSpec((1, nk, hd), lambda h, i: (h, 0, 0)),
            pl.BlockSpec((1, nk, hd), lambda h, i: (h, 0, 0)),
        ],
        out_shape=[
            jax.ShapeDtypeStruct((heads, hd, nq), f32),
            jax.ShapeDtypeStruct((heads, nk, hd), f32),
            jax.ShapeDtypeStruct((heads, nk, hd), f32),
        ],
        compiler_params=pltpu.CompilerParams(
            dimension_semantics=("parallel", "arbitrary"), vmem_limit_bytes=48 * 1024 * 1024
        ),
    )(qT, kT, vT, kTT, gaT, lt, dl, cm)


def on_device(queries_in, hits_in, w_query, w_key, w_value, w_out, mask_list, grad_out):
    f32 = jnp.float32
    bf16 = jnp.bfloat16
    region_index = lax.axis_index("region")
    n_queries, width = queries_in.shape
    n_hits = hits_in.shape[0]
    head_dim = width // HEADS
    scale = 1.0 / math.sqrt(head_dim)
    hit_blocks = n_hits // BLOCK
    q_blocks = n_queries // BLOCK
    local_ids = region_index * hit_blocks + jnp.arange(hit_blocks, dtype=jnp.int32)
    blockmask = jnp.any(mask_list[:, :, None] == local_ids[None, None, :], axis=1)
    cm = jnp.repeat(blockmask.T.astype(f32), BLOCK, axis=1).reshape(hit_blocks, 1, n_queries)

    def heads(x):
        return x.reshape(x.shape[0], HEADS, head_dim).transpose(1, 0, 2)

    def joined(x):
        return x.transpose(1, 0, 2).reshape(x.shape[1], width)

    query = jnp.dot(queries_in, w_query, preferred_element_type=f32).astype(bf16)
    keys = jnp.dot(hits_in, w_key, preferred_element_type=f32).astype(bf16)
    vals = jnp.dot(hits_in, w_value, preferred_element_type=f32).astype(bf16)
    qT, kT, vT = heads(query), heads(keys), heads(vals)

    regions = lax.axis_size("region")
    numer_r, max_r, total_r = _forward(qT, kT, vT.transpose(0, 2, 1), cm, scale)
    numer = numer_r.transpose(2, 0, 1).reshape(n_queries, width)
    peak = max_r.reshape(HEADS, n_queries)
    total = total_r.reshape(HEADS, n_queries)
    rows = n_queries
    base = 0
    steps = []
    k = 0
    while (1 << k) < regions:
        bit = (region_index >> k) & 1
        half = rows // 2
        pairs = [(i, i ^ (1 << k)) for i in range(regions)]
        mine = (
            lax.dynamic_slice_in_dim(numer, bit * half, half, 0),
            lax.dynamic_slice_in_dim(peak, bit * half, half, 1),
            lax.dynamic_slice_in_dim(total, bit * half, half, 1),
        )
        theirs = lax.ppermute(
            (
                lax.dynamic_slice_in_dim(numer, (1 - bit) * half, half, 0).astype(bf16),
                lax.dynamic_slice_in_dim(peak, (1 - bit) * half, half, 1),
                lax.dynamic_slice_in_dim(total, (1 - bit) * half, half, 1),
            ),
            "region",
            pairs,
        )
        top = jnp.maximum(mine[1], theirs[1])
        scale_a = jnp.exp(mine[1] - top)
        scale_b = jnp.exp(theirs[1] - top)
        numer = mine[0] * jnp.repeat(scale_a.T, head_dim, axis=1) + theirs[0].astype(f32) * jnp.repeat(
            scale_b.T, head_dim, axis=1
        )
        total = mine[2] * scale_a + theirs[2] * scale_b
        peak = top
        base = base + bit * half
        steps.append((k, bit, half))
        rows = half
        k += 1
    attended_part = (numer / jnp.repeat(total.T, head_dim, axis=1)).astype(bf16)
    log_part = peak + jnp.log(total)
    grad_att = lax.dot_general(
        grad_out, w_out, (((1,), (1,)), ((), ())), preferred_element_type=f32
    ).astype(bf16)
    grad_att_part = lax.dynamic_slice_in_dim(grad_att, base, rows, 0)
    delta_part = jnp.sum(
        (grad_att_part.astype(f32) * attended_part.astype(f32)).reshape(rows, HEADS, head_dim),
        axis=2,
    ).T
    gathered = (attended_part, jnp.concatenate([log_part, delta_part], axis=0))
    for k, bit, half in reversed(steps):
        pairs = [(i, i ^ (1 << k)) for i in range(regions)]
        other = lax.ppermute(gathered, "region", pairs)
        lo = jax.tree.map(lambda a, b: jnp.where(bit == 0, a, b), gathered, other)
        hi = jax.tree.map(lambda a, b: jnp.where(bit == 0, b, a), gathered, other)
        gathered = (
            jnp.concatenate([lo[0], hi[0]], axis=0),
            jnp.concatenate([lo[1], hi[1]], axis=1),
        )
    attended = gathered[0]
    log_total = gathered[1][:HEADS].reshape(HEADS, 1, n_queries)
    deltas = gathered[1][HEADS:].reshape(HEADS, 1, n_queries)
    layer_out = (
        queries_in.astype(f32) + jnp.dot(attended, w_out, preferred_element_type=f32)
    ).astype(bf16)
    grad_wo = jnp.einsum("qa,qb->ab", attended, grad_out, preferred_element_type=f32)
    gaT = heads(grad_att)

    dq_r, dk, dv = _backward(qT, kT, vT, kT.transpose(0, 2, 1), gaT, log_total, deltas, cm, scale)
    keys_grad = joined(dk).astype(bf16)
    vals_grad = joined(dv).astype(bf16)
    wk_part = jnp.einsum("ka,kb->ab", hits_in, keys_grad, preferred_element_type=f32)
    wv_part = jnp.einsum("ka,kb->ab", hits_in, vals_grad, preferred_element_type=f32)
    query_grad_sum, grad_wk, grad_wv = lax.psum(
        (dq_r.transpose(2, 0, 1).reshape(n_queries, width).astype(bf16), wk_part.astype(bf16), wv_part.astype(bf16)), "region"
    )
    grad_wk = grad_wk.astype(f32)
    grad_wv = grad_wv.astype(f32)
    grad_q = query_grad_sum
    grad_wq = jnp.einsum("qa,qb->ab", queries_in, grad_q, preferred_element_type=f32)
    grad_queries = (
        grad_out.astype(f32)
        + lax.dot_general(grad_q, w_query, (((1,), (1,)), ((), ())), preferred_element_type=f32)
    ).astype(bf16)
    grad_hits = (
        lax.dot_general(keys_grad, w_key, (((1,), (1,)), ((), ())), preferred_element_type=f32)
        + lax.dot_general(vals_grad, w_value, (((1,), (1,)), ((), ())), preferred_element_type=f32)
    ).astype(bf16)
    return (layer_out, grad_queries, grad_hits, grad_wq, grad_wk, grad_wv, grad_wo)


def solution(mesh):
    in_specs = (
        P("event", None),
        P(("event", "region"), None),
        P(),
        P(),
        P(),
        P(),
        P("event", None),
        P("event", None),
    )
    out_specs = (
        P("event", None),
        P("event", None),
        P(("event", "region"), None),
        P("event", None),
        P("event", None),
        P("event", None),
        P("event", None),
    )
    return jax.shard_map(
        on_device, mesh=mesh, in_specs=in_specs, out_specs=out_specs, check_vma=False
    )
```

```python
import functools
import math

import jax
import jax.numpy as jnp
from jax import lax
from jax.experimental import pallas as pl
from jax.experimental.pallas import tpu as pltpu
from jax.sharding import PartitionSpec as P

HEADS = 8
BLOCK = 128
TQ = 512


def _fwd_kernel(q_ref, k_ref, vt_ref, cm_ref, numer_ref, m_ref, l_ref, *, scale):
    q = q_ref[0]
    k = k_ref[0]
    vt = vt_ref[0]
    s = lax.dot_general(k, q, (((1,), (1,)), ((), ())), preferred_element_type=jnp.float32) * scale
    nk, tq = s.shape
    hb = nk // BLOCK
    s3 = s.reshape(hb, BLOCK, tq)
    allowed = cm_ref[...] > 0.5
    masked = jnp.where(allowed, s3, -1e30)
    mx = jnp.max(jnp.max(masked, axis=0), axis=0, keepdims=True)
    e = jnp.where(allowed, jnp.exp(masked - mx[None]), 0.0)
    tot = jnp.sum(jnp.sum(e, axis=0), axis=0, keepdims=True)
    numer_ref[0] = jnp.dot(
        vt, e.reshape(nk, tq).astype(jnp.bfloat16), preferred_element_type=jnp.float32
    )
    m_ref[0] = mx
    l_ref[0] = tot


def _bwd_kernel(q_ref, k_ref, v_ref, kt_ref, ga_ref, lt_ref, dl_ref, cm_ref, dq_ref, dk_ref, dv_ref, *, scale):
    i = pl.program_id(1)

    @pl.when(i == 0)
    def _():
        dk_ref[...] = jnp.zeros_like(dk_ref)
        dv_ref[...] = jnp.zeros_like(dv_ref)

    q = q_ref[0]
    k = k_ref[0]
    v = v_ref[0]
    ga = ga_ref[0]
    s = lax.dot_general(k, q, (((1,), (1,)), ((), ())), preferred_element_type=jnp.float32) * scale
    nk, tq = s.shape
    hb = nk // BLOCK
    s3 = s.reshape(hb, BLOCK, tq)
    allowed = cm_ref[...] > 0.5
    p = jnp.where(allowed, jnp.exp(s3 - lt_ref[...]), 0.0).reshape(nk, tq)
    dv_ref[0] += jnp.dot(p.astype(jnp.bfloat16), ga, preferred_element_type=jnp.float32)
    dp = lax.dot_general(v, ga, (((1,), (1,)), ((), ())), preferred_element_type=jnp.float32)
    ds = (p * (dp - dl_ref[0]) * scale).astype(jnp.bfloat16)
    dk_ref[0] += jnp.dot(ds, q, preferred_element_type=jnp.float32)
    dq_ref[0] = jnp.dot(kt_ref[0], ds, preferred_element_type=jnp.float32)


def _forward(qT, kT, vTT, cm, scale):
    heads, nq, hd = qT.shape
    nk = kT.shape[1]
    hb = nk // BLOCK
    tile = min(nq, 2 * TQ)
    f32 = jnp.float32
    return pl.pallas_call(
        functools.partial(_fwd_kernel, scale=scale),
        grid=(heads, nq // tile),
        in_specs=[
            pl.BlockSpec((1, tile, hd), lambda h, i: (h, i, 0)),
            pl.BlockSpec((1, nk, hd), lambda h, i: (h, 0, 0)),
            pl.BlockSpec((1, hd, nk), lambda h, i: (h, 0, 0)),
            pl.BlockSpec((hb, 1, tile), lambda h, i: (0, 0, i)),
        ],
        out_specs=[
            pl.BlockSpec((1, hd, tile), lambda h, i: (h, 0, i)),
            pl.BlockSpec((1, 1, tile), lambda h, i: (h, 0, i)),
            pl.BlockSpec((1, 1, tile), lambda h, i: (h, 0, i)),
        ],
        out_shape=[
            jax.ShapeDtypeStruct((heads, hd, nq), f32),
            jax.ShapeDtypeStruct((heads, 1, nq), f32),
            jax.ShapeDtypeStruct((heads, 1, nq), f32),
        ],
        compiler_params=pltpu.CompilerParams(vmem_limit_bytes=48 * 1024 * 1024),
    )(qT, kT, vTT, cm)


def _backward(qT, kT, vT, kTT, gaT, lt, dl, cm, scale):
    heads, nq, hd = qT.shape
    nk = kT.shape[1]
    hb = nk // BLOCK
    tile = min(nq, 2 * TQ)
    f32 = jnp.float32
    return pl.pallas_call(
        functools.partial(_bwd_kernel, scale=scale),
        grid=(heads, nq // tile),
        in_specs=[
            pl.BlockSpec((1, tile, hd), lambda h, i: (h, i, 0)),
            pl.BlockSpec((1, nk, hd), lambda h, i: (h, 0, 0)),
            pl.BlockSpec((1, nk, hd), lambda h, i: (h, 0, 0)),
            pl.BlockSpec((1, hd, nk), lambda h, i: (h, 0, 0)),
            pl.BlockSpec((1, tile, hd), lambda h, i: (h, i, 0)),
            pl.BlockSpec((1, 1, tile), lambda h, i: (h, 0, i)),
            pl.BlockSpec((1, 1, tile), lambda h, i: (h, 0, i)),
            pl.BlockSpec((hb, 1, tile), lambda h, i: (0, 0, i)),
        ],
        out_specs=[
            pl.BlockSpec((1, hd, tile), lambda h, i: (h, 0, i)),
            pl.BlockSpec((1, nk, hd), lambda h, i: (h, 0, 0)),
            pl.BlockSpec((1, nk, hd), lambda h, i: (h, 0, 0)),
        ],
        out_shape=[
            jax.ShapeDtypeStruct((heads, hd, nq), f32),
            jax.ShapeDtypeStruct((heads, nk, hd), f32),
            jax.ShapeDtypeStruct((heads, nk, hd), f32),
        ],
        compiler_params=pltpu.CompilerParams(
            dimension_semantics=("parallel", "arbitrary"), vmem_limit_bytes=48 * 1024 * 1024
        ),
    )(qT, kT, vT, kTT, gaT, lt, dl, cm)


def on_device(queries_in, hits_in, w_query, w_key, w_value, w_out, mask_list, grad_out):
    f32 = jnp.float32
    bf16 = jnp.bfloat16
    region_index = lax.axis_index("region")
    n_queries, width = queries_in.shape
    n_hits = hits_in.shape[0]
    head_dim = width // HEADS
    scale = 1.0 / math.sqrt(head_dim)
    hit_blocks = n_hits // BLOCK
    q_blocks = n_queries // BLOCK
    local_ids = region_index * hit_blocks + jnp.arange(hit_blocks, dtype=jnp.int32)
    blockmask = jnp.any(mask_list[:, :, None] == local_ids[None, None, :], axis=1)
    cm = jnp.repeat(blockmask.T.astype(f32), BLOCK, axis=1).reshape(hit_blocks, 1, n_queries)

    def heads(x):
        return x.reshape(x.shape[0], HEADS, head_dim).transpose(1, 0, 2)

    def joined(x):
        return x.transpose(1, 0, 2).reshape(x.shape[1], width)

    query = jnp.dot(queries_in, w_query, preferred_element_type=f32).astype(bf16)
    keys = jnp.dot(hits_in, w_key, preferred_element_type=f32).astype(bf16)
    vals = jnp.dot(hits_in, w_value, preferred_element_type=f32).astype(bf16)
    qT, kT, vT = heads(query), heads(keys), heads(vals)

    regions = lax.axis_size("region")
    numer_r, max_r, total_r = _forward(qT, kT, vT.transpose(0, 2, 1), cm, scale)
    numer = numer_r.transpose(2, 0, 1).reshape(n_queries, width)
    peak = max_r.reshape(HEADS, n_queries)
    total = total_r.reshape(HEADS, n_queries)
    rows = n_queries
    base = 0
    steps = []
    k = 0
    while (1 << k) < regions:
        bit = (region_index >> k) & 1
        half = rows // 2
        pairs = [(i, i ^ (1 << k)) for i in range(regions)]
        mine = (
            lax.dynamic_slice_in_dim(numer, bit * half, half, 0),
            lax.dynamic_slice_in_dim(peak, bit * half, half, 1),
            lax.dynamic_slice_in_dim(total, bit * half, half, 1),
        )
        theirs = lax.ppermute(
            (
                lax.dynamic_slice_in_dim(numer, (1 - bit) * half, half, 0).astype(bf16),
                lax.dynamic_slice_in_dim(peak, (1 - bit) * half, half, 1),
                lax.dynamic_slice_in_dim(total, (1 - bit) * half, half, 1),
            ),
            "region",
            pairs,
        )
        top = jnp.maximum(mine[1], theirs[1])
        scale_a = jnp.exp(mine[1] - top)
        scale_b = jnp.exp(theirs[1] - top)
        numer = mine[0] * jnp.repeat(scale_a.T, head_dim, axis=1) + theirs[0].astype(f32) * jnp.repeat(
            scale_b.T, head_dim, axis=1
        )
        total = mine[2] * scale_a + theirs[2] * scale_b
        peak = top
        base = base + bit * half
        steps.append((k, bit, half))
        rows = half
        k += 1
    attended_part = (numer / jnp.repeat(total.T, head_dim, axis=1)).astype(bf16)
    log_part = peak + jnp.log(total)
    grad_att = lax.dot_general(
        grad_out, w_out, (((1,), (1,)), ((), ())), preferred_element_type=f32
    ).astype(bf16)
    grad_att_part = lax.dynamic_slice_in_dim(grad_att, base, rows, 0)
    delta_part = jnp.sum(
        (grad_att_part.astype(f32) * attended_part.astype(f32)).reshape(rows, HEADS, head_dim),
        axis=2,
    ).T
    gathered = (attended_part, jnp.concatenate([log_part, delta_part], axis=0))
    for k, bit, half in reversed(steps):
        pairs = [(i, i ^ (1 << k)) for i in range(regions)]
        other = lax.ppermute(gathered, "region", pairs)
        lo = jax.tree.map(lambda a, b: jnp.where(bit == 0, a, b), gathered, other)
        hi = jax.tree.map(lambda a, b: jnp.where(bit == 0, b, a), gathered, other)
        gathered = (
            jnp.concatenate([lo[0], hi[0]], axis=0),
            jnp.concatenate([lo[1], hi[1]], axis=1),
        )
    attended = gathered[0]
    log_total = gathered[1][:HEADS].reshape(HEADS, 1, n_queries)
    deltas = gathered[1][HEADS:].reshape(HEADS, 1, n_queries)
    attended, log_total, deltas = lax.optimization_barrier((attended, log_total, deltas))
    layer_out = (
        queries_in.astype(f32) + jnp.dot(attended, w_out, preferred_element_type=f32)
    ).astype(bf16)
    grad_wo = jnp.einsum("qa,qb->ab", attended, grad_out, preferred_element_type=f32)
    gaT = heads(grad_att)

    dq_r, dk, dv = _backward(qT, kT, vT, kT.transpose(0, 2, 1), gaT, log_total, deltas, cm, scale)
    keys_grad = joined(dk).astype(bf16)
    vals_grad = joined(dv).astype(bf16)
    wk_part = jnp.einsum("ka,kb->ab", hits_in, keys_grad, preferred_element_type=f32)
    wv_part = jnp.einsum("ka,kb->ab", hits_in, vals_grad, preferred_element_type=f32)
    query_grad_sum, grad_wk, grad_wv = lax.psum(
        (dq_r.transpose(2, 0, 1).reshape(n_queries, width).astype(bf16), wk_part.astype(bf16), wv_part.astype(bf16)), "region"
    )
    grad_wk = grad_wk.astype(f32)
    grad_wv = grad_wv.astype(f32)
    grad_q = query_grad_sum
    grad_wq = jnp.einsum("qa,qb->ab", queries_in, grad_q, preferred_element_type=f32)
    grad_queries = (
        grad_out.astype(f32)
        + lax.dot_general(grad_q, w_query, (((1,), (1,)), ((), ())), preferred_element_type=f32)
    ).astype(bf16)
    grad_hits = (
        lax.dot_general(keys_grad, w_key, (((1,), (1,)), ((), ())), preferred_element_type=f32)
        + lax.dot_general(vals_grad, w_value, (((1,), (1,)), ((), ())), preferred_element_type=f32)
    ).astype(bf16)
    return (layer_out, grad_queries, grad_hits, grad_wq, grad_wk, grad_wv, grad_wo)


def solution(mesh):
    in_specs = (
        P("event", None),
        P(("event", "region"), None),
        P(),
        P(),
        P(),
        P(),
        P("event", None),
        P("event", None),
    )
    out_specs = (
        P("event", None),
        P("event", None),
        P(("event", "region"), None),
        P("event", None),
        P("event", None),
        P("event", None),
        P("event", None),
    )
    return jax.shard_map(
        on_device, mesh=mesh, in_specs=in_specs, out_specs=out_specs, check_vma=False
    )
```

```python
import functools
import math

import jax
import jax.numpy as jnp
from jax import lax
from jax.experimental import pallas as pl
from jax.experimental.pallas import tpu as pltpu
from jax.sharding import PartitionSpec as P

HEADS = 8
BLOCK = 128
TQ = 512


def _fwd_kernel(q_ref, k_ref, vt_ref, cm_ref, numer_ref, m_ref, l_ref, *, scale):
    q = q_ref[0]
    k = k_ref[0]
    vt = vt_ref[0]
    s = lax.dot_general(k, q, (((1,), (1,)), ((), ())), preferred_element_type=jnp.float32) * scale
    nk, tq = s.shape
    hb = nk // BLOCK
    s3 = s.reshape(hb, BLOCK, tq)
    allowed = cm_ref[...] > 0.5
    masked = jnp.where(allowed, s3, -1e30)
    mx = jnp.max(jnp.max(masked, axis=0), axis=0, keepdims=True)
    e = jnp.where(allowed, jnp.exp(masked - mx[None]), 0.0)
    tot = jnp.sum(jnp.sum(e, axis=0), axis=0, keepdims=True)
    numer_ref[0] = jnp.dot(
        vt, e.reshape(nk, tq).astype(jnp.bfloat16), preferred_element_type=jnp.float32
    )
    m_ref[0] = mx
    l_ref[0] = tot


def _bwd_kernel(q_ref, k_ref, v_ref, kt_ref, ga_ref, lt_ref, dl_ref, cm_ref, dq_ref, dk_ref, dv_ref, *, scale):
    i = pl.program_id(1)

    @pl.when(i == 0)
    def _():
        dk_ref[...] = jnp.zeros_like(dk_ref)
        dv_ref[...] = jnp.zeros_like(dv_ref)

    q = q_ref[0]
    k = k_ref[0]
    v = v_ref[0]
    ga = ga_ref[0]
    s = lax.dot_general(k, q, (((1,), (1,)), ((), ())), preferred_element_type=jnp.float32) * scale
    nk, tq = s.shape
    hb = nk // BLOCK
    s3 = s.reshape(hb, BLOCK, tq)
    allowed = cm_ref[...] > 0.5
    p = jnp.where(allowed, jnp.exp(s3 - lt_ref[...]), 0.0).reshape(nk, tq)
    dv_ref[0] += jnp.dot(p.astype(jnp.bfloat16), ga, preferred_element_type=jnp.float32)
    dp = lax.dot_general(v, ga, (((1,), (1,)), ((), ())), preferred_element_type=jnp.float32)
    ds = (p * (dp - dl_ref[0]) * scale).astype(jnp.bfloat16)
    dk_ref[0] += jnp.dot(ds, q, preferred_element_type=jnp.float32)
    dq_ref[0] = jnp.dot(kt_ref[0], ds, preferred_element_type=jnp.float32)


def _forward(qT, kT, vTT, cm, scale):
    heads, nq, hd = qT.shape
    nk = kT.shape[1]
    hb = nk // BLOCK
    tile = min(nq, 2 * TQ)
    f32 = jnp.float32
    return pl.pallas_call(
        functools.partial(_fwd_kernel, scale=scale),
        grid=(heads, nq // tile),
        in_specs=[
            pl.BlockSpec((1, tile, hd), lambda h, i: (h, i, 0)),
            pl.BlockSpec((1, nk, hd), lambda h, i: (h, 0, 0)),
            pl.BlockSpec((1, hd, nk), lambda h, i: (h, 0, 0)),
            pl.BlockSpec((hb, 1, tile), lambda h, i: (0, 0, i)),
        ],
        out_specs=[
            pl.BlockSpec((1, hd, tile), lambda h, i: (h, 0, i)),
            pl.BlockSpec((1, 1, tile), lambda h, i: (h, 0, i)),
            pl.BlockSpec((1, 1, tile), lambda h, i: (h, 0, i)),
        ],
        out_shape=[
            jax.ShapeDtypeStruct((heads, hd, nq), f32),
            jax.ShapeDtypeStruct((heads, 1, nq), f32),
            jax.ShapeDtypeStruct((heads, 1, nq), f32),
        ],
        compiler_params=pltpu.CompilerParams(vmem_limit_bytes=48 * 1024 * 1024),
    )(qT, kT, vTT, cm)


def _backward(qT, kT, vT, kTT, gaT, lt, dl, cm, scale):
    heads, nq, hd = qT.shape
    nk = kT.shape[1]
    hb = nk // BLOCK
    tile = min(nq, 2 * TQ)
    f32 = jnp.float32
    return pl.pallas_call(
        functools.partial(_bwd_kernel, scale=scale),
        grid=(heads, nq // tile),
        in_specs=[
            pl.BlockSpec((1, tile, hd), lambda h, i: (h, i, 0)),
            pl.BlockSpec((1, nk, hd), lambda h, i: (h, 0, 0)),
            pl.BlockSpec((1, nk, hd), lambda h, i: (h, 0, 0)),
            pl.BlockSpec((1, hd, nk), lambda h, i: (h, 0, 0)),
            pl.BlockSpec((1, tile, hd), lambda h, i: (h, i, 0)),
            pl.BlockSpec((1, 1, tile), lambda h, i: (h, 0, i)),
            pl.BlockSpec((1, 1, tile), lambda h, i: (h, 0, i)),
            pl.BlockSpec((hb, 1, tile), lambda h, i: (0, 0, i)),
        ],
        out_specs=[
            pl.BlockSpec((1, hd, tile), lambda h, i: (h, 0, i)),
            pl.BlockSpec((1, nk, hd), lambda h, i: (h, 0, 0)),
            pl.BlockSpec((1, nk, hd), lambda h, i: (h, 0, 0)),
        ],
        out_shape=[
            jax.ShapeDtypeStruct((heads, hd, nq), f32),
            jax.ShapeDtypeStruct((heads, nk, hd), f32),
            jax.ShapeDtypeStruct((heads, nk, hd), f32),
        ],
        compiler_params=pltpu.CompilerParams(
            dimension_semantics=("parallel", "arbitrary"), vmem_limit_bytes=48 * 1024 * 1024
        ),
    )(qT, kT, vT, kTT, gaT, lt, dl, cm)


def on_device(queries_in, hits_in, w_query, w_key, w_value, w_out, mask_list, grad_out):
    f32 = jnp.float32
    bf16 = jnp.bfloat16
    region_index = lax.axis_index("region")
    n_queries, width = queries_in.shape
    n_hits = hits_in.shape[0]
    head_dim = width // HEADS
    scale = 1.0 / math.sqrt(head_dim)
    hit_blocks = n_hits // BLOCK
    q_blocks = n_queries // BLOCK
    local_ids = region_index * hit_blocks + jnp.arange(hit_blocks, dtype=jnp.int32)
    blockmask = jnp.any(mask_list[:, :, None] == local_ids[None, None, :], axis=1)
    cm = jnp.repeat(blockmask.T.astype(f32), BLOCK, axis=1).reshape(hit_blocks, 1, n_queries)

    def heads(x):
        return x.reshape(x.shape[0], HEADS, head_dim).transpose(1, 0, 2)

    def joined(x):
        return x.transpose(1, 0, 2).reshape(x.shape[1], width)

    query = jnp.dot(queries_in, w_query, preferred_element_type=f32).astype(bf16)
    keys = jnp.dot(hits_in, w_key, preferred_element_type=f32).astype(bf16)
    vals = jnp.dot(hits_in, w_value, preferred_element_type=f32).astype(bf16)
    qT, kT, vT = heads(query), heads(keys), heads(vals)

    regions = lax.axis_size("region")
    numer_r, max_r, total_r = _forward(qT, kT, vT.transpose(0, 2, 1), cm, scale)
    numer = numer_r.transpose(2, 0, 1).reshape(n_queries, width)
    peak = max_r.reshape(HEADS, n_queries)
    total = total_r.reshape(HEADS, n_queries)
    rows = n_queries
    base = 0
    steps = []
    k = 0
    while (1 << k) < regions:
        bit = (region_index >> k) & 1
        half = rows // 2
        pairs = [(i, i ^ (1 << k)) for i in range(regions)]
        mine = (
            lax.dynamic_slice_in_dim(numer, bit * half, half, 0),
            lax.dynamic_slice_in_dim(peak, bit * half, half, 1),
            lax.dynamic_slice_in_dim(total, bit * half, half, 1),
        )
        theirs = lax.ppermute(
            (
                lax.dynamic_slice_in_dim(numer, (1 - bit) * half, half, 0).astype(bf16),
                lax.dynamic_slice_in_dim(peak, (1 - bit) * half, half, 1),
                lax.dynamic_slice_in_dim(total, (1 - bit) * half, half, 1),
            ),
            "region",
            pairs,
        )
        top = jnp.maximum(mine[1], theirs[1])
        scale_a = jnp.exp(mine[1] - top)
        scale_b = jnp.exp(theirs[1] - top)
        numer = mine[0] * jnp.repeat(scale_a.T, head_dim, axis=1) + theirs[0].astype(f32) * jnp.repeat(
            scale_b.T, head_dim, axis=1
        )
        total = mine[2] * scale_a + theirs[2] * scale_b
        peak = top
        base = base + bit * half
        steps.append((k, bit, half))
        rows = half
        k += 1
    attended_part = (numer / jnp.repeat(total.T, head_dim, axis=1)).astype(bf16)
    log_part = peak + jnp.log(total)
    grad_att = lax.dot_general(
        grad_out, w_out, (((1,), (1,)), ((), ())), preferred_element_type=f32
    ).astype(bf16)
    grad_att_part = lax.dynamic_slice_in_dim(grad_att, base, rows, 0)
    delta_part = jnp.sum(
        (grad_att_part.astype(f32) * attended_part.astype(f32)).reshape(rows, HEADS, head_dim),
        axis=2,
    ).T
    gathered = (attended_part, jnp.concatenate([log_part, delta_part], axis=0))
    for k, bit, half in reversed(steps):
        pairs = [(i, i ^ (1 << k)) for i in range(regions)]
        other = lax.ppermute(gathered, "region", pairs)
        lo = jax.tree.map(lambda a, b: jnp.where(bit == 0, a, b), gathered, other)
        hi = jax.tree.map(lambda a, b: jnp.where(bit == 0, b, a), gathered, other)
        gathered = (
            jnp.concatenate([lo[0], hi[0]], axis=0),
            jnp.concatenate([lo[1], hi[1]], axis=1),
        )
    attended = gathered[0]
    log_total = gathered[1][:HEADS].reshape(HEADS, 1, n_queries)
    deltas = gathered[1][HEADS:].reshape(HEADS, 1, n_queries)
    layer_out = (
        queries_in.astype(f32) + jnp.dot(attended, w_out, preferred_element_type=f32)
    ).astype(bf16)
    grad_wo = jnp.einsum("qa,qb->ab", attended, grad_out, preferred_element_type=f32)
    gaT = heads(grad_att)

    dq_r, dk, dv = _backward(qT, kT, vT, kT.transpose(0, 2, 1), gaT, log_total, deltas, cm, scale)
    keys_grad = joined(dk).astype(bf16)
    vals_grad = joined(dv).astype(bf16)
    wk_part = jnp.einsum("ka,kb->ab", hits_in, keys_grad, preferred_element_type=f32)
    wv_part = jnp.einsum("ka,kb->ab", hits_in, vals_grad, preferred_element_type=f32)
    query_grad_sum, grad_wk, grad_wv = lax.psum(
        (dq_r.transpose(2, 0, 1).reshape(n_queries, width).astype(bf16), wk_part.astype(bf16), wv_part.astype(bf16)), "region"
    )
    grad_wk = grad_wk.astype(f32)
    grad_wv = grad_wv.astype(f32)
    grad_q = query_grad_sum
    grad_wq = jnp.einsum("qa,qb->ab", queries_in, grad_q, preferred_element_type=f32)
    grad_queries = (
        grad_out.astype(f32)
        + lax.dot_general(grad_q, w_query, (((1,), (1,)), ((), ())), preferred_element_type=f32)
    ).astype(bf16)
    grad_hits = (
        lax.dot_general(keys_grad, w_key, (((1,), (1,)), ((), ())), preferred_element_type=f32)
        + lax.dot_general(vals_grad, w_value, (((1,), (1,)), ((), ())), preferred_element_type=f32)
    ).astype(bf16)
    return (layer_out, grad_queries, grad_hits, grad_wq, grad_wk, grad_wv, grad_wo)


def solution(mesh):
    in_specs = (
        P("event", None),
        P(("event", "region"), None),
        P(),
        P(),
        P(),
        P(),
        P("event", None),
        P("event", None),
    )
    out_specs = (
        P("event", None),
        P("event", None),
        P(("event", "region"), None),
        P("event", None),
        P("event", None),
        P("event", None),
        P("event", None),
    )
    return jax.shard_map(
        on_device, mesh=mesh, in_specs=in_specs, out_specs=out_specs, check_vma=False
    )
```

```python
import functools
import math

import jax
import jax.numpy as jnp
from jax import lax
from jax.experimental import pallas as pl
from jax.experimental.pallas import tpu as pltpu
from jax.sharding import PartitionSpec as P

HEADS = 8
BLOCK = 128
TQ = 512


def _fwd_kernel(q_ref, k_ref, vt_ref, cm_ref, numer_ref, m_ref, l_ref, *, scale):
    q = q_ref[0]
    k = k_ref[0]
    vt = vt_ref[0]
    s = lax.dot_general(k, q, (((1,), (1,)), ((), ())), preferred_element_type=jnp.float32) * scale
    nk, tq = s.shape
    hb = nk // BLOCK
    s3 = s.reshape(hb, BLOCK, tq)
    allowed = cm_ref[...] > 0.5
    masked = jnp.where(allowed, s3, -1e30)
    mx = jnp.max(jnp.max(masked, axis=0), axis=0, keepdims=True)
    e = jnp.where(allowed, jnp.exp(masked - mx[None]), 0.0)
    tot = jnp.sum(jnp.sum(e, axis=0), axis=0, keepdims=True)
    numer_ref[0] = jnp.dot(
        vt, e.reshape(nk, tq).astype(jnp.bfloat16), preferred_element_type=jnp.float32
    )
    m_ref[0] = mx
    l_ref[0] = tot


def _bwd_kernel(q_ref, k_ref, v_ref, kt_ref, ga_ref, lt_ref, dl_ref, cm_ref, dq_ref, dk_ref, dv_ref, *, scale):
    i = pl.program_id(1)

    @pl.when(i == 0)
    def _():
        dk_ref[...] = jnp.zeros_like(dk_ref)
        dv_ref[...] = jnp.zeros_like(dv_ref)

    q = q_ref[0]
    k = k_ref[0]
    v = v_ref[0]
    ga = ga_ref[0]
    s = lax.dot_general(k, q, (((1,), (1,)), ((), ())), preferred_element_type=jnp.float32) * scale
    nk, tq = s.shape
    hb = nk // BLOCK
    s3 = s.reshape(hb, BLOCK, tq)
    allowed = cm_ref[...] > 0.5
    p = jnp.where(allowed, jnp.exp(s3 - lt_ref[...]), 0.0).reshape(nk, tq)
    dv_ref[0] += jnp.dot(p.astype(jnp.bfloat16), ga, preferred_element_type=jnp.float32)
    dp = lax.dot_general(v, ga, (((1,), (1,)), ((), ())), preferred_element_type=jnp.float32)
    ds = (p * (dp - dl_ref[0]) * scale).astype(jnp.bfloat16)
    dk_ref[0] += jnp.dot(ds, q, preferred_element_type=jnp.float32)
    dq_ref[0] = jnp.dot(kt_ref[0], ds, preferred_element_type=jnp.float32)


def _forward(qT, kT, vTT, cm, scale):
    heads, nq, hd = qT.shape
    nk = kT.shape[1]
    hb = nk // BLOCK
    tile = min(nq, 2 * TQ)
    f32 = jnp.float32
    return pl.pallas_call(
        functools.partial(_fwd_kernel, scale=scale),
        grid=(heads, nq // tile),
        in_specs=[
            pl.BlockSpec((1, tile, hd), lambda h, i: (h, i, 0)),
            pl.BlockSpec((1, nk, hd), lambda h, i: (h, 0, 0)),
            pl.BlockSpec((1, hd, nk), lambda h, i: (h, 0, 0)),
            pl.BlockSpec((hb, 1, tile), lambda h, i: (0, 0, i)),
        ],
        out_specs=[
            pl.BlockSpec((1, hd, tile), lambda h, i: (h, 0, i)),
            pl.BlockSpec((1, 1, tile), lambda h, i: (h, 0, i)),
            pl.BlockSpec((1, 1, tile), lambda h, i: (h, 0, i)),
        ],
        out_shape=[
            jax.ShapeDtypeStruct((heads, hd, nq), f32),
            jax.ShapeDtypeStruct((heads, 1, nq), f32),
            jax.ShapeDtypeStruct((heads, 1, nq), f32),
        ],
        compiler_params=pltpu.CompilerParams(vmem_limit_bytes=48 * 1024 * 1024),
    )(qT, kT, vTT, cm)


def _backward(qT, kT, vT, kTT, gaT, lt, dl, cm, scale):
    heads, nq, hd = qT.shape
    nk = kT.shape[1]
    hb = nk // BLOCK
    tile = min(nq, 2 * TQ)
    f32 = jnp.float32
    return pl.pallas_call(
        functools.partial(_bwd_kernel, scale=scale),
        grid=(heads, nq // tile),
        in_specs=[
            pl.BlockSpec((1, tile, hd), lambda h, i: (h, i, 0)),
            pl.BlockSpec((1, nk, hd), lambda h, i: (h, 0, 0)),
            pl.BlockSpec((1, nk, hd), lambda h, i: (h, 0, 0)),
            pl.BlockSpec((1, hd, nk), lambda h, i: (h, 0, 0)),
            pl.BlockSpec((1, tile, hd), lambda h, i: (h, i, 0)),
            pl.BlockSpec((1, 1, tile), lambda h, i: (h, 0, i)),
            pl.BlockSpec((1, 1, tile), lambda h, i: (h, 0, i)),
            pl.BlockSpec((hb, 1, tile), lambda h, i: (0, 0, i)),
        ],
        out_specs=[
            pl.BlockSpec((1, hd, tile), lambda h, i: (h, 0, i)),
            pl.BlockSpec((1, nk, hd), lambda h, i: (h, 0, 0)),
            pl.BlockSpec((1, nk, hd), lambda h, i: (h, 0, 0)),
        ],
        out_shape=[
            jax.ShapeDtypeStruct((heads, hd, nq), f32),
            jax.ShapeDtypeStruct((heads, nk, hd), f32),
            jax.ShapeDtypeStruct((heads, nk, hd), f32),
        ],
        compiler_params=pltpu.CompilerParams(
            dimension_semantics=("parallel", "arbitrary"), vmem_limit_bytes=48 * 1024 * 1024
        ),
    )(qT, kT, vT, kTT, gaT, lt, dl, cm)


def on_device(queries_in, hits_in, w_query, w_key, w_value, w_out, mask_list, grad_out):
    f32 = jnp.float32
    bf16 = jnp.bfloat16
    region_index = lax.axis_index("region")
    n_queries, width = queries_in.shape
    n_hits = hits_in.shape[0]
    head_dim = width // HEADS
    scale = 1.0 / math.sqrt(head_dim)
    hit_blocks = n_hits // BLOCK
    q_blocks = n_queries // BLOCK
    local_ids = region_index * hit_blocks + jnp.arange(hit_blocks, dtype=jnp.int32)
    blockmask = jnp.any(mask_list[:, :, None] == local_ids[None, None, :], axis=1)
    cm = jnp.repeat(blockmask.T.astype(f32), BLOCK, axis=1).reshape(hit_blocks, 1, n_queries)

    def heads(x):
        return x.reshape(x.shape[0], HEADS, head_dim).transpose(1, 0, 2)

    def joined(x):
        return x.transpose(1, 0, 2).reshape(x.shape[1], width)

    query = jnp.dot(queries_in, w_query, preferred_element_type=f32).astype(bf16)
    keys = jnp.dot(hits_in, w_key, preferred_element_type=f32).astype(bf16)
    vals = jnp.dot(hits_in, w_value, preferred_element_type=f32).astype(bf16)
    qT, kT, vT = heads(query), heads(keys), heads(vals)

    regions = lax.axis_size("region")
    numer_r, max_r, total_r = _forward(qT, kT, vT.transpose(0, 2, 1), cm, scale)
    numer = numer_r.transpose(2, 0, 1).reshape(n_queries, width)
    peak = max_r.reshape(HEADS, n_queries)
    total = total_r.reshape(HEADS, n_queries)
    rows = n_queries
    base = 0
    steps = []
    k = 0
    while (1 << k) < regions:
        bit = (region_index >> k) & 1
        half = rows // 2
        pairs = [(i, i ^ (1 << k)) for i in range(regions)]
        mine = (
            lax.dynamic_slice_in_dim(numer, bit * half, half, 0),
            lax.dynamic_slice_in_dim(peak, bit * half, half, 1),
            lax.dynamic_slice_in_dim(total, bit * half, half, 1),
        )
        theirs = lax.ppermute(
            (
                lax.dynamic_slice_in_dim(numer, (1 - bit) * half, half, 0).astype(bf16),
                lax.dynamic_slice_in_dim(peak, (1 - bit) * half, half, 1),
                lax.dynamic_slice_in_dim(total, (1 - bit) * half, half, 1),
            ),
            "region",
            pairs,
        )
        top = jnp.maximum(mine[1], theirs[1])
        scale_a = jnp.exp(mine[1] - top)
        scale_b = jnp.exp(theirs[1] - top)
        numer = mine[0] * jnp.repeat(scale_a.T, head_dim, axis=1) + theirs[0].astype(f32) * jnp.repeat(
            scale_b.T, head_dim, axis=1
        )
        total = mine[2] * scale_a + theirs[2] * scale_b
        peak = top
        base = base + bit * half
        steps.append((k, bit, half))
        rows = half
        k += 1
    attended_part = (numer / jnp.repeat(total.T, head_dim, axis=1)).astype(bf16)
    log_part = peak + jnp.log(total)
    grad_att = lax.dot_general(
        grad_out, w_out, (((1,), (1,)), ((), ())), preferred_element_type=f32
    ).astype(bf16)
    grad_att_part = lax.dynamic_slice_in_dim(grad_att, base, rows, 0)
    delta_part = jnp.sum(
        (grad_att_part.astype(f32) * attended_part.astype(f32)).reshape(rows, HEADS, head_dim),
        axis=2,
    ).T
    gathered = (attended_part, jnp.concatenate([log_part, delta_part], axis=0))
    for k, bit, half in reversed(steps):
        pairs = [(i, i ^ (1 << k)) for i in range(regions)]
        other = lax.ppermute(gathered, "region", pairs)
        lo = jax.tree.map(lambda a, b: jnp.where(bit == 0, a, b), gathered, other)
        hi = jax.tree.map(lambda a, b: jnp.where(bit == 0, b, a), gathered, other)
        gathered = (
            jnp.concatenate([lo[0], hi[0]], axis=0),
            jnp.concatenate([lo[1], hi[1]], axis=1),
        )
    attended = gathered[0]
    log_total = gathered[1][:HEADS].reshape(HEADS, 1, n_queries)
    deltas = gathered[1][HEADS:].reshape(HEADS, 1, n_queries)
    layer_out = (
        queries_in.astype(f32) + jnp.dot(attended, w_out, preferred_element_type=f32)
    ).astype(bf16)
    grad_wo = jnp.einsum("qa,qb->ab", attended, grad_out, preferred_element_type=f32)
    gaT = heads(grad_att)

    dq_r, dk, dv = _backward(qT, kT, vT, kT.transpose(0, 2, 1), gaT, log_total, deltas, cm, scale)
    keys_grad = joined(dk).astype(bf16)
    vals_grad = joined(dv).astype(bf16)
    wk_part = jnp.einsum("ka,kb->ab", hits_in, keys_grad, preferred_element_type=f32)
    wv_part = jnp.einsum("ka,kb->ab", hits_in, vals_grad, preferred_element_type=f32)
    query_grad_sum = lax.psum(
        dq_r.transpose(2, 0, 1).reshape(n_queries, width).astype(bf16), "region"
    )
    summed = jnp.concatenate([wk_part, wv_part], axis=0)
    for k, bit, half in steps:
        half = summed.shape[0] // 2
        pairs = [(i, i ^ (1 << k)) for i in range(regions)]
        other = lax.ppermute(
            lax.dynamic_slice_in_dim(summed, (1 - bit) * half, half, 0).astype(bf16), "region", pairs
        )
        summed = lax.dynamic_slice_in_dim(summed, bit * half, half, 0) + other.astype(f32)
    summed = summed.astype(bf16)
    for k, bit, half in reversed(steps):
        pairs = [(i, i ^ (1 << k)) for i in range(regions)]
        other = lax.ppermute(summed, "region", pairs)
        summed = jnp.concatenate(
            [jnp.where(bit == 0, summed, other), jnp.where(bit == 0, other, summed)], axis=0
        )
    summed = summed.astype(f32)
    grad_wk = summed[:width]
    grad_wv = summed[width:]
    grad_q = query_grad_sum
    grad_wq = jnp.einsum("qa,qb->ab", queries_in, grad_q, preferred_element_type=f32)
    grad_queries = (
        grad_out.astype(f32)
        + lax.dot_general(grad_q, w_query, (((1,), (1,)), ((), ())), preferred_element_type=f32)
    ).astype(bf16)
    grad_hits = (
        lax.dot_general(keys_grad, w_key, (((1,), (1,)), ((), ())), preferred_element_type=f32)
        + lax.dot_general(vals_grad, w_value, (((1,), (1,)), ((), ())), preferred_element_type=f32)
    ).astype(bf16)
    return (layer_out, grad_queries, grad_hits, grad_wq, grad_wk, grad_wv, grad_wo)


def solution(mesh):
    in_specs = (
        P("event", None),
        P(("event", "region"), None),
        P(),
        P(),
        P(),
        P(),
        P("event", None),
        P("event", None),
    )
    out_specs = (
        P("event", None),
        P("event", None),
        P(("event", "region"), None),
        P("event", None),
        P("event", None),
        P("event", None),
        P("event", None),
    )
    return jax.shard_map(
        on_device, mesh=mesh, in_specs=in_specs, out_specs=out_specs, check_vma=False
    )
```

```python
import functools
import math

import jax
import jax.numpy as jnp
from jax import lax
from jax.experimental import pallas as pl
from jax.experimental.pallas import tpu as pltpu
from jax.sharding import PartitionSpec as P

HEADS = 8
BLOCK = 128
TQ = 512


def _fwd_kernel(q_ref, k_ref, vt_ref, cm_ref, numer_ref, m_ref, l_ref, *, scale):
    q = q_ref[0]
    k = k_ref[0]
    vt = vt_ref[0]
    s = lax.dot_general(k, q, (((1,), (1,)), ((), ())), preferred_element_type=jnp.float32) * scale
    nk, tq = s.shape
    hb = nk // BLOCK
    s3 = s.reshape(hb, BLOCK, tq)
    allowed = cm_ref[...] > 0.5
    masked = jnp.where(allowed, s3, -1e30)
    mx = jnp.max(jnp.max(masked, axis=0), axis=0, keepdims=True)
    e = jnp.where(allowed, jnp.exp(masked - mx[None]), 0.0)
    tot = jnp.sum(jnp.sum(e, axis=0), axis=0, keepdims=True)
    numer_ref[0] = jnp.dot(
        vt, e.reshape(nk, tq).astype(jnp.bfloat16), preferred_element_type=jnp.float32
    )
    m_ref[0] = mx
    l_ref[0] = tot


def _bwd_kernel(q_ref, k_ref, v_ref, kt_ref, ga_ref, lt_ref, dl_ref, cm_ref, dq_ref, dk_ref, dv_ref, *, scale):
    i = pl.program_id(1)
    single = dk_ref.dtype == jnp.bfloat16

    if not single:
        @pl.when(i == 0)
        def _():
            dk_ref[...] = jnp.zeros_like(dk_ref)
            dv_ref[...] = jnp.zeros_like(dv_ref)

    q = q_ref[0]
    k = k_ref[0]
    v = v_ref[0]
    ga = ga_ref[0]
    s = lax.dot_general(k, q, (((1,), (1,)), ((), ())), preferred_element_type=jnp.float32) * scale
    nk, tq = s.shape
    hb = nk // BLOCK
    s3 = s.reshape(hb, BLOCK, tq)
    allowed = cm_ref[...] > 0.5
    p = jnp.where(allowed, jnp.exp(s3 - lt_ref[...]), 0.0).reshape(nk, tq)
    dv = jnp.dot(p.astype(jnp.bfloat16), ga, preferred_element_type=jnp.float32)
    dp = lax.dot_general(v, ga, (((1,), (1,)), ((), ())), preferred_element_type=jnp.float32)
    ds = (p * (dp - dl_ref[0]) * scale).astype(jnp.bfloat16)
    dk = jnp.dot(ds, q, preferred_element_type=jnp.float32)
    if single:
        dv_ref[0] = dv.astype(dv_ref.dtype)
        dk_ref[0] = dk.astype(dk_ref.dtype)
    else:
        dv_ref[0] += dv
        dk_ref[0] += dk
    dq_ref[0] = jnp.dot(kt_ref[0], ds, preferred_element_type=jnp.float32).astype(dq_ref.dtype)


def _forward(qT, kT, vTT, cm, scale):
    heads, nq, hd = qT.shape
    nk = kT.shape[1]
    hb = nk // BLOCK
    tile = min(nq, 2 * TQ)
    f32 = jnp.float32
    return pl.pallas_call(
        functools.partial(_fwd_kernel, scale=scale),
        grid=(heads, nq // tile),
        in_specs=[
            pl.BlockSpec((1, tile, hd), lambda h, i: (h, i, 0)),
            pl.BlockSpec((1, nk, hd), lambda h, i: (h, 0, 0)),
            pl.BlockSpec((1, hd, nk), lambda h, i: (h, 0, 0)),
            pl.BlockSpec((hb, 1, tile), lambda h, i: (0, 0, i)),
        ],
        out_specs=[
            pl.BlockSpec((1, hd, tile), lambda h, i: (h, 0, i)),
            pl.BlockSpec((1, 1, tile), lambda h, i: (h, 0, i)),
            pl.BlockSpec((1, 1, tile), lambda h, i: (h, 0, i)),
        ],
        out_shape=[
            jax.ShapeDtypeStruct((heads, hd, nq), f32),
            jax.ShapeDtypeStruct((heads, 1, nq), f32),
            jax.ShapeDtypeStruct((heads, 1, nq), f32),
        ],
        compiler_params=pltpu.CompilerParams(vmem_limit_bytes=48 * 1024 * 1024),
    )(qT, kT, vTT, cm)


def _backward(qT, kT, vT, kTT, gaT, lt, dl, cm, scale):
    heads, nq, hd = qT.shape
    nk = kT.shape[1]
    hb = nk // BLOCK
    tile = min(nq, 2 * TQ)
    f32 = jnp.float32
    grad_type = jnp.bfloat16 if tile == nq else f32
    return pl.pallas_call(
        functools.partial(_bwd_kernel, scale=scale),
        grid=(heads, nq // tile),
        in_specs=[
            pl.BlockSpec((1, tile, hd), lambda h, i: (h, i, 0)),
            pl.BlockSpec((1, nk, hd), lambda h, i: (h, 0, 0)),
            pl.BlockSpec((1, nk, hd), lambda h, i: (h, 0, 0)),
            pl.BlockSpec((1, hd, nk), lambda h, i: (h, 0, 0)),
            pl.BlockSpec((1, tile, hd), lambda h, i: (h, i, 0)),
            pl.BlockSpec((1, 1, tile), lambda h, i: (h, 0, i)),
            pl.BlockSpec((1, 1, tile), lambda h, i: (h, 0, i)),
            pl.BlockSpec((hb, 1, tile), lambda h, i: (0, 0, i)),
        ],
        out_specs=[
            pl.BlockSpec((1, hd, tile), lambda h, i: (h, 0, i)),
            pl.BlockSpec((1, nk, hd), lambda h, i: (h, 0, 0)),
            pl.BlockSpec((1, nk, hd), lambda h, i: (h, 0, 0)),
        ],
        out_shape=[
            jax.ShapeDtypeStruct((heads, hd, nq), jnp.bfloat16),
            jax.ShapeDtypeStruct((heads, nk, hd), grad_type),
            jax.ShapeDtypeStruct((heads, nk, hd), grad_type),
        ],
        compiler_params=pltpu.CompilerParams(
            dimension_semantics=("parallel", "arbitrary"), vmem_limit_bytes=48 * 1024 * 1024
        ),
    )(qT, kT, vT, kTT, gaT, lt, dl, cm)


def on_device(queries_in, hits_in, w_query, w_key, w_value, w_out, mask_list, grad_out):
    f32 = jnp.float32
    bf16 = jnp.bfloat16
    region_index = lax.axis_index("region")
    n_queries, width = queries_in.shape
    n_hits = hits_in.shape[0]
    head_dim = width // HEADS
    scale = 1.0 / math.sqrt(head_dim)
    hit_blocks = n_hits // BLOCK
    q_blocks = n_queries // BLOCK
    local_ids = region_index * hit_blocks + jnp.arange(hit_blocks, dtype=jnp.int32)
    blockmask = jnp.any(mask_list[:, :, None] == local_ids[None, None, :], axis=1)
    cm = jnp.repeat(blockmask.T.astype(f32), BLOCK, axis=1).reshape(hit_blocks, 1, n_queries)

    def heads(x):
        return x.reshape(x.shape[0], HEADS, head_dim).transpose(1, 0, 2)

    def joined(x):
        return x.transpose(1, 0, 2).reshape(x.shape[1], width)

    query = jnp.dot(queries_in, w_query, preferred_element_type=f32).astype(bf16)
    keys = jnp.dot(hits_in, w_key, preferred_element_type=f32).astype(bf16)
    vals = jnp.dot(hits_in, w_value, preferred_element_type=f32).astype(bf16)
    qT, kT, vT = heads(query), heads(keys), heads(vals)

    regions = lax.axis_size("region")
    numer_r, max_r, total_r = _forward(qT, kT, vT.transpose(0, 2, 1), cm, scale)
    numer = numer_r.transpose(2, 0, 1).reshape(n_queries, width)
    peak = max_r.reshape(HEADS, n_queries)
    total = total_r.reshape(HEADS, n_queries)
    rows = n_queries
    base = 0
    steps = []
    k = 0
    while (1 << k) < regions:
        bit = (region_index >> k) & 1
        half = rows // 2
        pairs = [(i, i ^ (1 << k)) for i in range(regions)]
        mine = (
            lax.dynamic_slice_in_dim(numer, bit * half, half, 0),
            lax.dynamic_slice_in_dim(peak, bit * half, half, 1),
            lax.dynamic_slice_in_dim(total, bit * half, half, 1),
        )
        theirs = lax.ppermute(
            (
                lax.dynamic_slice_in_dim(numer, (1 - bit) * half, half, 0).astype(bf16),
                lax.dynamic_slice_in_dim(peak, (1 - bit) * half, half, 1),
                lax.dynamic_slice_in_dim(total, (1 - bit) * half, half, 1),
            ),
            "region",
            pairs,
        )
        top = jnp.maximum(mine[1], theirs[1])
        scale_a = jnp.exp(mine[1] - top)
        scale_b = jnp.exp(theirs[1] - top)
        numer = mine[0] * jnp.repeat(scale_a.T, head_dim, axis=1) + theirs[0].astype(f32) * jnp.repeat(
            scale_b.T, head_dim, axis=1
        )
        total = mine[2] * scale_a + theirs[2] * scale_b
        peak = top
        base = base + bit * half
        steps.append((k, bit, half))
        rows = half
        k += 1
    attended_part = (numer / jnp.repeat(total.T, head_dim, axis=1)).astype(bf16)
    log_part = peak + jnp.log(total)
    grad_att = lax.dot_general(
        grad_out, w_out, (((1,), (1,)), ((), ())), preferred_element_type=f32
    ).astype(bf16)
    grad_att_part = lax.dynamic_slice_in_dim(grad_att, base, rows, 0)
    delta_part = jnp.sum(
        (grad_att_part.astype(f32) * attended_part.astype(f32)).reshape(rows, HEADS, head_dim),
        axis=2,
    ).T
    gathered = (attended_part, jnp.concatenate([log_part, delta_part], axis=0))
    for k, bit, half in reversed(steps):
        pairs = [(i, i ^ (1 << k)) for i in range(regions)]
        other = lax.ppermute(gathered, "region", pairs)
        lo = jax.tree.map(lambda a, b: jnp.where(bit == 0, a, b), gathered, other)
        hi = jax.tree.map(lambda a, b: jnp.where(bit == 0, b, a), gathered, other)
        gathered = (
            jnp.concatenate([lo[0], hi[0]], axis=0),
            jnp.concatenate([lo[1], hi[1]], axis=1),
        )
    attended = gathered[0]
    log_total = gathered[1][:HEADS].reshape(HEADS, 1, n_queries)
    deltas = gathered[1][HEADS:].reshape(HEADS, 1, n_queries)
    layer_out = (
        queries_in.astype(f32) + jnp.dot(attended, w_out, preferred_element_type=f32)
    ).astype(bf16)
    grad_wo = jnp.einsum("qa,qb->ab", attended, grad_out, preferred_element_type=f32)
    gaT = heads(grad_att)

    dq_r, dk, dv = _backward(qT, kT, vT, kT.transpose(0, 2, 1), gaT, log_total, deltas, cm, scale)
    keys_grad = joined(dk).astype(bf16)
    vals_grad = joined(dv).astype(bf16)
    wk_part = jnp.einsum("ka,kb->ab", hits_in, keys_grad, preferred_element_type=f32)
    wv_part = jnp.einsum("ka,kb->ab", hits_in, vals_grad, preferred_element_type=f32)
    query_grad_sum, grad_wk, grad_wv = lax.psum(
        (dq_r.transpose(2, 0, 1).reshape(n_queries, width).astype(bf16), wk_part.astype(bf16), wv_part.astype(bf16)), "region"
    )
    grad_wk = grad_wk.astype(f32)
    grad_wv = grad_wv.astype(f32)
    grad_q = query_grad_sum
    grad_wq = jnp.einsum("qa,qb->ab", queries_in, grad_q, preferred_element_type=f32)
    grad_queries = (
        grad_out.astype(f32)
        + lax.dot_general(grad_q, w_query, (((1,), (1,)), ((), ())), preferred_element_type=f32)
    ).astype(bf16)
    grad_hits = (
        lax.dot_general(keys_grad, w_key, (((1,), (1,)), ((), ())), preferred_element_type=f32)
        + lax.dot_general(vals_grad, w_value, (((1,), (1,)), ((), ())), preferred_element_type=f32)
    ).astype(bf16)
    return (layer_out, grad_queries, grad_hits, grad_wq, grad_wk, grad_wv, grad_wo)


def solution(mesh):
    in_specs = (
        P("event", None),
        P(("event", "region"), None),
        P(),
        P(),
        P(),
        P(),
        P("event", None),
        P("event", None),
    )
    out_specs = (
        P("event", None),
        P("event", None),
        P(("event", "region"), None),
        P("event", None),
        P("event", None),
        P("event", None),
        P("event", None),
    )
    return jax.shard_map(
        on_device, mesh=mesh, in_specs=in_specs, out_specs=out_specs, check_vma=False
    )
```

```python
import functools
import math

import jax
import jax.numpy as jnp
from jax import lax
from jax.experimental import pallas as pl
from jax.experimental.pallas import tpu as pltpu
from jax.sharding import PartitionSpec as P

HEADS = 8
BLOCK = 128
TQ = 512


def _fwd_kernel(q_ref, k_ref, vt_ref, cm_ref, numer_ref, m_ref, l_ref, *, scale):
    q = q_ref[0]
    k = k_ref[0]
    vt = vt_ref[0]
    s = lax.dot_general(k, q, (((1,), (1,)), ((), ())), preferred_element_type=jnp.float32) * scale
    nk, tq = s.shape
    hb = nk // BLOCK
    s3 = s.reshape(hb, BLOCK, tq)
    allowed = cm_ref[...] > 0.5
    masked = jnp.where(allowed, s3, -1e30)
    mx = jnp.max(jnp.max(masked, axis=0), axis=0, keepdims=True)
    e = jnp.where(allowed, jnp.exp(masked - mx[None]), 0.0)
    tot = jnp.sum(jnp.sum(e, axis=0), axis=0, keepdims=True)
    numer_ref[0] = jnp.dot(
        vt, e.reshape(nk, tq).astype(jnp.bfloat16), preferred_element_type=jnp.float32
    )
    m_ref[0] = mx
    l_ref[0] = tot


def _bwd_kernel(q_ref, k_ref, v_ref, kt_ref, ga_ref, lt_ref, dl_ref, cm_ref, dq_ref, dk_ref, dv_ref, *, scale):
    i = pl.program_id(1)
    single = dk_ref.dtype == jnp.bfloat16

    if not single:
        @pl.when(i == 0)
        def _():
            dk_ref[...] = jnp.zeros_like(dk_ref)
            dv_ref[...] = jnp.zeros_like(dv_ref)

    q = q_ref[0]
    k = k_ref[0]
    v = v_ref[0]
    ga = ga_ref[0]
    s = lax.dot_general(k, q, (((1,), (1,)), ((), ())), preferred_element_type=jnp.float32) * scale
    nk, tq = s.shape
    hb = nk // BLOCK
    s3 = s.reshape(hb, BLOCK, tq)
    allowed = cm_ref[...] > 0.5
    p = jnp.where(allowed, jnp.exp(s3 - lt_ref[...]), 0.0).reshape(nk, tq)
    dv = jnp.dot(p.astype(jnp.bfloat16), ga, preferred_element_type=jnp.float32)
    dp = lax.dot_general(v, ga, (((1,), (1,)), ((), ())), preferred_element_type=jnp.float32)
    ds = (p * (dp - dl_ref[0]) * scale).astype(jnp.bfloat16)
    dk = jnp.dot(ds, q, preferred_element_type=jnp.float32)
    if single:
        dv_ref[0] = dv.astype(dv_ref.dtype)
        dk_ref[0] = dk.astype(dk_ref.dtype)
    else:
        dv_ref[0] += dv
        dk_ref[0] += dk
    dq_ref[0] = jnp.dot(kt_ref[0], ds, preferred_element_type=jnp.float32).astype(dq_ref.dtype)


def _forward(qT, kT, vTT, cm, scale):
    heads, nq, hd = qT.shape
    nk = kT.shape[1]
    hb = nk // BLOCK
    tile = min(nq, 2 * TQ)
    f32 = jnp.float32
    return pl.pallas_call(
        functools.partial(_fwd_kernel, scale=scale),
        grid=(heads, nq // tile),
        in_specs=[
            pl.BlockSpec((1, tile, hd), lambda h, i: (h, i, 0)),
            pl.BlockSpec((1, nk, hd), lambda h, i: (h, 0, 0)),
            pl.BlockSpec((1, hd, nk), lambda h, i: (h, 0, 0)),
            pl.BlockSpec((hb, 1, tile), lambda h, i: (0, 0, i)),
        ],
        out_specs=[
            pl.BlockSpec((1, hd, tile), lambda h, i: (h, 0, i)),
            pl.BlockSpec((1, 1, tile), lambda h, i: (h, 0, i)),
            pl.BlockSpec((1, 1, tile), lambda h, i: (h, 0, i)),
        ],
        out_shape=[
            jax.ShapeDtypeStruct((heads, hd, nq), f32),
            jax.ShapeDtypeStruct((heads, 1, nq), f32),
            jax.ShapeDtypeStruct((heads, 1, nq), f32),
        ],
        compiler_params=pltpu.CompilerParams(vmem_limit_bytes=48 * 1024 * 1024),
    )(qT, kT, vTT, cm)


def _backward(qT, kT, vT, kTT, gaT, lt, dl, cm, scale):
    heads, nq, hd = qT.shape
    nk = kT.shape[1]
    hb = nk // BLOCK
    tile = min(nq, 2 * TQ)
    f32 = jnp.float32
    grad_type = jnp.bfloat16 if tile == nq else f32
    return pl.pallas_call(
        functools.partial(_bwd_kernel, scale=scale),
        grid=(heads, nq // tile),
        in_specs=[
            pl.BlockSpec((1, tile, hd), lambda h, i: (h, i, 0)),
            pl.BlockSpec((1, nk, hd), lambda h, i: (h, 0, 0)),
            pl.BlockSpec((1, nk, hd), lambda h, i: (h, 0, 0)),
            pl.BlockSpec((1, hd, nk), lambda h, i: (h, 0, 0)),
            pl.BlockSpec((1, tile, hd), lambda h, i: (h, i, 0)),
            pl.BlockSpec((1, 1, tile), lambda h, i: (h, 0, i)),
            pl.BlockSpec((1, 1, tile), lambda h, i: (h, 0, i)),
            pl.BlockSpec((hb, 1, tile), lambda h, i: (0, 0, i)),
        ],
        out_specs=[
            pl.BlockSpec((1, hd, tile), lambda h, i: (h, 0, i)),
            pl.BlockSpec((1, nk, hd), lambda h, i: (h, 0, 0)),
            pl.BlockSpec((1, nk, hd), lambda h, i: (h, 0, 0)),
        ],
        out_shape=[
            jax.ShapeDtypeStruct((heads, hd, nq), jnp.bfloat16),
            jax.ShapeDtypeStruct((heads, nk, hd), grad_type),
            jax.ShapeDtypeStruct((heads, nk, hd), grad_type),
        ],
        compiler_params=pltpu.CompilerParams(
            dimension_semantics=("parallel", "arbitrary"), vmem_limit_bytes=48 * 1024 * 1024
        ),
    )(qT, kT, vT, kTT, gaT, lt, dl, cm)


def on_device(queries_in, hits_in, w_query, w_key, w_value, w_out, mask_list, grad_out):
    f32 = jnp.float32
    bf16 = jnp.bfloat16
    region_index = lax.axis_index("region")
    n_queries, width = queries_in.shape
    n_hits = hits_in.shape[0]
    head_dim = width // HEADS
    scale = 1.0 / math.sqrt(head_dim)
    hit_blocks = n_hits // BLOCK
    q_blocks = n_queries // BLOCK
    local_ids = region_index * hit_blocks + jnp.arange(hit_blocks, dtype=jnp.int32)
    blockmask = jnp.any(mask_list[:, :, None] == local_ids[None, None, :], axis=1)
    cm = jnp.repeat(blockmask.T.astype(f32), BLOCK, axis=1).reshape(hit_blocks, 1, n_queries)

    def heads(x):
        return x.reshape(x.shape[0], HEADS, head_dim).transpose(1, 0, 2)

    def joined(x):
        return x.transpose(1, 0, 2).reshape(x.shape[1], width)

    query = jnp.dot(queries_in, w_query, preferred_element_type=f32).astype(bf16)
    keys = jnp.dot(hits_in, w_key, preferred_element_type=f32).astype(bf16)
    vals = jnp.dot(hits_in, w_value, preferred_element_type=f32).astype(bf16)
    qT, kT, vT = heads(query), heads(keys), heads(vals)

    regions = lax.axis_size("region")
    numer_r, max_r, total_r = _forward(qT, kT, vT.transpose(0, 2, 1), cm, scale)
    numer = numer_r.transpose(2, 0, 1).reshape(n_queries, width)
    stats = jnp.concatenate([max_r.reshape(HEADS, n_queries), total_r.reshape(HEADS, n_queries)], axis=0)
    rows = n_queries
    base = 0
    steps = []
    k = 0
    while (1 << k) < regions:
        bit = (region_index >> k) & 1
        half = rows // 2
        pairs = [(i, i ^ (1 << k)) for i in range(regions)]
        mine_n = lax.dynamic_slice_in_dim(numer, bit * half, half, 0)
        mine_s = lax.dynamic_slice_in_dim(stats, bit * half, half, 1)
        theirs_n, theirs_s = lax.ppermute(
            (
                lax.dynamic_slice_in_dim(numer, (1 - bit) * half, half, 0).astype(bf16),
                lax.dynamic_slice_in_dim(stats, (1 - bit) * half, half, 1),
            ),
            "region",
            pairs,
        )
        top = jnp.maximum(mine_s[:HEADS], theirs_s[:HEADS])
        scale_a = jnp.exp(mine_s[:HEADS] - top)
        scale_b = jnp.exp(theirs_s[:HEADS] - top)
        numer = mine_n * jnp.repeat(scale_a.T, head_dim, axis=1) + theirs_n.astype(f32) * jnp.repeat(
            scale_b.T, head_dim, axis=1
        )
        stats = jnp.concatenate([top, mine_s[HEADS:] * scale_a + theirs_s[HEADS:] * scale_b], axis=0)
        base = base + bit * half
        steps.append((k, bit, half))
        rows = half
        k += 1
    peak = stats[:HEADS]
    total = stats[HEADS:]
    attended_part = (numer / jnp.repeat(total.T, head_dim, axis=1)).astype(bf16)
    log_part = peak + jnp.log(total)
    grad_att = lax.dot_general(
        grad_out, w_out, (((1,), (1,)), ((), ())), preferred_element_type=f32
    ).astype(bf16)
    grad_att_part = lax.dynamic_slice_in_dim(grad_att, base, rows, 0)
    delta_part = jnp.sum(
        (grad_att_part.astype(f32) * attended_part.astype(f32)).reshape(rows, HEADS, head_dim),
        axis=2,
    ).T
    gathered = (attended_part, jnp.concatenate([log_part, delta_part], axis=0))
    for k, bit, half in reversed(steps):
        pairs = [(i, i ^ (1 << k)) for i in range(regions)]
        other = lax.ppermute(gathered, "region", pairs)
        lo = jax.tree.map(lambda a, b: jnp.where(bit == 0, a, b), gathered, other)
        hi = jax.tree.map(lambda a, b: jnp.where(bit == 0, b, a), gathered, other)
        gathered = (
            jnp.concatenate([lo[0], hi[0]], axis=0),
            jnp.concatenate([lo[1], hi[1]], axis=1),
        )
    attended = gathered[0]
    log_total = gathered[1][:HEADS].reshape(HEADS, 1, n_queries)
    deltas = gathered[1][HEADS:].reshape(HEADS, 1, n_queries)
    layer_out = (
        queries_in.astype(f32) + jnp.dot(attended, w_out, preferred_element_type=f32)
    ).astype(bf16)
    grad_wo = jnp.einsum("qa,qb->ab", attended, grad_out, preferred_element_type=f32)
    gaT = heads(grad_att)

    dq_r, dk, dv = _backward(qT, kT, vT, kT.transpose(0, 2, 1), gaT, log_total, deltas, cm, scale)
    keys_grad = joined(dk).astype(bf16)
    vals_grad = joined(dv).astype(bf16)
    wk_part = jnp.einsum("ka,kb->ab", hits_in, keys_grad, preferred_element_type=f32)
    wv_part = jnp.einsum("ka,kb->ab", hits_in, vals_grad, preferred_element_type=f32)
    query_grad_sum, grad_wk, grad_wv = lax.psum(
        (dq_r.transpose(2, 0, 1).reshape(n_queries, width).astype(bf16), wk_part.astype(bf16), wv_part.astype(bf16)), "region"
    )
    grad_wk = grad_wk.astype(f32)
    grad_wv = grad_wv.astype(f32)
    grad_q = query_grad_sum
    grad_wq = jnp.einsum("qa,qb->ab", queries_in, grad_q, preferred_element_type=f32)
    grad_queries = (
        grad_out.astype(f32)
        + lax.dot_general(grad_q, w_query, (((1,), (1,)), ((), ())), preferred_element_type=f32)
    ).astype(bf16)
    grad_hits = (
        lax.dot_general(keys_grad, w_key, (((1,), (1,)), ((), ())), preferred_element_type=f32)
        + lax.dot_general(vals_grad, w_value, (((1,), (1,)), ((), ())), preferred_element_type=f32)
    ).astype(bf16)
    return (layer_out, grad_queries, grad_hits, grad_wq, grad_wk, grad_wv, grad_wo)


def solution(mesh):
    in_specs = (
        P("event", None),
        P(("event", "region"), None),
        P(),
        P(),
        P(),
        P(),
        P("event", None),
        P("event", None),
    )
    out_specs = (
        P("event", None),
        P("event", None),
        P(("event", "region"), None),
        P("event", None),
        P("event", None),
        P("event", None),
        P("event", None),
    )
    return jax.shard_map(
        on_device, mesh=mesh, in_specs=in_specs, out_specs=out_specs, check_vma=False
    )
```

```python
import functools
import math

import jax
import jax.numpy as jnp
from jax import lax
from jax.experimental import pallas as pl
from jax.experimental.pallas import tpu as pltpu
from jax.sharding import PartitionSpec as P

HEADS = 8
BLOCK = 128
TQ = 512


def _fwd_kernel(q_ref, k_ref, vt_ref, cm_ref, numer_ref, m_ref, l_ref, *, scale):
    q = q_ref[0]
    k = k_ref[0]
    vt = vt_ref[0]
    s = lax.dot_general(k, q, (((1,), (1,)), ((), ())), preferred_element_type=jnp.float32) * scale
    nk, tq = s.shape
    hb = nk // BLOCK
    s3 = s.reshape(hb, BLOCK, tq)
    allowed = cm_ref[...] > 0.5
    masked = jnp.where(allowed, s3, -1e30)
    mx = jnp.max(jnp.max(masked, axis=0), axis=0, keepdims=True)
    e = jnp.where(allowed, jnp.exp(masked - mx[None]), 0.0)
    tot = jnp.sum(jnp.sum(e, axis=0), axis=0, keepdims=True)
    numer_ref[0] = jnp.dot(
        vt, e.reshape(nk, tq).astype(jnp.bfloat16), preferred_element_type=jnp.float32
    )
    m_ref[0] = mx
    l_ref[0] = tot


def _bwd_kernel(q_ref, k_ref, v_ref, kt_ref, ga_ref, lt_ref, dl_ref, cm_ref, dq_ref, dk_ref, dv_ref, *, scale):
    i = pl.program_id(1)
    single = dk_ref.dtype == jnp.bfloat16

    if not single:
        @pl.when(i == 0)
        def _():
            dk_ref[...] = jnp.zeros_like(dk_ref)
            dv_ref[...] = jnp.zeros_like(dv_ref)

    q = q_ref[0]
    k = k_ref[0]
    v = v_ref[0]
    ga = ga_ref[0]
    s = lax.dot_general(k, q, (((1,), (1,)), ((), ())), preferred_element_type=jnp.float32) * scale
    nk, tq = s.shape
    hb = nk // BLOCK
    s3 = s.reshape(hb, BLOCK, tq)
    allowed = cm_ref[...] > 0.5
    p = jnp.where(allowed, jnp.exp(s3 - lt_ref[...]), 0.0).reshape(nk, tq)
    dv = jnp.dot(p.astype(jnp.bfloat16), ga, preferred_element_type=jnp.float32)
    dp = lax.dot_general(v, ga, (((1,), (1,)), ((), ())), preferred_element_type=jnp.float32)
    ds = (p * (dp - dl_ref[0]) * scale).astype(jnp.bfloat16)
    dk = jnp.dot(ds, q, preferred_element_type=jnp.float32)
    if single:
        dv_ref[0] = dv.astype(dv_ref.dtype)
        dk_ref[0] = dk.astype(dk_ref.dtype)
    else:
        dv_ref[0] += dv
        dk_ref[0] += dk
    dq_ref[0] = jnp.dot(kt_ref[0], ds, preferred_element_type=jnp.float32).astype(dq_ref.dtype)


def _forward(qT, kT, vTT, cm, scale):
    heads, nq, hd = qT.shape
    nk = kT.shape[1]
    hb = nk // BLOCK
    tile = min(nq, 2 * TQ)
    f32 = jnp.float32
    return pl.pallas_call(
        functools.partial(_fwd_kernel, scale=scale),
        grid=(heads, nq // tile),
        in_specs=[
            pl.BlockSpec((1, tile, hd), lambda h, i: (h, i, 0)),
            pl.BlockSpec((1, nk, hd), lambda h, i: (h, 0, 0)),
            pl.BlockSpec((1, hd, nk), lambda h, i: (h, 0, 0)),
            pl.BlockSpec((hb, 1, tile), lambda h, i: (0, 0, i)),
        ],
        out_specs=[
            pl.BlockSpec((1, hd, tile), lambda h, i: (h, 0, i)),
            pl.BlockSpec((1, 1, tile), lambda h, i: (h, 0, i)),
            pl.BlockSpec((1, 1, tile), lambda h, i: (h, 0, i)),
        ],
        out_shape=[
            jax.ShapeDtypeStruct((heads, hd, nq), f32),
            jax.ShapeDtypeStruct((heads, 1, nq), f32),
            jax.ShapeDtypeStruct((heads, 1, nq), f32),
        ],
        compiler_params=pltpu.CompilerParams(vmem_limit_bytes=48 * 1024 * 1024),
    )(qT, kT, vTT, cm)


def _backward(qT, kT, vT, kTT, gaT, lt, dl, cm, scale):
    heads, nq, hd = qT.shape
    nk = kT.shape[1]
    hb = nk // BLOCK
    tile = min(nq, 2 * TQ)
    f32 = jnp.float32
    grad_type = jnp.bfloat16 if tile == nq else f32
    return pl.pallas_call(
        functools.partial(_bwd_kernel, scale=scale),
        grid=(heads, nq // tile),
        in_specs=[
            pl.BlockSpec((1, tile, hd), lambda h, i: (h, i, 0)),
            pl.BlockSpec((1, nk, hd), lambda h, i: (h, 0, 0)),
            pl.BlockSpec((1, nk, hd), lambda h, i: (h, 0, 0)),
            pl.BlockSpec((1, hd, nk), lambda h, i: (h, 0, 0)),
            pl.BlockSpec((1, tile, hd), lambda h, i: (h, i, 0)),
            pl.BlockSpec((1, 1, tile), lambda h, i: (h, 0, i)),
            pl.BlockSpec((1, 1, tile), lambda h, i: (h, 0, i)),
            pl.BlockSpec((hb, 1, tile), lambda h, i: (0, 0, i)),
        ],
        out_specs=[
            pl.BlockSpec((1, hd, tile), lambda h, i: (h, 0, i)),
            pl.BlockSpec((1, nk, hd), lambda h, i: (h, 0, 0)),
            pl.BlockSpec((1, nk, hd), lambda h, i: (h, 0, 0)),
        ],
        out_shape=[
            jax.ShapeDtypeStruct((heads, hd, nq), jnp.bfloat16),
            jax.ShapeDtypeStruct((heads, nk, hd), grad_type),
            jax.ShapeDtypeStruct((heads, nk, hd), grad_type),
        ],
        compiler_params=pltpu.CompilerParams(
            dimension_semantics=("parallel", "arbitrary"), vmem_limit_bytes=48 * 1024 * 1024
        ),
    )(qT, kT, vT, kTT, gaT, lt, dl, cm)


def on_device(queries_in, hits_in, w_query, w_key, w_value, w_out, mask_list, grad_out):
    f32 = jnp.float32
    bf16 = jnp.bfloat16
    region_index = lax.axis_index("region")
    n_queries, width = queries_in.shape
    n_hits = hits_in.shape[0]
    head_dim = width // HEADS
    scale = 1.0 / math.sqrt(head_dim)
    hit_blocks = n_hits // BLOCK
    q_blocks = n_queries // BLOCK
    local_ids = region_index * hit_blocks + jnp.arange(hit_blocks, dtype=jnp.int32)
    blockmask = jnp.any(mask_list[:, :, None] == local_ids[None, None, :], axis=1)
    cm = jnp.repeat(blockmask.T.astype(f32), BLOCK, axis=1).reshape(hit_blocks, 1, n_queries)

    def heads(x):
        return x.reshape(x.shape[0], HEADS, head_dim).transpose(1, 0, 2)

    def joined(x):
        return x.transpose(1, 0, 2).reshape(x.shape[1], width)

    query = jnp.dot(queries_in, w_query, preferred_element_type=f32).astype(bf16)
    keys = jnp.dot(hits_in, w_key, preferred_element_type=f32).astype(bf16)
    vals = jnp.dot(hits_in, w_value, preferred_element_type=f32).astype(bf16)
    qT, kT, vT = heads(query), heads(keys), heads(vals)

    regions = lax.axis_size("region")
    numer_r, max_r, total_r = _forward(qT, kT, vT.transpose(0, 2, 1), cm, scale)
    numer = numer_r.transpose(2, 0, 1).reshape(n_queries, width)
    k_late = lax.optimization_barrier((kT, numer_r))[0]
    peak = max_r.reshape(HEADS, n_queries)
    total = total_r.reshape(HEADS, n_queries)
    rows = n_queries
    base = 0
    steps = []
    k = 0
    while (1 << k) < regions:
        bit = (region_index >> k) & 1
        half = rows // 2
        pairs = [(i, i ^ (1 << k)) for i in range(regions)]
        mine = (
            lax.dynamic_slice_in_dim(numer, bit * half, half, 0),
            lax.dynamic_slice_in_dim(peak, bit * half, half, 1),
            lax.dynamic_slice_in_dim(total, bit * half, half, 1),
        )
        theirs = lax.ppermute(
            (
                lax.dynamic_slice_in_dim(numer, (1 - bit) * half, half, 0).astype(bf16),
                lax.dynamic_slice_in_dim(peak, (1 - bit) * half, half, 1),
                lax.dynamic_slice_in_dim(total, (1 - bit) * half, half, 1),
            ),
            "region",
            pairs,
        )
        top = jnp.maximum(mine[1], theirs[1])
        scale_a = jnp.exp(mine[1] - top)
        scale_b = jnp.exp(theirs[1] - top)
        numer = mine[0] * jnp.repeat(scale_a.T, head_dim, axis=1) + theirs[0].astype(f32) * jnp.repeat(
            scale_b.T, head_dim, axis=1
        )
        total = mine[2] * scale_a + theirs[2] * scale_b
        peak = top
        base = base + bit * half
        steps.append((k, bit, half))
        rows = half
        k += 1
    attended_part = (numer / jnp.repeat(total.T, head_dim, axis=1)).astype(bf16)
    log_part = peak + jnp.log(total)
    grad_att = lax.dot_general(
        grad_out, w_out, (((1,), (1,)), ((), ())), preferred_element_type=f32
    ).astype(bf16)
    grad_att_part = lax.dynamic_slice_in_dim(grad_att, base, rows, 0)
    delta_part = jnp.sum(
        (grad_att_part.astype(f32) * attended_part.astype(f32)).reshape(rows, HEADS, head_dim),
        axis=2,
    ).T
    gathered = (attended_part, jnp.concatenate([log_part, delta_part], axis=0))
    for k, bit, half in reversed(steps):
        pairs = [(i, i ^ (1 << k)) for i in range(regions)]
        other = lax.ppermute(gathered, "region", pairs)
        lo = jax.tree.map(lambda a, b: jnp.where(bit == 0, a, b), gathered, other)
        hi = jax.tree.map(lambda a, b: jnp.where(bit == 0, b, a), gathered, other)
        gathered = (
            jnp.concatenate([lo[0], hi[0]], axis=0),
            jnp.concatenate([lo[1], hi[1]], axis=1),
        )
    attended = gathered[0]
    log_total = gathered[1][:HEADS].reshape(HEADS, 1, n_queries)
    deltas = gathered[1][HEADS:].reshape(HEADS, 1, n_queries)
    layer_out = (
        queries_in.astype(f32) + jnp.dot(attended, w_out, preferred_element_type=f32)
    ).astype(bf16)
    grad_wo = jnp.einsum("qa,qb->ab", attended, grad_out, preferred_element_type=f32)
    gaT = heads(grad_att)

    dq_r, dk, dv = _backward(qT, kT, vT, k_late.transpose(0, 2, 1), gaT, log_total, deltas, cm, scale)
    keys_grad = joined(dk).astype(bf16)
    vals_grad = joined(dv).astype(bf16)
    wk_part = jnp.einsum("ka,kb->ab", hits_in, keys_grad, preferred_element_type=f32)
    wv_part = jnp.einsum("ka,kb->ab", hits_in, vals_grad, preferred_element_type=f32)
    query_grad_sum, grad_wk, grad_wv = lax.psum(
        (dq_r.transpose(2, 0, 1).reshape(n_queries, width).astype(bf16), wk_part.astype(bf16), wv_part.astype(bf16)), "region"
    )
    grad_wk = grad_wk.astype(f32)
    grad_wv = grad_wv.astype(f32)
    grad_q = query_grad_sum
    grad_wq = jnp.einsum("qa,qb->ab", queries_in, grad_q, preferred_element_type=f32)
    grad_queries = (
        grad_out.astype(f32)
        + lax.dot_general(grad_q, w_query, (((1,), (1,)), ((), ())), preferred_element_type=f32)
    ).astype(bf16)
    grad_hits = (
        lax.dot_general(keys_grad, w_key, (((1,), (1,)), ((), ())), preferred_element_type=f32)
        + lax.dot_general(vals_grad, w_value, (((1,), (1,)), ((), ())), preferred_element_type=f32)
    ).astype(bf16)
    return (layer_out, grad_queries, grad_hits, grad_wq, grad_wk, grad_wv, grad_wo)


def solution(mesh):
    in_specs = (
        P("event", None),
        P(("event", "region"), None),
        P(),
        P(),
        P(),
        P(),
        P("event", None),
        P("event", None),
    )
    out_specs = (
        P("event", None),
        P("event", None),
        P(("event", "region"), None),
        P("event", None),
        P("event", None),
        P("event", None),
        P("event", None),
    )
    return jax.shard_map(
        on_device, mesh=mesh, in_specs=in_specs, out_specs=out_specs, check_vma=False
    )
```

```python
import functools
import math

import jax
import jax.numpy as jnp
from jax import lax
from jax.experimental import pallas as pl
from jax.experimental.pallas import tpu as pltpu
from jax.sharding import PartitionSpec as P

HEADS = 8
BLOCK = 128
TQ = 512


def _fwd_kernel(q_ref, k_ref, vt_ref, cm_ref, numer_ref, m_ref, l_ref, *, scale):
    q = q_ref[0]
    k = k_ref[0]
    vt = vt_ref[0]
    s = lax.dot_general(k, q, (((1,), (1,)), ((), ())), preferred_element_type=jnp.float32) * scale
    nk, tq = s.shape
    hb = nk // BLOCK
    s3 = s.reshape(hb, BLOCK, tq)
    allowed = cm_ref[...] > 0.5
    masked = jnp.where(allowed, s3, -1e30)
    mx = jnp.max(jnp.max(masked, axis=0), axis=0, keepdims=True)
    e = jnp.where(allowed, jnp.exp(masked - mx[None]), 0.0)
    tot = jnp.sum(jnp.sum(e, axis=0), axis=0, keepdims=True)
    numer_ref[0] = jnp.dot(
        vt, e.reshape(nk, tq).astype(jnp.bfloat16), preferred_element_type=jnp.float32
    )
    m_ref[0] = mx
    l_ref[0] = tot


def _bwd_kernel(q_ref, k_ref, v_ref, kt_ref, ga_ref, lt_ref, dl_ref, cm_ref, dq_ref, dk_ref, dv_ref, *, scale):
    i = pl.program_id(1)
    single = dk_ref.dtype == jnp.bfloat16

    if not single:
        @pl.when(i == 0)
        def _():
            dk_ref[...] = jnp.zeros_like(dk_ref)
            dv_ref[...] = jnp.zeros_like(dv_ref)

    q = q_ref[0]
    k = k_ref[0]
    v = v_ref[0]
    ga = ga_ref[0]
    s = lax.dot_general(k, q, (((1,), (1,)), ((), ())), preferred_element_type=jnp.float32) * scale
    nk, tq = s.shape
    hb = nk // BLOCK
    s3 = s.reshape(hb, BLOCK, tq)
    allowed = cm_ref[...] > 0.5
    p = jnp.where(allowed, jnp.exp(s3 - lt_ref[...]), 0.0).reshape(nk, tq)
    dv = jnp.dot(p.astype(jnp.bfloat16), ga, preferred_element_type=jnp.float32)
    dp = lax.dot_general(v, ga, (((1,), (1,)), ((), ())), preferred_element_type=jnp.float32)
    ds = (p * (dp - dl_ref[0]) * scale).astype(jnp.bfloat16)
    dk = jnp.dot(ds, q, preferred_element_type=jnp.float32)
    if single:
        dv_ref[0] = dv.astype(dv_ref.dtype)
        dk_ref[0] = dk.astype(dk_ref.dtype)
    else:
        dv_ref[0] += dv
        dk_ref[0] += dk
    dq_ref[0] = jnp.dot(kt_ref[0], ds, preferred_element_type=jnp.float32).astype(dq_ref.dtype)


def _forward(qT, kT, vTT, cm, scale):
    heads, nq, hd = qT.shape
    nk = kT.shape[1]
    hb = nk // BLOCK
    tile = min(nq, 2 * TQ)
    f32 = jnp.float32
    return pl.pallas_call(
        functools.partial(_fwd_kernel, scale=scale),
        grid=(heads, nq // tile),
        in_specs=[
            pl.BlockSpec((1, tile, hd), lambda h, i: (h, i, 0)),
            pl.BlockSpec((1, nk, hd), lambda h, i: (h, 0, 0)),
            pl.BlockSpec((1, hd, nk), lambda h, i: (h, 0, 0)),
            pl.BlockSpec((hb, 1, tile), lambda h, i: (0, 0, i)),
        ],
        out_specs=[
            pl.BlockSpec((1, hd, tile), lambda h, i: (h, 0, i)),
            pl.BlockSpec((1, 1, tile), lambda h, i: (h, 0, i)),
            pl.BlockSpec((1, 1, tile), lambda h, i: (h, 0, i)),
        ],
        out_shape=[
            jax.ShapeDtypeStruct((heads, hd, nq), f32),
            jax.ShapeDtypeStruct((heads, 1, nq), f32),
            jax.ShapeDtypeStruct((heads, 1, nq), f32),
        ],
        compiler_params=pltpu.CompilerParams(vmem_limit_bytes=48 * 1024 * 1024),
    )(qT, kT, vTT, cm)


def _backward(qT, kT, vT, kTT, gaT, lt, dl, cm, scale):
    heads, nq, hd = qT.shape
    nk = kT.shape[1]
    hb = nk // BLOCK
    tile = min(nq, 2 * TQ)
    f32 = jnp.float32
    grad_type = jnp.bfloat16 if tile == nq else f32
    return pl.pallas_call(
        functools.partial(_bwd_kernel, scale=scale),
        grid=(heads, nq // tile),
        in_specs=[
            pl.BlockSpec((1, tile, hd), lambda h, i: (h, i, 0)),
            pl.BlockSpec((1, nk, hd), lambda h, i: (h, 0, 0)),
            pl.BlockSpec((1, nk, hd), lambda h, i: (h, 0, 0)),
            pl.BlockSpec((1, hd, nk), lambda h, i: (h, 0, 0)),
            pl.BlockSpec((1, tile, hd), lambda h, i: (h, i, 0)),
            pl.BlockSpec((1, 1, tile), lambda h, i: (h, 0, i)),
            pl.BlockSpec((1, 1, tile), lambda h, i: (h, 0, i)),
            pl.BlockSpec((hb, 1, tile), lambda h, i: (0, 0, i)),
        ],
        out_specs=[
            pl.BlockSpec((1, hd, tile), lambda h, i: (h, 0, i)),
            pl.BlockSpec((1, nk, hd), lambda h, i: (h, 0, 0)),
            pl.BlockSpec((1, nk, hd), lambda h, i: (h, 0, 0)),
        ],
        out_shape=[
            jax.ShapeDtypeStruct((heads, hd, nq), jnp.bfloat16),
            jax.ShapeDtypeStruct((heads, nk, hd), grad_type),
            jax.ShapeDtypeStruct((heads, nk, hd), grad_type),
        ],
        compiler_params=pltpu.CompilerParams(
            dimension_semantics=("parallel", "arbitrary"), vmem_limit_bytes=48 * 1024 * 1024
        ),
    )(qT, kT, vT, kTT, gaT, lt, dl, cm)


def on_device(queries_in, hits_in, w_query, w_key, w_value, w_out, mask_list, grad_out):
    f32 = jnp.float32
    bf16 = jnp.bfloat16
    region_index = lax.axis_index("region")
    n_queries, width = queries_in.shape
    n_hits = hits_in.shape[0]
    head_dim = width // HEADS
    scale = 1.0 / math.sqrt(head_dim)
    hit_blocks = n_hits // BLOCK
    q_blocks = n_queries // BLOCK
    local_ids = region_index * hit_blocks + jnp.arange(hit_blocks, dtype=jnp.int32)
    blockmask = jnp.any(mask_list[:, :, None] == local_ids[None, None, :], axis=1)
    cm = jnp.repeat(blockmask.T.astype(f32), BLOCK, axis=1).reshape(hit_blocks, 1, n_queries)

    def heads(x):
        return x.reshape(x.shape[0], HEADS, head_dim).transpose(1, 0, 2)

    def joined(x):
        return x.transpose(1, 0, 2).reshape(x.shape[1], width)

    query = jnp.dot(queries_in, w_query, preferred_element_type=f32).astype(bf16)
    keys = jnp.dot(hits_in, w_key, preferred_element_type=f32).astype(bf16)
    vals = jnp.dot(hits_in, w_value, preferred_element_type=f32).astype(bf16)
    qT, kT, vT = heads(query), heads(keys), heads(vals)

    regions = lax.axis_size("region")
    numer_r, max_r, total_r = _forward(qT, kT, vT.transpose(0, 2, 1), cm, scale)
    numer = numer_r.transpose(2, 0, 1).reshape(n_queries, width)
    peak = max_r.reshape(HEADS, n_queries)
    total = total_r.reshape(HEADS, n_queries)
    rows = n_queries
    base = 0
    steps = []
    k = 0
    while (1 << k) < regions:
        bit = (region_index >> k) & 1
        half = rows // 2
        pairs = [(i, i ^ (1 << k)) for i in range(regions)]
        mine = (
            lax.dynamic_slice_in_dim(numer, bit * half, half, 0),
            lax.dynamic_slice_in_dim(peak, bit * half, half, 1),
            lax.dynamic_slice_in_dim(total, bit * half, half, 1),
        )
        theirs = lax.ppermute(
            (
                lax.dynamic_slice_in_dim(numer, (1 - bit) * half, half, 0).astype(bf16),
                lax.dynamic_slice_in_dim(peak, (1 - bit) * half, half, 1),
                lax.dynamic_slice_in_dim(total, (1 - bit) * half, half, 1),
            ),
            "region",
            pairs,
        )
        top = jnp.maximum(mine[1], theirs[1])
        scale_a = jnp.exp(mine[1] - top)
        scale_b = jnp.exp(theirs[1] - top)
        numer = mine[0] * jnp.repeat(scale_a.T, head_dim, axis=1) + theirs[0].astype(f32) * jnp.repeat(
            scale_b.T, head_dim, axis=1
        )
        total = mine[2] * scale_a + theirs[2] * scale_b
        peak = top
        base = base + bit * half
        steps.append((k, bit, half))
        rows = half
        k += 1
    attended_part = (numer / jnp.repeat(total.T, head_dim, axis=1)).astype(bf16)
    log_part = peak + jnp.log(total)
    grad_att = lax.dot_general(
        grad_out, w_out, (((1,), (1,)), ((), ())), preferred_element_type=f32
    ).astype(bf16)
    grad_att_part = lax.dynamic_slice_in_dim(grad_att, base, rows, 0)
    delta_part = jnp.sum(
        (grad_att_part.astype(f32) * attended_part.astype(f32)).reshape(rows, HEADS, head_dim),
        axis=2,
    ).T
    gathered = (attended_part, jnp.concatenate([log_part, delta_part], axis=0))
    for k, bit, half in reversed(steps):
        pairs = [(i, i ^ (1 << k)) for i in range(regions)]
        other = lax.ppermute(gathered, "region", pairs)
        lo = jax.tree.map(lambda a, b: jnp.where(bit == 0, a, b), gathered, other)
        hi = jax.tree.map(lambda a, b: jnp.where(bit == 0, b, a), gathered, other)
        gathered = (
            jnp.concatenate([lo[0], hi[0]], axis=0),
            jnp.concatenate([lo[1], hi[1]], axis=1),
        )
    attended = gathered[0]
    log_total = gathered[1][:HEADS].reshape(HEADS, 1, n_queries)
    deltas = gathered[1][HEADS:].reshape(HEADS, 1, n_queries)
    layer_out = (
        queries_in.astype(f32) + jnp.dot(attended, w_out, preferred_element_type=f32)
    ).astype(bf16)
    grad_wo = jnp.einsum("qa,qb->ab", attended, grad_out, preferred_element_type=f32)
    gaT = heads(grad_att)

    dq_r, dk, dv = _backward(qT, kT, vT, kT.transpose(0, 2, 1), gaT, log_total, deltas, cm, scale)
    keys_grad = joined(dk).astype(bf16)
    vals_grad = joined(dv).astype(bf16)
    wk_part = jnp.einsum("ka,kb->ab", hits_in, keys_grad, preferred_element_type=f32)
    wv_part = jnp.einsum("ka,kb->ab", hits_in, vals_grad, preferred_element_type=f32)
    summed = lax.psum(
        jnp.concatenate(
            [
                dq_r.transpose(2, 0, 1).reshape(n_queries, width).astype(bf16),
                wk_part.astype(bf16),
                wv_part.astype(bf16),
            ],
            axis=0,
        ),
        "region",
    )
    query_grad_sum = summed[:n_queries]
    grad_wk = summed[n_queries : n_queries + width]
    grad_wv = summed[n_queries + width :]
    grad_wk = grad_wk.astype(f32)
    grad_wv = grad_wv.astype(f32)
    grad_q = query_grad_sum
    grad_wq = jnp.einsum("qa,qb->ab", queries_in, grad_q, preferred_element_type=f32)
    grad_queries = (
        grad_out.astype(f32)
        + lax.dot_general(grad_q, w_query, (((1,), (1,)), ((), ())), preferred_element_type=f32)
    ).astype(bf16)
    grad_hits = (
        lax.dot_general(keys_grad, w_key, (((1,), (1,)), ((), ())), preferred_element_type=f32)
        + lax.dot_general(vals_grad, w_value, (((1,), (1,)), ((), ())), preferred_element_type=f32)
    ).astype(bf16)
    return (layer_out, grad_queries, grad_hits, grad_wq, grad_wk, grad_wv, grad_wo)


def solution(mesh):
    in_specs = (
        P("event", None),
        P(("event", "region"), None),
        P(),
        P(),
        P(),
        P(),
        P("event", None),
        P("event", None),
    )
    out_specs = (
        P("event", None),
        P("event", None),
        P(("event", "region"), None),
        P("event", None),
        P("event", None),
        P("event", None),
        P("event", None),
    )
    return jax.shard_map(
        on_device, mesh=mesh, in_specs=in_specs, out_specs=out_specs, check_vma=False
    )
```
